32 devices in a mesh: dom: 2 (over x), shot: 8 (over z, y), space: 2 (over core).
Axes of the slice: x: 2, y: 2, z: 4, core: 2. Of those that a mesh axis runs over, the one named last changes fastest.
Arguments:
- wave_prev: float32 [16, 64, 64, 128], P(('dom', 'shot'), 'space'), parts along dimension 0, may hold values from -13 to 13
- wave_now: float32 [16, 64, 64, 128], P(('dom', 'shot'), 'space'), parts along dimension 0, may hold values from -13 to 13
- velocity_code: int32 [128, 64, 128], P(('dom', 'space')), parts along dimension 0, may hold values from 0 to 255
- perturb: float32 [128, 64, 128], P(('dom', 'space'), None, 'shot'), parts along dimension 0, may hold values from -3 to 3
- gains: float32 [256, 64], P(('dom', 'shot')), parts along dimension 0, may hold values from 0.25 to 4
- wavelet: float32 [16, 4], P(('dom', 'shot')), parts along dimension 0, may hold values from -12 to 12
- source_index: int32 [16], P(('dom', 'shot')), parts along dimension 0, may hold values from 0 to 524287
- receiver_index: int32 [16, 256], P(('dom', 'shot')), parts along dimension 0, may hold values from 0 to 524287
- absorb_width: int32 [12], P('dom'), parts along dimension 0, may hold values from 4 to 20
Outputs:
- filtered: float32 [128, 64, 128], P(('dom', 'space'), None, 'shot'), parts along dimension 0
- born_field: float32 [16, 64, 64, 128], P(('dom', 'shot'), 'space'), parts along dimension 0
- traces: float32 [16, 2, 256], P(('dom', 'shot')), parts along dimension 0
The draws below stay inside these ranges and needn't reach their ends.
There are 2 independent parts, one for each index of `dom`. The reference program is written for one: setup_inputs(seed, part) draws one part's arguments, and reference() takes and returns one part's arrays. A program takes and returns all parts, laid end to end along the dimension named above; each array names one. Nothing has to cross between parts.
Inputs may be any that keep to these rules, and one draw needn't show every extreme that they name: `absorb_width`: entries are the widths at the low and high end of the first, second and third dimension, in that order. `source_index`: flat row-major cell indices of the whole window. `receiver_index`: flat row-major cell indices of the whole window.
All inputs are finite; a program needn't handle non-finite values.
Results may differ from the reference program's by a relative error of at most 0.0003.
Values sent between devices are 32-bit elements; how exact they have to be, the bound alone decides.
No kernel may reach another device: no remote copies, remote signals or barrier semaphores. Data moves between devices by JAX's collectives and lax.ppermute only.
A program may use at most 64 MiB of HBM per device.

```python
import math
import jax
import jax.numpy as jnp

NX = 64
NY = 64
NZ = 128
STEPS_A = 2
STEPS_B = 2
RECV = 256
SHOTS = 8
STEPS = 4


def checkpoint_field(key, salt):
    base = jax.random.fold_in(key, salt)
    scale_key, noise_key = jax.random.split(base, 2)
    scales = jnp.exp(jax.random.uniform(scale_key, (SHOTS, 1, 1, 1), jnp.float32, math.log(0.3), math.log(3.0)))
    field = scales * jnp.clip(jax.random.normal(noise_key, (SHOTS, NX, NY, NZ), jnp.float32), -4.0, 4.0)
    return field.astype(jnp.float32)


def draw_wave_prev(key, part):
    return checkpoint_field(key, 11)


def draw_wave_now(key, part):
    return checkpoint_field(key, 12)


def touch_ends(entries, rng, least, top_value):
    dims = entries.shape
    index_at = [jax.random.randint(jax.random.fold_in(rng, axis), (), 0, dims[axis]) for axis in range(len(dims))]
    entries = entries.at[tuple(index_at)].set(least)
    longest = dims.index(max(dims))
    index_at[longest] = (index_at[longest] + 1) % dims[longest]
    return entries.at[tuple(index_at)].set(top_value)


def block_levels(key, shape, cuts, low, high):
    def one(axis_at, parts):
        heights = jax.random.uniform(jax.random.fold_in(jax.random.fold_in(key, 6), axis_at), (parts,), jnp.float32, low / len(cuts), high / len(cuts))
        return jnp.repeat(jnp.exp(heights), shape[axis_at] // parts).reshape((-1,) + (1,) * (len(shape) - axis_at - 1))

    loudness = one(*cuts[0])
    for cut in cuts[1:]:
        loudness = loudness * one(*cut)
    return loudness


def gaussian(stream_key, shape, deviation, limit, shards=(), kind=jnp.bfloat16):
    result = jax.random.normal(stream_key, shape, jnp.float32) * deviation
    if len(shards) > 0:
        result = block_levels(stream_key, shape, shards, -0.22, 0.18) * result
    return jnp.clip(result, min=-limit, max=limit).astype(kind)


def setup_inputs(seed: int = 0, part: int = 0) -> dict:
    seeds = jax.random.split(jax.random.key(seed), 10)
    own_keys = jax.random.split(jax.random.fold_in(seeds[9], part), 10)
    return {
        "wave_prev": draw_wave_prev(jax.random.fold_in(jax.random.fold_in(seeds[9], part), 71), part),
        "wave_now": draw_wave_now(jax.random.fold_in(jax.random.fold_in(seeds[9], part), 71), part),
        "velocity_code": touch_ends(jax.random.randint(own_keys[2], (NX, NY, NZ), 0, 256), jax.random.fold_in(own_keys[2], 1), 0, 255).astype(jnp.int32),
        "perturb": gaussian(own_keys[3], (NX, NY, NZ), 0.5, 3.0, ((0, 2), (2, 8)), jnp.float32),
        "gains": jnp.clip(jnp.exp(math.log(4.0) - 2.7725887 * jax.random.uniform(own_keys[4], (NZ, NY), jnp.float32) ** block_levels(own_keys[4], (NZ, NY), ((0, 8),), -0.2, 0.2)), 0.25, 4.0),
        "wavelet": gaussian(own_keys[5], (SHOTS, STEPS), 4.0, 12.0, ((0, 8),), jnp.float32),
        "source_index": touch_ends(jax.random.randint(own_keys[6], (SHOTS,), 0, NX * NY * NZ), jax.random.fold_in(own_keys[6], 1), 0, (NX * NY * NZ) - 1).astype(jnp.int32),
        "receiver_index": touch_ends(jax.random.randint(own_keys[7], (SHOTS, RECV), 0, NX * NY * NZ), jax.random.fold_in(own_keys[7], 1), 0, (NX * NY * NZ) - 1).astype(jnp.int32),
        "absorb_width": touch_ends(jax.random.randint(own_keys[8], (6,), 4, NY // 4 + 5), jax.random.fold_in(own_keys[8], 1), 4, (NY // 4 + 5) - 1).astype(jnp.int32),
    }


STENCIL = (-205.0 / 72.0, 8.0 / 5.0, -1.0 / 5.0, 8.0 / 315.0, -1.0 / 560.0)
damp_peak = 0.5
eps = 1e-5


def coefficient(levels):
    speed = 1500.0 + 15.0 * levels.astype(jnp.float32)
    ratio = 0.45 * speed / 5325.0
    return ratio * ratio


def ramp(position, count, lower, upper):
    low_part = jnp.maximum(lower - position, 0.0) / lower
    high_part = jnp.maximum(upper - (count - 1.0 - position), 0.0) / upper
    return low_part * low_part + high_part * high_part


def damping(widths, positions, count_x, count_y, count_z):
    edges = widths.astype(jnp.float32)
    along_x = ramp(positions, count_x, edges[0], edges[1])
    along_y = ramp(jnp.arange(count_y, dtype=jnp.float32), count_y, edges[2], edges[3])
    along_z = ramp(jnp.arange(count_z, dtype=jnp.float32), count_z, edges[4], edges[5])
    return damp_peak * (along_x[:, None, None] + along_y[None, :, None] + along_z[None, None, :])


def widen(field):
    lead = [(0, 0)] * (field.ndim - 3)
    return jnp.pad(field, lead + [(4, 4), (4, 4), (4, 4)])


def laplace(padded):
    width_x = padded.shape[-3] - 8
    width_y = padded.shape[-2] - 8
    width_z = padded.shape[-1] - 8

    def part(move_x, move_y, move_z):
        return padded[..., 4 + move_x:4 + move_x + width_x, 4 + move_y:4 + move_y + width_y, 4 + move_z:4 + move_z + width_z]

    total = 3.0 * STENCIL[0] * part(0, 0, 0)
    for reach in range(1, 5):
        beside_all = part(reach, 0, 0) + part(-reach, 0, 0) + part(0, reach, 0) + part(0, -reach, 0) + part(0, 0, reach) + part(0, 0, -reach)
        total = total + STENCIL[reach] * beside_all
    return total


def reference(wave_prev, wave_now, velocity_code, perturb, gains, wavelet, source_index, receiver_index, absorb_width):
    shots = wave_now.shape[0]
    speed_term = coefficient(velocity_code)
    absorber = damping(absorb_width, jnp.arange(NX, dtype=jnp.float32), NX, NY, NZ)
    term_flat = speed_term.reshape(-1)
    rows = jnp.arange(shots)

    def inject(field, moment):
        flat = field.reshape(shots, -1)
        flat = flat.at[rows, source_index].add(term_flat[source_index] * wavelet[:, moment])
        return flat.reshape(field.shape)

    def advance(current, prior, born, born_prior, model, moment):
        drive = speed_term * laplace(widen(current))
        later = inject(2.0 * current - prior + drive - absorber * (current - prior), moment)
        born_later = 2.0 * born - born_prior + speed_term * laplace(widen(born)) - absorber * (born - born_prior) + model * drive
        return later, born_later, drive

    current, prior = wave_now, wave_prev
    born = jnp.zeros_like(wave_now)
    born_prior = jnp.zeros_like(wave_now)
    image = jnp.zeros((NX, NY, NZ), jnp.float32)
    light = jnp.zeros((NX, NY, NZ), jnp.float32)
    for moment in range(STEPS_A):
        later, born_later, drive = advance(current, prior, born, born_prior, perturb, moment)
        image = image + jnp.sum(drive * born_later, axis=0)
        light = light + jnp.sum(drive * drive, axis=0)
        prior, current = current, later
        born_prior, born = born, born_later
    scaled = image / (light + eps)
    spectrum = jnp.fft.fft(scaled, axis=1) * jnp.transpose(gains)[None, :, :]
    filtered = jnp.real(jnp.fft.ifft(spectrum, axis=1)).astype(jnp.float32)
    born = jnp.zeros_like(wave_now)
    born_prior = jnp.zeros_like(wave_now)
    records = []
    for moment in range(STEPS_B):
        later, born_later, drive = advance(current, prior, born, born_prior, filtered, STEPS_A + moment)
        records.append(jnp.take_along_axis(born_later.reshape(shots, -1), receiver_index, axis=1))
        prior, current = current, later
        born_prior, born = born, born_later
    return filtered, born, jnp.stack(records, axis=1)
```

```python
import math

import jax
import jax.numpy as jnp
from jax import lax
from jax.sharding import PartitionSpec as P

STEPS_A = 2
STEPS_B = 2


STENCIL = (-205.0 / 72.0, 8.0 / 5.0, -1.0 / 5.0, 8.0 / 315.0, -1.0 / 560.0)
damp_peak = 0.5
eps = 1e-05
HALO = 4


def coefficient(levels):
    speed = 1500.0 + 15.0 * levels.astype(jnp.float32)
    ratio = 0.45 * speed / 5325.0
    return ratio * ratio


def ramp(position, count, lower, upper):
    low_part = jnp.maximum(lower - position, 0.0) / lower
    high_part = jnp.maximum(upper - (count - 1.0 - position), 0.0) / upper
    return low_part * low_part + high_part * high_part


def damping(widths, positions, count_x, count_y, count_z):
    edges = widths.astype(jnp.float32)
    along_x = ramp(positions, count_x, edges[0], edges[1])
    along_y = ramp(jnp.arange(count_y, dtype=jnp.float32), count_y, edges[2], edges[3])
    along_z = ramp(jnp.arange(count_z, dtype=jnp.float32), count_z, edges[4], edges[5])
    return damp_peak * (along_x[:, None, None] + along_y[None, :, None] + along_z[None, None, :])


def with_halo(x):
    size = lax.axis_size("space")
    length = x.shape[0]
    if size == 2:
        me = lax.axis_index("space")
        piece = lax.dynamic_slice_in_dim(x, (1 - me) * (length - HALO), HALO, 0)
        got = lax.ppermute(piece, "space", [(0, 1), (1, 0)])
        zeros = jnp.zeros((HALO,) + x.shape[1:], x.dtype)
        padded = jnp.concatenate([zeros, x, zeros], axis=0)
        return lax.dynamic_update_slice_in_dim(padded, got, (1 - me) * (length + HALO), 0)
    up = [(i, (i + 1) % size) for i in range(size - 1)]
    down = [(j, i) for i, j in up]
    before = lax.ppermute(x[length - HALO :], "space", up)
    after = lax.ppermute(x[:HALO], "space", down)
    return jnp.concatenate([before, x, after], axis=0)


def laplace_x(padded):
    width_x = padded.shape[0] - 8
    width_y = padded.shape[1]
    width_z = padded.shape[2]
    full = jnp.pad(padded, [(0, 0), (4, 4), (4, 4)])

    def part(move_x, move_y, move_z):
        return full[
            4 + move_x : 4 + move_x + width_x,
            4 + move_y : 4 + move_y + width_y,
            4 + move_z : 4 + move_z + width_z,
        ]

    total = 3.0 * STENCIL[0] * part(0, 0, 0)
    for reach in range(1, 5):
        beside_all = (
            part(reach, 0, 0)
            + part(-reach, 0, 0)
            + part(0, reach, 0)
            + part(0, -reach, 0)
            + part(0, 0, reach)
            + part(0, 0, -reach)
        )
        total = total + STENCIL[reach] * beside_all
    return total


def lateral_filter(field, table):
    count = field.shape[1]
    index = jnp.arange(count)
    phase = index[:, None] * index[None, :] % count
    angle = 2.0 * math.pi / count * phase.astype(jnp.float32)
    cosine = jnp.cos(angle)
    sine = jnp.sin(angle)
    real_part = jnp.einsum("xyz,yk->xzk", field, cosine, precision=lax.Precision.HIGHEST)
    imag_part = jnp.einsum("xyz,yk->xzk", field, sine, precision=lax.Precision.HIGHEST)
    weight = table[None, :, :]
    back = jnp.einsum("xzk,yk->xyz", real_part * weight, cosine, precision=lax.Precision.HIGHEST)
    back = back + jnp.einsum(
        "xzk,yk->xyz", imag_part * weight, sine, precision=lax.Precision.HIGHEST
    )
    return back / count


def shot_bits(n):
    bits = []
    k = 1
    while k < n:
        bits.append(k)
        k *= 2
    assert k == n
    return bits


def gather_shot(block):
    n = lax.axis_size("shot")
    me = lax.axis_index("shot")
    held = block[None]
    for k in reversed(shot_bits(n)):
        theirs = lax.ppermute(held, "shot", [(i, i ^ k) for i in range(n)])
        low = (me // k) % 2 == 0
        pair = jnp.where(low, jnp.stack([held, theirs], axis=1), jnp.stack([theirs, held], axis=1))
        held = pair.reshape((-1,) + block.shape)
    return held


def scatter_shot(parts):
    n = lax.axis_size("shot")
    me = lax.axis_index("shot")
    held = parts
    for k in shot_bits(n):
        m = held.shape[0] // 2
        split = held.reshape((m, 2) + held.shape[1:])
        mine = (me // k) % 2
        keep = lax.dynamic_index_in_dim(split, mine, axis=1, keepdims=False)
        send = lax.dynamic_index_in_dim(split, 1 - mine, axis=1, keepdims=False)
        held = keep + lax.ppermute(send, "shot", [(i, i ^ k) for i in range(n)])
    return held[0]


def body(
    wave_prev,
    wave_now,
    velocity_code,
    perturb,
    gains,
    wavelet,
    source_index,
    receiver_index,
    absorb_width,
):
    shots, span_x, span_y, span_z = wave_now.shape
    n_shot = lax.axis_size("shot")
    me_shot = lax.axis_index("shot")
    start_x = lax.axis_index("space") * span_x
    total_x = span_x * lax.axis_size("space")
    speed_term = coefficient(velocity_code)
    positions = start_x.astype(jnp.float32) + jnp.arange(span_x, dtype=jnp.float32)
    absorber = damping(absorb_width, positions, total_x, span_y, span_z)
    term_flat = speed_term.reshape(-1)
    cells = span_x * span_y * span_z
    offset = start_x * span_y * span_z
    source_local = source_index - offset
    source_owned = (source_local >= 0) & (source_local < cells)
    source_safe = jnp.clip(source_local, 0, cells - 1)
    source_gain = jnp.where(source_owned, term_flat[source_safe], 0.0)

    depth = perturb.shape[2]
    dense = perturb.reshape(span_x, span_y * depth // span_z, span_z)
    blocks = gather_shot(dense)
    model = (
        blocks.reshape(n_shot, span_x, span_y, depth)
        .transpose(1, 2, 0, 3)
        .reshape(span_x, span_y, span_z)
    )
    table_all = gather_shot(gains).reshape(n_shot * gains.shape[0], gains.shape[1])

    def inject(field, moment):
        flat = field.reshape(1, -1)
        flat = flat.at[jnp.arange(1), source_safe].add(source_gain * wavelet[:, moment])
        return flat.reshape(field.shape)

    def wave_step(current, prior, moment, last):
        drive = speed_term * laplace_x(with_halo(current))
        if last:
            return None, drive
        later = inject(2.0 * current - prior + drive - absorber * (current - prior), moment)
        return later, drive

    def born_second(born, field_model, drive):
        return (
            2.0 * born
            + speed_term * laplace_x(with_halo(born))
            - absorber * born
            + field_model * drive
        )

    w0, wp = wave_now[0], wave_prev[0]
    w1, drive0 = wave_step(w0, wp, 0, False)
    w2, drive1 = wave_step(w1, w0, 1, False)
    w3, drive2 = wave_step(w2, w1, 2, False)
    _, drive3 = wave_step(w3, w2, 3, True)

    slab = span_x // n_shot
    light = drive0 * drive0 + drive1 * drive1
    light_part = scatter_shot(light.reshape(n_shot, slab, span_y, span_z))

    born1 = model * drive0
    born2 = born_second(born1, model, drive1)
    image = drive0 * born1 + drive1 * born2
    image_part = scatter_shot(image.reshape(n_shot, slab, span_y, span_z))

    table_x = table_all
    filt_part = lateral_filter(image_part / (light_part + eps), table_x)
    new_model = gather_shot(filt_part).reshape(span_x, span_y, span_z)
    filtered = lax.dynamic_slice_in_dim(new_model, me_shot * depth, depth, 2)

    b1 = new_model * drive2
    b2 = born_second(b1, new_model, drive3)

    receiver_local = receiver_index[0] - offset
    receiver_owned = (receiver_local >= 0) & (receiver_local < cells)
    receiver_safe = jnp.clip(receiver_local, 0, cells - 1)
    rx = receiver_safe // (span_y * span_z)
    ry = (receiver_safe // span_z) % span_y
    rz = receiver_safe % span_z
    lane = jnp.arange(span_z)[None, :] == rz[:, None]

    def sample(field):
        rows = field[rx, ry]
        picked = jnp.sum(jnp.where(lane, rows, 0.0), axis=1)
        return jnp.where(receiver_owned, picked, 0.0)

    records = jnp.stack([sample(b1), sample(b2)], axis=0)[None]
    traces = records + lax.ppermute(records, "space", [(0, 1), (1, 0)])
    return (filtered, b2[None], traces)


def solution(mesh):
    in_specs = (
        P(("dom", "shot"), "space", None, None),
        P(("dom", "shot"), "space", None, None),
        P(("dom", "space"), None, None),
        P(("dom", "space"), None, "shot"),
        P(("dom", "shot"), None),
        P(("dom", "shot"), None),
        P(("dom", "shot")),
        P(("dom", "shot"), None),
        P("dom"),
    )
    out_specs = (
        P(("dom", "space"), None, "shot"),
        P(("dom", "shot"), "space", None, None),
        P(("dom", "shot"), None, None),
    )
    return jax.shard_map(body, mesh=mesh, in_specs=in_specs, out_specs=out_specs, check_vma=False)
```

```python
import math

import jax
import jax.numpy as jnp
from jax import lax
from jax.sharding import PartitionSpec as P

STEPS_A = 2
STEPS_B = 2


STENCIL = (-205.0 / 72.0, 8.0 / 5.0, -1.0 / 5.0, 8.0 / 315.0, -1.0 / 560.0)
damp_peak = 0.5
eps = 1e-05
HALO = 4


def coefficient(levels):
    speed = 1500.0 + 15.0 * levels.astype(jnp.float32)
    ratio = 0.45 * speed / 5325.0
    return ratio * ratio


def ramp(position, count, lower, upper):
    low_part = jnp.maximum(lower - position, 0.0) / lower
    high_part = jnp.maximum(upper - (count - 1.0 - position), 0.0) / upper
    return low_part * low_part + high_part * high_part


def damping(widths, positions, count_x, count_y, count_z):
    edges = widths.astype(jnp.float32)
    along_x = ramp(positions, count_x, edges[0], edges[1])
    along_y = ramp(jnp.arange(count_y, dtype=jnp.float32), count_y, edges[2], edges[3])
    along_z = ramp(jnp.arange(count_z, dtype=jnp.float32), count_z, edges[4], edges[5])
    return damp_peak * (along_x[:, None, None] + along_y[None, :, None] + along_z[None, None, :])


def with_halo(x):
    size = lax.axis_size("space")
    length = x.shape[0]
    if size == 2:
        me = lax.axis_index("space")
        piece = lax.dynamic_slice_in_dim(x, (1 - me) * (length - HALO), HALO, 0)
        got = lax.ppermute(piece, "space", [(0, 1), (1, 0)])
        zeros = jnp.zeros((HALO,) + x.shape[1:], x.dtype)
        padded = jnp.concatenate([zeros, x, zeros], axis=0)
        return lax.dynamic_update_slice_in_dim(padded, got, (1 - me) * (length + HALO), 0)
    up = [(i, (i + 1) % size) for i in range(size - 1)]
    down = [(j, i) for i, j in up]
    before = lax.ppermute(x[length - HALO :], "space", up)
    after = lax.ppermute(x[:HALO], "space", down)
    return jnp.concatenate([before, x, after], axis=0)


def laplace_x(padded):
    width_x = padded.shape[0] - 8
    width_y = padded.shape[1]
    width_z = padded.shape[2]
    full = jnp.pad(padded, [(0, 0), (4, 4), (4, 4)])

    def part(move_x, move_y, move_z):
        return full[
            4 + move_x : 4 + move_x + width_x,
            4 + move_y : 4 + move_y + width_y,
            4 + move_z : 4 + move_z + width_z,
        ]

    total = 3.0 * STENCIL[0] * part(0, 0, 0)
    for reach in range(1, 5):
        beside_all = (
            part(reach, 0, 0)
            + part(-reach, 0, 0)
            + part(0, reach, 0)
            + part(0, -reach, 0)
            + part(0, 0, reach)
            + part(0, 0, -reach)
        )
        total = total + STENCIL[reach] * beside_all
    return total


def lateral_filter(field, table):
    count = field.shape[1]
    index = jnp.arange(count)
    phase = index[:, None] * index[None, :] % count
    angle = 2.0 * math.pi / count * phase.astype(jnp.float32)
    cosine = jnp.cos(angle)
    sine = jnp.sin(angle)
    real_part = jnp.einsum("xyz,yk->xzk", field, cosine, precision=lax.Precision.HIGHEST)
    imag_part = jnp.einsum("xyz,yk->xzk", field, sine, precision=lax.Precision.HIGHEST)
    weight = table[None, :, :]
    back = jnp.einsum("xzk,yk->xyz", real_part * weight, cosine, precision=lax.Precision.HIGHEST)
    back = back + jnp.einsum(
        "xzk,yk->xyz", imag_part * weight, sine, precision=lax.Precision.HIGHEST
    )
    return back / count


def shot_bits(n):
    bits = []
    k = 1
    while k < n:
        bits.append(k)
        k *= 2
    assert k == n
    return bits


def ag_step(held, k):
    n = lax.axis_size("shot")
    me = lax.axis_index("shot")
    theirs = lax.ppermute(held, "shot", [(i, i ^ k) for i in range(n)])
    low = (me // k) % 2 == 0
    pair = jnp.where(low, jnp.stack([held, theirs], axis=1), jnp.stack([theirs, held], axis=1))
    return pair.reshape((-1,) + held.shape[1:])


def rs_step(held, k):
    n = lax.axis_size("shot")
    me = lax.axis_index("shot")
    m = held.shape[0] // 2
    split = held.reshape((m, 2) + held.shape[1:])
    mine = (me // k) % 2
    keep = lax.dynamic_index_in_dim(split, mine, axis=1, keepdims=False)
    send = lax.dynamic_index_in_dim(split, 1 - mine, axis=1, keepdims=False)
    return keep + lax.ppermute(send, "shot", [(i, i ^ k) for i in range(n)])


def body(
    wave_prev,
    wave_now,
    velocity_code,
    perturb,
    gains,
    wavelet,
    source_index,
    receiver_index,
    absorb_width,
):
    shots, span_x, span_y, span_z = wave_now.shape
    n_shot = lax.axis_size("shot")
    me_shot = lax.axis_index("shot")
    bits = shot_bits(n_shot)
    start_x = lax.axis_index("space") * span_x
    total_x = span_x * lax.axis_size("space")
    speed_term = coefficient(velocity_code)
    positions = start_x.astype(jnp.float32) + jnp.arange(span_x, dtype=jnp.float32)
    absorber = damping(absorb_width, positions, total_x, span_y, span_z)
    term_flat = speed_term.reshape(-1)
    cells = span_x * span_y * span_z
    offset = start_x * span_y * span_z
    source_local = source_index - offset
    source_owned = (source_local >= 0) & (source_local < cells)
    source_safe = jnp.clip(source_local, 0, cells - 1)
    source_gain = jnp.where(source_owned, term_flat[source_safe], 0.0)
    barrier = lax.optimization_barrier

    def inject(field, moment):
        flat = field.reshape(1, -1)
        flat = flat.at[jnp.arange(1), source_safe].add(source_gain * wavelet[:, moment])
        return flat.reshape(field.shape)

    def wave_step(current, prior, moment, last):
        drive = speed_term * laplace_x(with_halo(current))
        if last:
            return None, drive
        later = inject(2.0 * current - prior + drive - absorber * (current - prior), moment)
        return later, drive

    def born_second(born, field_model, drive):
        return (
            2.0 * born
            + speed_term * laplace_x(with_halo(born))
            - absorber * born
            + field_model * drive
        )

    slab = span_x // n_shot
    depth = perturb.shape[2]
    model_held = perturb.transpose(2, 0, 1).reshape(1, depth, span_x * span_y)
    gains_held = gains[None]
    st = {"w0": wave_now[0], "wp": wave_prev[0]}

    def task_wave(i):
        def run():
            last = i == 3
            cur, pri = (st["w0"], st["wp"]) if i == 0 else (st["w%d" % i], st["w%d" % (i - 1)])
            later, drive = wave_step(cur, pri, i, last)
            st["drive%d" % i] = drive
            if not last:
                st["w%d" % (i + 1)] = later
        return run

    tasks = [task_wave(0), task_wave(1), task_wave(2)]
    keys = []
    for i, k in enumerate(reversed(bits)):
        model_held = ag_step(model_held, k)
        gains_held = ag_step(gains_held, k)
        if i < len(tasks):
            tasks[i]()
        keys = sorted(st.keys())
        out = barrier((model_held, gains_held, [st[n] for n in keys]))
        model_held, gains_held = out[0], out[1]
        st.update(zip(keys, out[2]))
    for i in range(len(bits), len(tasks)):
        tasks[i]()

    light = st["drive0"] * st["drive0"] + st["drive1"] * st["drive1"]
    light_held = light.reshape(n_shot, slab, span_y, span_z)

    def born_one():
        model = model_held.reshape(span_z, span_x * span_y).T.reshape(span_x, span_y, span_z)
        st["model"] = model
        st["born1"] = model * st["drive0"]

    def born_two():
        st["born2"] = born_second(st["born1"], st["model"], st["drive1"])

    tasks = [born_one, born_two]
    for i, k in enumerate(bits):
        light_held = rs_step(light_held, k)
        if i < len(tasks):
            tasks[i]()
        keys = sorted(st.keys())
        out = barrier((light_held, [st[n] for n in keys]))
        light_held = out[0]
        st.update(zip(keys, out[1]))
    for i in range(len(bits), len(tasks)):
        tasks[i]()

    image = st["drive0"] * st["born1"] + st["drive1"] * st["born2"]
    image_held = image.reshape(n_shot, slab, span_y, span_z)
    tasks = [task_wave(3)]
    for i, k in enumerate(bits):
        image_held = rs_step(image_held, k)
        if i < len(tasks):
            tasks[i]()
        keys = sorted(st.keys())
        out = barrier((image_held, [st[n] for n in keys]))
        image_held = out[0]
        st.update(zip(keys, out[1]))
    for i in range(len(bits), len(tasks)):
        tasks[i]()

    table_all = gains_held.reshape(n_shot * gains.shape[0], gains.shape[1])
    filt_part = lateral_filter(image_held[0] / (light_held[0] + eps), table_all)
    filt_held = filt_part[None]
    for k in reversed(bits):
        filt_held = ag_step(filt_held, k)
    new_model = filt_held.reshape(span_x, span_y, span_z)
    filtered = lax.dynamic_slice_in_dim(new_model, me_shot * depth, depth, 2)

    b1 = new_model * st["drive2"]
    b2 = born_second(b1, new_model, st["drive3"])

    receiver_local = receiver_index[0] - offset
    receiver_owned = (receiver_local >= 0) & (receiver_local < cells)
    receiver_safe = jnp.clip(receiver_local, 0, cells - 1)
    row = receiver_safe // span_z
    rz = receiver_safe % span_z
    lane = jnp.arange(span_z)[None, :] == rz[:, None]

    def sample(field):
        rows = jnp.take(field.reshape(span_x * span_y, span_z), row, axis=0)
        picked = jnp.sum(jnp.where(lane, rows, 0.0), axis=1)
        return jnp.where(receiver_owned, picked, 0.0)

    records = jnp.stack([sample(b1), sample(b2)], axis=0)[None]
    traces = records + lax.ppermute(records, "space", [(0, 1), (1, 0)])
    return (filtered, b2[None], traces)


def solution(mesh):
    in_specs = (
        P(("dom", "shot"), "space", None, None),
        P(("dom", "shot"), "space", None, None),
        P(("dom", "space"), None, None),
        P(("dom", "space"), None, "shot"),
        P(("dom", "shot"), None),
        P(("dom", "shot"), None),
        P(("dom", "shot")),
        P(("dom", "shot"), None),
        P("dom"),
    )
    out_specs = (
        P(("dom", "space"), None, "shot"),
        P(("dom", "shot"), "space", None, None),
        P(("dom", "shot"), None, None),
    )
    return jax.shard_map(body, mesh=mesh, in_specs=in_specs, out_specs=out_specs, check_vma=False)
```

```python
import math

import jax
import jax.numpy as jnp
from jax import lax
from jax.sharding import PartitionSpec as P

STEPS_A = 2
STEPS_B = 2


STENCIL = (-205.0 / 72.0, 8.0 / 5.0, -1.0 / 5.0, 8.0 / 315.0, -1.0 / 560.0)
damp_peak = 0.5
eps = 1e-05
HALO = 4


def coefficient(levels):
    speed = 1500.0 + 15.0 * levels.astype(jnp.float32)
    ratio = 0.45 * speed / 5325.0
    return ratio * ratio


def ramp(position, count, lower, upper):
    low_part = jnp.maximum(lower - position, 0.0) / lower
    high_part = jnp.maximum(upper - (count - 1.0 - position), 0.0) / upper
    return low_part * low_part + high_part * high_part


def damping(widths, positions, count_x, count_y, count_z):
    edges = widths.astype(jnp.float32)
    along_x = ramp(positions, count_x, edges[0], edges[1])
    along_y = ramp(jnp.arange(count_y, dtype=jnp.float32), count_y, edges[2], edges[3])
    along_z = ramp(jnp.arange(count_z, dtype=jnp.float32), count_z, edges[4], edges[5])
    return damp_peak * (along_x[:, None, None] + along_y[None, :, None] + along_z[None, None, :])


def with_halo(x):
    size = lax.axis_size("space")
    length = x.shape[0]
    if size == 2:
        me = lax.axis_index("space")
        piece = lax.dynamic_slice_in_dim(x, (1 - me) * (length - HALO), HALO, 0)
        got = lax.ppermute(piece, "space", [(0, 1), (1, 0)])
        zeros = jnp.zeros((HALO,) + x.shape[1:], x.dtype)
        padded = jnp.concatenate([zeros, x, zeros], axis=0)
        return lax.dynamic_update_slice_in_dim(padded, got, (1 - me) * (length + HALO), 0)
    up = [(i, (i + 1) % size) for i in range(size - 1)]
    down = [(j, i) for i, j in up]
    before = lax.ppermute(x[length - HALO :], "space", up)
    after = lax.ppermute(x[:HALO], "space", down)
    return jnp.concatenate([before, x, after], axis=0)


def laplace_x(padded):
    width_x = padded.shape[0] - 8
    width_y = padded.shape[1]
    width_z = padded.shape[2]
    full = jnp.pad(padded, [(0, 0), (4, 4), (4, 4)])

    def part(move_x, move_y, move_z):
        return full[
            4 + move_x : 4 + move_x + width_x,
            4 + move_y : 4 + move_y + width_y,
            4 + move_z : 4 + move_z + width_z,
        ]

    total = 3.0 * STENCIL[0] * part(0, 0, 0)
    for reach in range(1, 5):
        beside_all = (
            part(reach, 0, 0)
            + part(-reach, 0, 0)
            + part(0, reach, 0)
            + part(0, -reach, 0)
            + part(0, 0, reach)
            + part(0, 0, -reach)
        )
        total = total + STENCIL[reach] * beside_all
    return total


def lateral_filter(field, table):
    count = field.shape[1]
    index = jnp.arange(count)
    phase = index[:, None] * index[None, :] % count
    angle = 2.0 * math.pi / count * phase.astype(jnp.float32)
    cosine = jnp.cos(angle)
    sine = jnp.sin(angle)
    real_part = jnp.einsum("xyz,yk->xzk", field, cosine, precision=lax.Precision.HIGHEST)
    imag_part = jnp.einsum("xyz,yk->xzk", field, sine, precision=lax.Precision.HIGHEST)
    weight = table[None, :, :]
    back = jnp.einsum("xzk,yk->xyz", real_part * weight, cosine, precision=lax.Precision.HIGHEST)
    back = back + jnp.einsum(
        "xzk,yk->xyz", imag_part * weight, sine, precision=lax.Precision.HIGHEST
    )
    return back / count


def shot_bits(n):
    bits = []
    k = 1
    while k < n:
        bits.append(k)
        k *= 2
    assert k == n
    return bits


def ag_step(held, k):
    n = lax.axis_size("shot")
    me = lax.axis_index("shot")
    theirs = lax.ppermute(held, "shot", [(i, i ^ k) for i in range(n)])
    low = (me // k) % 2 == 0
    pair = jnp.where(low, jnp.stack([held, theirs], axis=1), jnp.stack([theirs, held], axis=1))
    return pair.reshape((-1,) + held.shape[1:])


def rs_step(held, k):
    n = lax.axis_size("shot")
    me = lax.axis_index("shot")
    m = held.shape[0] // 2
    split = held.reshape((m, 2) + held.shape[1:])
    mine = (me // k) % 2
    keep = lax.dynamic_index_in_dim(split, mine, axis=1, keepdims=False)
    send = lax.dynamic_index_in_dim(split, 1 - mine, axis=1, keepdims=False)
    return keep + lax.ppermute(send, "shot", [(i, i ^ k) for i in range(n)])


def body(
    wave_prev,
    wave_now,
    velocity_code,
    perturb,
    gains,
    wavelet,
    source_index,
    receiver_index,
    absorb_width,
):
    shots, span_x, span_y, span_z = wave_now.shape
    n_shot = lax.axis_size("shot")
    me_shot = lax.axis_index("shot")
    bits = shot_bits(n_shot)
    start_x = lax.axis_index("space") * span_x
    total_x = span_x * lax.axis_size("space")
    speed_term = coefficient(velocity_code)
    positions = start_x.astype(jnp.float32) + jnp.arange(span_x, dtype=jnp.float32)
    absorber = damping(absorb_width, positions, total_x, span_y, span_z)
    term_flat = speed_term.reshape(-1)
    cells = span_x * span_y * span_z
    offset = start_x * span_y * span_z
    source_local = source_index - offset
    source_owned = (source_local >= 0) & (source_local < cells)
    source_safe = jnp.clip(source_local, 0, cells - 1)
    source_gain = jnp.where(source_owned, term_flat[source_safe], 0.0)
    barrier = lax.optimization_barrier

    def inject(field, moment):
        flat = field.reshape(1, -1)
        flat = flat.at[jnp.arange(1), source_safe].add(source_gain * wavelet[:, moment])
        return flat.reshape(field.shape)

    def wave_step(current, prior, moment, last):
        drive = speed_term * laplace_x(with_halo(current))
        if last:
            return None, drive
        later = inject(2.0 * current - prior + drive - absorber * (current - prior), moment)
        return later, drive

    def born_second(born, field_model, drive):
        return (
            2.0 * born
            + speed_term * laplace_x(with_halo(born))
            - absorber * born
            + field_model * drive
        )

    slab = span_x // n_shot
    depth = perturb.shape[2]
    model_held = perturb.transpose(2, 0, 1).reshape(1, depth, span_x * span_y)
    gains_held = gains[None]
    st = {"w0": wave_now[0], "wp": wave_prev[0]}

    def task_wave(i):
        def run():
            last = i == 3
            cur, pri = (st["w0"], st["wp"]) if i == 0 else (st["w%d" % i], st["w%d" % (i - 1)])
            later, drive = wave_step(cur, pri, i, last)
            st["drive%d" % i] = drive
            if not last:
                st["w%d" % (i + 1)] = later
        return run

    def run_group(comm, compute):
        moved = [step(held, k) for held, step, k in comm]
        compute()
        keys = sorted(st.keys())
        out = barrier((moved, [st[n] for n in keys]))
        st.update(zip(keys, out[1]))
        return out[0]

    def nothing():
        return None

    def light_prep():
        task_wave(2)()
        st["light"] = st["drive0"] * st["drive0"] + st["drive1"] * st["drive1"]

    ag_bits = list(reversed(bits))
    tasks = [task_wave(0), task_wave(1), light_prep]
    for i, k in enumerate(ag_bits):
        model_held, gains_held = run_group(
            [(model_held, ag_step, k), (gains_held, ag_step, k)],
            tasks[i] if i < len(tasks) else nothing,
        )
    for i in range(len(bits), len(tasks)):
        tasks[i]()
    light_held = st["light"].reshape(n_shot, slab, span_y, span_z)

    def born_pass():
        model = model_held.reshape(span_z, span_x * span_y).T.reshape(span_x, span_y, span_z)
        st["born1"] = model * st["drive0"]
        st["born2"] = born_second(st["born1"], model, st["drive1"])

    (light_held,) = run_group([(light_held, rs_step, bits[0])], born_pass)
    born1, born2 = st["born1"], st["born2"]

    image = st["drive0"] * born1 + st["drive1"] * born2
    image_held = image.reshape(n_shot, slab, span_y, span_z)
    tasks = [task_wave(3)]
    for i, k in enumerate(bits):
        comm = [(image_held, rs_step, k)]
        if i + 1 < len(bits):
            comm.append((light_held, rs_step, bits[i + 1]))
        moved = run_group(comm, tasks[i] if i < len(tasks) else nothing)
        image_held = moved[0]
        if i + 1 < len(bits):
            light_held = moved[1]
    for i in range(len(bits), len(tasks)):
        tasks[i]()

    table_all = gains_held.reshape(n_shot * gains.shape[0], gains.shape[1])
    filt_part = lateral_filter(image_held[0] / (light_held[0] + eps), table_all)
    filt_held = filt_part[None]
    for k in reversed(bits):
        filt_held = ag_step(filt_held, k)
    new_model = filt_held.reshape(span_x, span_y, span_z)
    filtered = lax.dynamic_slice_in_dim(new_model, me_shot * depth, depth, 2)

    b1 = new_model * st["drive2"]
    b2 = born_second(b1, new_model, st["drive3"])

    receiver_local = receiver_index[0] - offset
    receiver_owned = (receiver_local >= 0) & (receiver_local < cells)
    receiver_safe = jnp.clip(receiver_local, 0, cells - 1)
    row = receiver_safe // span_z
    rz = receiver_safe % span_z
    lane = jnp.arange(span_z)[None, :] == rz[:, None]

    def sample(field):
        rows = jnp.take(field.reshape(span_x * span_y, span_z), row, axis=0)
        picked = jnp.sum(jnp.where(lane, rows, 0.0), axis=1)
        return jnp.where(receiver_owned, picked, 0.0)

    records = jnp.stack([sample(b1), sample(b2)], axis=0)[None]
    traces = records + lax.ppermute(records, "space", [(0, 1), (1, 0)])
    return (filtered, b2[None], traces)


def solution(mesh):
    in_specs = (
        P(("dom", "shot"), "space", None, None),
        P(("dom", "shot"), "space", None, None),
        P(("dom", "space"), None, None),
        P(("dom", "space"), None, "shot"),
        P(("dom", "shot"), None),
        P(("dom", "shot"), None),
        P(("dom", "shot")),
        P(("dom", "shot"), None),
        P("dom"),
    )
    out_specs = (
        P(("dom", "space"), None, "shot"),
        P(("dom", "shot"), "space", None, None),
        P(("dom", "shot"), None, None),
    )
    return jax.shard_map(body, mesh=mesh, in_specs=in_specs, out_specs=out_specs, check_vma=False)
```

```python
import math

import jax
import jax.numpy as jnp
from jax import lax
from jax.sharding import PartitionSpec as P

STEPS_A = 2
STEPS_B = 2


STENCIL = (-205.0 / 72.0, 8.0 / 5.0, -1.0 / 5.0, 8.0 / 315.0, -1.0 / 560.0)
damp_peak = 0.5
eps = 1e-05
HALO = 4


def coefficient(levels):
    speed = 1500.0 + 15.0 * levels.astype(jnp.float32)
    ratio = 0.45 * speed / 5325.0
    return ratio * ratio


def ramp(position, count, lower, upper):
    low_part = jnp.maximum(lower - position, 0.0) / lower
    high_part = jnp.maximum(upper - (count - 1.0 - position), 0.0) / upper
    return low_part * low_part + high_part * high_part


def damping(widths, positions, count_x, count_y, count_z):
    edges = widths.astype(jnp.float32)
    along_x = ramp(positions, count_x, edges[0], edges[1])
    along_y = ramp(jnp.arange(count_y, dtype=jnp.float32), count_y, edges[2], edges[3])
    along_z = ramp(jnp.arange(count_z, dtype=jnp.float32), count_z, edges[4], edges[5])
    return damp_peak * (along_x[:, None, None] + along_y[None, :, None] + along_z[None, None, :])


def with_halo(x):
    size = lax.axis_size("space")
    length = x.shape[0]
    if size == 2:
        me = lax.axis_index("space")
        piece = lax.dynamic_slice_in_dim(x, (1 - me) * (length - HALO), HALO, 0)
        got = lax.ppermute(piece, "space", [(0, 1), (1, 0)])
        zero = jnp.zeros_like(got)
        before = jnp.where(me == 1, got, zero)
        after = jnp.where(me == 0, got, zero)
        return jnp.concatenate([before, x, after], axis=0)
    up = [(i, (i + 1) % size) for i in range(size - 1)]
    down = [(j, i) for i, j in up]
    before = lax.ppermute(x[length - HALO :], "space", up)
    after = lax.ppermute(x[:HALO], "space", down)
    return jnp.concatenate([before, x, after], axis=0)


def laplace_x(padded):
    width_x = padded.shape[0] - 8
    width_y = padded.shape[1]
    width_z = padded.shape[2]
    full = jnp.pad(padded, [(0, 0), (4, 4), (4, 4)])

    def part(move_x, move_y, move_z):
        return full[
            4 + move_x : 4 + move_x + width_x,
            4 + move_y : 4 + move_y + width_y,
            4 + move_z : 4 + move_z + width_z,
        ]

    total = 3.0 * STENCIL[0] * part(0, 0, 0)
    for reach in range(1, 5):
        beside_all = (
            part(reach, 0, 0)
            + part(-reach, 0, 0)
            + part(0, reach, 0)
            + part(0, -reach, 0)
            + part(0, 0, reach)
            + part(0, 0, -reach)
        )
        total = total + STENCIL[reach] * beside_all
    return total


def lateral_filter(field, table):
    count = field.shape[1]
    index = jnp.arange(count)
    phase = index[:, None] * index[None, :] % count
    angle = 2.0 * math.pi / count * phase.astype(jnp.float32)
    cosine = jnp.cos(angle)
    sine = jnp.sin(angle)
    real_part = jnp.einsum("xyz,yk->xzk", field, cosine, precision=lax.Precision.HIGHEST)
    imag_part = jnp.einsum("xyz,yk->xzk", field, sine, precision=lax.Precision.HIGHEST)
    weight = table[None, :, :]
    back = jnp.einsum("xzk,yk->xyz", real_part * weight, cosine, precision=lax.Precision.HIGHEST)
    back = back + jnp.einsum(
        "xzk,yk->xyz", imag_part * weight, sine, precision=lax.Precision.HIGHEST
    )
    return back / count


def shot_bits(n):
    bits = []
    k = 1
    while k < n:
        bits.append(k)
        k *= 2
    assert k == n
    return bits


def ag_step(held, k):
    n = lax.axis_size("shot")
    me = lax.axis_index("shot")
    theirs = lax.ppermute(held, "shot", [(i, i ^ k) for i in range(n)])
    low = (me // k) % 2 == 0
    pair = jnp.where(low, jnp.stack([held, theirs], axis=1), jnp.stack([theirs, held], axis=1))
    return pair.reshape((-1,) + held.shape[1:])


def rs_step(held, k):
    n = lax.axis_size("shot")
    me = lax.axis_index("shot")
    m = held.shape[0] // 2
    split = held.reshape((m, 2) + held.shape[1:])
    mine = (me // k) % 2
    keep = lax.dynamic_index_in_dim(split, mine, axis=1, keepdims=False)
    send = lax.dynamic_index_in_dim(split, 1 - mine, axis=1, keepdims=False)
    return keep + lax.ppermute(send, "shot", [(i, i ^ k) for i in range(n)])


def body(
    wave_prev,
    wave_now,
    velocity_code,
    perturb,
    gains,
    wavelet,
    source_index,
    receiver_index,
    absorb_width,
):
    shots, span_x, span_y, span_z = wave_now.shape
    n_shot = lax.axis_size("shot")
    me_shot = lax.axis_index("shot")
    bits = shot_bits(n_shot)
    start_x = lax.axis_index("space") * span_x
    total_x = span_x * lax.axis_size("space")
    speed_term = coefficient(velocity_code)
    positions = start_x.astype(jnp.float32) + jnp.arange(span_x, dtype=jnp.float32)
    absorber = damping(absorb_width, positions, total_x, span_y, span_z)
    term_flat = speed_term.reshape(-1)
    cells = span_x * span_y * span_z
    offset = start_x * span_y * span_z
    source_local = source_index - offset
    source_owned = (source_local >= 0) & (source_local < cells)
    source_safe = jnp.clip(source_local, 0, cells - 1)
    source_gain = jnp.where(source_owned, term_flat[source_safe], 0.0)
    barrier = lax.optimization_barrier

    plane = span_y * span_z
    hit = (
        (jnp.arange(span_x)[:, None, None] == source_safe[0] // plane)
        & (jnp.arange(span_y)[None, :, None] == (source_safe[0] // span_z) % span_y)
        & (jnp.arange(span_z)[None, None, :] == source_safe[0] % span_z)
    )

    def inject(field, moment):
        return field + jnp.where(hit, source_gain[0] * wavelet[0, moment], 0.0)

    def wave_step(current, prior, moment, last):
        drive = speed_term * laplace_x(with_halo(current))
        if last:
            return None, drive
        later = inject(2.0 * current - prior + drive - absorber * (current - prior), moment)
        return later, drive

    def born_second(born, field_model, drive):
        return (
            2.0 * born
            + speed_term * laplace_x(with_halo(born))
            - absorber * born
            + field_model * drive
        )

    slab = span_x // n_shot
    depth = perturb.shape[2]
    model_held = perturb.transpose(2, 0, 1).reshape(1, depth, span_x * span_y)
    gains_held = gains[None]
    st = {"w0": wave_now[0], "wp": wave_prev[0]}

    def task_wave(i):
        def run():
            last = i == 3
            cur, pri = (st["w0"], st["wp"]) if i == 0 else (st["w%d" % i], st["w%d" % (i - 1)])
            later, drive = wave_step(cur, pri, i, last)
            st["drive%d" % i] = drive
            if not last:
                st["w%d" % (i + 1)] = later
        return run

    def run_group(comm, compute):
        moved = [step(held, k) for held, step, k in comm]
        compute()
        keys = sorted(st.keys())
        out = barrier((moved, [st[n] for n in keys]))
        st.update(zip(keys, out[1]))
        return out[0]

    def nothing():
        return None

    def early_waves():
        task_wave(0)()
        task_wave(1)()
        st["light"] = st["drive0"] * st["drive0"] + st["drive1"] * st["drive1"]

    ag_bits = list(reversed(bits))
    model_held, gains_held = run_group(
        [(model_held, ag_step, ag_bits[0]), (gains_held, ag_step, ag_bits[0])], early_waves
    )
    light_held = st["light"].reshape(n_shot, slab, span_y, span_z)
    tasks = [task_wave(2)]
    for i in range(1, len(bits)):
        model_held, gains_held, light_held = run_group(
            [
                (model_held, ag_step, ag_bits[i]),
                (gains_held, ag_step, ag_bits[i]),
                (light_held, rs_step, bits[i - 1]),
            ],
            tasks[i - 1] if i - 1 < len(tasks) else nothing,
        )
    for i in range(len(bits) - 1, len(tasks)):
        tasks[i]()

    def born_pass():
        model = model_held.reshape(span_z, span_x * span_y).T.reshape(span_x, span_y, span_z)
        st["born1"] = model * st["drive0"]
        st["born2"] = born_second(st["born1"], model, st["drive1"])

    (light_held,) = run_group([(light_held, rs_step, bits[-1])], born_pass)
    born1, born2 = st["born1"], st["born2"]

    image = st["drive0"] * born1 + st["drive1"] * born2
    image_held = image.reshape(n_shot, slab, span_y, span_z)
    tasks = [task_wave(3)]
    for i, k in enumerate(bits):
        (image_held,) = run_group([(image_held, rs_step, k)], tasks[i] if i < len(tasks) else nothing)
    for i in range(len(bits), len(tasks)):
        tasks[i]()

    table_all = gains_held.reshape(n_shot * gains.shape[0], gains.shape[1])
    filt_part = lateral_filter(image_held[0] / (light_held[0] + eps), table_all)
    filt_held = filt_part[None]
    for k in reversed(bits):
        filt_held = ag_step(filt_held, k)
    new_model = filt_held.reshape(span_x, span_y, span_z)
    filtered = lax.dynamic_slice_in_dim(new_model, me_shot * depth, depth, 2)

    b1 = new_model * st["drive2"]
    b2 = born_second(b1, new_model, st["drive3"])

    receiver_local = receiver_index[0] - offset
    receiver_owned = (receiver_local >= 0) & (receiver_local < cells)
    receiver_safe = jnp.clip(receiver_local, 0, cells - 1)
    row = receiver_safe // span_z
    rz = receiver_safe % span_z
    lane = jnp.arange(span_z)[None, :] == rz[:, None]

    def sample(field):
        rows = jnp.take(field.reshape(span_x * span_y, span_z), row, axis=0)
        picked = jnp.sum(jnp.where(lane, rows, 0.0), axis=1)
        return jnp.where(receiver_owned, picked, 0.0)

    records = jnp.stack([sample(b1), sample(b2)], axis=0)[None]
    traces = records + lax.ppermute(records, "space", [(0, 1), (1, 0)])
    return (filtered, b2[None], traces)


def solution(mesh):
    in_specs = (
        P(("dom", "shot"), "space", None, None),
        P(("dom", "shot"), "space", None, None),
        P(("dom", "space"), None, None),
        P(("dom", "space"), None, "shot"),
        P(("dom", "shot"), None),
        P(("dom", "shot"), None),
        P(("dom", "shot")),
        P(("dom", "shot"), None),
        P("dom"),
    )
    out_specs = (
        P(("dom", "space"), None, "shot"),
        P(("dom", "shot"), "space", None, None),
        P(("dom", "shot"), None, None),
    )
    return jax.shard_map(body, mesh=mesh, in_specs=in_specs, out_specs=out_specs, check_vma=False)
```

```python
import math

import jax
import jax.numpy as jnp
from jax import lax
from jax.sharding import PartitionSpec as P

STEPS_A = 2
STEPS_B = 2


STENCIL = (-205.0 / 72.0, 8.0 / 5.0, -1.0 / 5.0, 8.0 / 315.0, -1.0 / 560.0)
damp_peak = 0.5
eps = 1e-05
HALO = 4


def coefficient(levels):
    speed = 1500.0 + 15.0 * levels.astype(jnp.float32)
    ratio = 0.45 * speed / 5325.0
    return ratio * ratio


def ramp(position, count, lower, upper):
    low_part = jnp.maximum(lower - position, 0.0) / lower
    high_part = jnp.maximum(upper - (count - 1.0 - position), 0.0) / upper
    return low_part * low_part + high_part * high_part


def damping(widths, positions, count_x, count_y, count_z):
    edges = widths.astype(jnp.float32)
    along_x = ramp(positions, count_x, edges[0], edges[1])
    along_y = ramp(jnp.arange(count_y, dtype=jnp.float32), count_y, edges[2], edges[3])
    along_z = ramp(jnp.arange(count_z, dtype=jnp.float32), count_z, edges[4], edges[5])
    return damp_peak * (along_x[:, None, None] + along_y[None, :, None] + along_z[None, None, :])


def with_halo(x):
    size = lax.axis_size("space")
    length = x.shape[0]
    if size == 2:
        me = lax.axis_index("space")
        piece = lax.dynamic_slice_in_dim(x, (1 - me) * (length - HALO), HALO, 0)
        got = lax.ppermute(piece, "space", [(0, 1), (1, 0)])
        zeros = jnp.zeros((HALO,) + x.shape[1:], x.dtype)
        padded = jnp.concatenate([zeros, x, zeros], axis=0)
        return lax.dynamic_update_slice_in_dim(padded, got, (1 - me) * (length + HALO), 0)
    up = [(i, (i + 1) % size) for i in range(size - 1)]
    down = [(j, i) for i, j in up]
    before = lax.ppermute(x[length - HALO :], "space", up)
    after = lax.ppermute(x[:HALO], "space", down)
    return jnp.concatenate([before, x, after], axis=0)


def laplace_x(padded):
    width_x = padded.shape[0] - 8
    width_y = padded.shape[1]
    width_z = padded.shape[2]
    full = jnp.pad(padded, [(0, 0), (4, 4), (4, 4)])

    def part(move_x, move_y, move_z):
        return full[
            4 + move_x : 4 + move_x + width_x,
            4 + move_y : 4 + move_y + width_y,
            4 + move_z : 4 + move_z + width_z,
        ]

    total = 3.0 * STENCIL[0] * part(0, 0, 0)
    for reach in range(1, 5):
        beside_all = (
            part(reach, 0, 0)
            + part(-reach, 0, 0)
            + part(0, reach, 0)
            + part(0, -reach, 0)
            + part(0, 0, reach)
            + part(0, 0, -reach)
        )
        total = total + STENCIL[reach] * beside_all
    return total


def lateral_filter(field, table):
    count = field.shape[1]
    index = jnp.arange(count)
    phase = index[:, None] * index[None, :] % count
    angle = 2.0 * math.pi / count * phase.astype(jnp.float32)
    cosine = jnp.cos(angle)
    sine = jnp.sin(angle)
    real_part = jnp.einsum("xyz,yk->xzk", field, cosine, precision=lax.Precision.HIGHEST)
    imag_part = jnp.einsum("xyz,yk->xzk", field, sine, precision=lax.Precision.HIGHEST)
    weight = table[None, :, :]
    back = jnp.einsum("xzk,yk->xyz", real_part * weight, cosine, precision=lax.Precision.HIGHEST)
    back = back + jnp.einsum(
        "xzk,yk->xyz", imag_part * weight, sine, precision=lax.Precision.HIGHEST
    )
    return back / count


def shot_bits(n):
    bits = []
    k = 1
    while k < n:
        bits.append(k)
        k *= 2
    assert k == n
    return bits


def ag_step(held, k):
    n = lax.axis_size("shot")
    me = lax.axis_index("shot")
    theirs = lax.ppermute(held, "shot", [(i, i ^ k) for i in range(n)])
    low = (me // k) % 2 == 0
    pair = jnp.where(low, jnp.stack([held, theirs], axis=1), jnp.stack([theirs, held], axis=1))
    return pair.reshape((-1,) + held.shape[1:])


def rs_step(held, k):
    n = lax.axis_size("shot")
    me = lax.axis_index("shot")
    m = held.shape[0] // 2
    split = held.reshape((m, 2) + held.shape[1:])
    mine = (me // k) % 2
    keep = lax.dynamic_index_in_dim(split, mine, axis=1, keepdims=False)
    send = lax.dynamic_index_in_dim(split, 1 - mine, axis=1, keepdims=False)
    return keep + lax.ppermute(send, "shot", [(i, i ^ k) for i in range(n)])


def body(
    wave_prev,
    wave_now,
    velocity_code,
    perturb,
    gains,
    wavelet,
    source_index,
    receiver_index,
    absorb_width,
):
    shots, span_x, span_y, span_z = wave_now.shape
    n_shot = lax.axis_size("shot")
    me_shot = lax.axis_index("shot")
    bits = shot_bits(n_shot)
    start_x = lax.axis_index("space") * span_x
    total_x = span_x * lax.axis_size("space")
    speed_term = coefficient(velocity_code)
    positions = start_x.astype(jnp.float32) + jnp.arange(span_x, dtype=jnp.float32)
    absorber = damping(absorb_width, positions, total_x, span_y, span_z)
    term_flat = speed_term.reshape(-1)
    cells = span_x * span_y * span_z
    offset = start_x * span_y * span_z
    source_local = source_index - offset
    source_owned = (source_local >= 0) & (source_local < cells)
    source_safe = jnp.clip(source_local, 0, cells - 1)
    source_gain = jnp.where(source_owned, term_flat[source_safe], 0.0)
    barrier = lax.optimization_barrier

    plane = span_y * span_z
    hit = (
        (jnp.arange(span_x)[:, None, None] == source_safe[0] // plane)
        & (jnp.arange(span_y)[None, :, None] == (source_safe[0] // span_z) % span_y)
        & (jnp.arange(span_z)[None, None, :] == source_safe[0] % span_z)
    )

    def inject(field, moment):
        return field + jnp.where(hit, source_gain[0] * wavelet[0, moment], 0.0)

    def wave_step(current, prior, moment, last):
        drive = speed_term * laplace_x(with_halo(current))
        if last:
            return None, drive
        later = inject(2.0 * current - prior + drive - absorber * (current - prior), moment)
        return later, drive

    def born_second(born, field_model, drive):
        return (
            2.0 * born
            + speed_term * laplace_x(with_halo(born))
            - absorber * born
            + field_model * drive
        )

    slab = span_x // n_shot
    depth = perturb.shape[2]
    model_held = perturb.transpose(2, 0, 1).reshape(1, depth, span_x * span_y)
    gains_held = gains[None]
    st = {"w0": wave_now[0], "wp": wave_prev[0]}

    def task_wave(i):
        def run():
            last = i == 3
            cur, pri = (st["w0"], st["wp"]) if i == 0 else (st["w%d" % i], st["w%d" % (i - 1)])
            later, drive = wave_step(cur, pri, i, last)
            st["drive%d" % i] = drive
            if not last:
                st["w%d" % (i + 1)] = later
        return run

    def run_group(comm, compute):
        moved = [step(held, k) for held, step, k in comm]
        compute()
        keys = sorted(st.keys())
        out = barrier((moved, [st[n] for n in keys]))
        st.update(zip(keys, out[1]))
        return out[0]

    def nothing():
        return None

    def early_waves():
        task_wave(0)()
        task_wave(1)()
        st["light"] = st["drive0"] * st["drive0"] + st["drive1"] * st["drive1"]

    ag_bits = list(reversed(bits))
    model_held, gains_held = run_group(
        [(model_held, ag_step, ag_bits[0]), (gains_held, ag_step, ag_bits[0])], early_waves
    )
    light_held = st["light"].reshape(n_shot, slab, span_y, span_z)
    tasks = [task_wave(2)]
    for i in range(1, len(bits)):
        model_held, gains_held, light_held = run_group(
            [
                (model_held, ag_step, ag_bits[i]),
                (gains_held, ag_step, ag_bits[i]),
                (light_held, rs_step, bits[i - 1]),
            ],
            tasks[i - 1] if i - 1 < len(tasks) else nothing,
        )
    for i in range(len(bits) - 1, len(tasks)):
        tasks[i]()

    def born_pass():
        model = model_held.reshape(span_z, span_x * span_y).T.reshape(span_x, span_y, span_z)
        st["born1"] = model * st["drive0"]
        st["born2"] = born_second(st["born1"], model, st["drive1"])

    (light_held,) = run_group([(light_held, rs_step, bits[-1])], born_pass)
    born1, born2 = st["born1"], st["born2"]

    image = st["drive0"] * born1 + st["drive1"] * born2
    image_held = image.reshape(n_shot, slab, span_y, span_z)
    tasks = [task_wave(3)]
    for i, k in enumerate(bits):
        (image_held,) = run_group([(image_held, rs_step, k)], tasks[i] if i < len(tasks) else nothing)
    for i in range(len(bits), len(tasks)):
        tasks[i]()

    table_all = gains_held.reshape(n_shot * gains.shape[0], gains.shape[1])
    filt_part = lateral_filter(image_held[0] / (light_held[0] + eps), table_all)
    filt_held = filt_part[None]
    for k in reversed(bits):
        filt_held = ag_step(filt_held, k)
    new_model = filt_held.reshape(span_x, span_y, span_z)
    filtered = lax.dynamic_slice_in_dim(new_model, me_shot * depth, depth, 2)

    b1 = new_model * st["drive2"]
    b2 = born_second(b1, new_model, st["drive3"])

    receiver_local = receiver_index[0] - offset
    receiver_owned = (receiver_local >= 0) & (receiver_local < cells)
    receiver_safe = jnp.clip(receiver_local, 0, cells - 1)
    row = receiver_safe // span_z
    rz = receiver_safe % span_z
    lane = jnp.arange(span_z)[None, :] == rz[:, None]

    def sample(field):
        rows = jnp.take(field.reshape(span_x * span_y, span_z), row, axis=0)
        picked = jnp.sum(jnp.where(lane, rows, 0.0), axis=1)
        return jnp.where(receiver_owned, picked, 0.0)

    records = jnp.stack([sample(b1), sample(b2)], axis=0)[None]
    traces = records + lax.ppermute(records, "space", [(0, 1), (1, 0)])
    return (filtered, b2[None], traces)


def solution(mesh):
    in_specs = (
        P(("dom", "shot"), "space", None, None),
        P(("dom", "shot"), "space", None, None),
        P(("dom", "space"), None, None),
        P(("dom", "space"), None, "shot"),
        P(("dom", "shot"), None),
        P(("dom", "shot"), None),
        P(("dom", "shot")),
        P(("dom", "shot"), None),
        P("dom"),
    )
    out_specs = (
        P(("dom", "space"), None, "shot"),
        P(("dom", "shot"), "space", None, None),
        P(("dom", "shot"), None, None),
    )
    return jax.shard_map(body, mesh=mesh, in_specs=in_specs, out_specs=out_specs, check_vma=False)
```

```python
import math

import jax
import jax.numpy as jnp
from jax import lax
from jax.sharding import PartitionSpec as P

STEPS_A = 2
STEPS_B = 2


STENCIL = (-205.0 / 72.0, 8.0 / 5.0, -1.0 / 5.0, 8.0 / 315.0, -1.0 / 560.0)
damp_peak = 0.5
eps = 1e-05
HALO = 4


def coefficient(levels):
    speed = 1500.0 + 15.0 * levels.astype(jnp.float32)
    ratio = 0.45 * speed / 5325.0
    return ratio * ratio


def ramp(position, count, lower, upper):
    low_part = jnp.maximum(lower - position, 0.0) / lower
    high_part = jnp.maximum(upper - (count - 1.0 - position), 0.0) / upper
    return low_part * low_part + high_part * high_part


def damping(widths, positions, count_x, count_y, count_z):
    edges = widths.astype(jnp.float32)
    along_x = ramp(positions, count_x, edges[0], edges[1])
    along_y = ramp(jnp.arange(count_y, dtype=jnp.float32), count_y, edges[2], edges[3])
    along_z = ramp(jnp.arange(count_z, dtype=jnp.float32), count_z, edges[4], edges[5])
    return damp_peak * (along_x[:, None, None] + along_y[None, :, None] + along_z[None, None, :])


def with_halo(x):
    size = lax.axis_size("space")
    length = x.shape[0]
    if size == 2:
        me = lax.axis_index("space")
        piece = lax.dynamic_slice_in_dim(x, (1 - me) * (length - HALO), HALO, 0)
        got = lax.ppermute(piece, "space", [(0, 1), (1, 0)])
        zeros = jnp.zeros((HALO,) + x.shape[1:], x.dtype)
        padded = jnp.concatenate([zeros, x, zeros], axis=0)
        return lax.dynamic_update_slice_in_dim(padded, got, (1 - me) * (length + HALO), 0)
    up = [(i, (i + 1) % size) for i in range(size - 1)]
    down = [(j, i) for i, j in up]
    before = lax.ppermute(x[length - HALO :], "space", up)
    after = lax.ppermute(x[:HALO], "space", down)
    return jnp.concatenate([before, x, after], axis=0)


def laplace_x(padded):
    width_x = padded.shape[0] - 8
    width_y = padded.shape[1]
    width_z = padded.shape[2]
    full = jnp.pad(padded, [(0, 0), (4, 4), (4, 4)])

    def part(move_x, move_y, move_z):
        return full[
            4 + move_x : 4 + move_x + width_x,
            4 + move_y : 4 + move_y + width_y,
            4 + move_z : 4 + move_z + width_z,
        ]

    total = 3.0 * STENCIL[0] * part(0, 0, 0)
    for reach in range(1, 5):
        beside_all = (
            part(reach, 0, 0)
            + part(-reach, 0, 0)
            + part(0, reach, 0)
            + part(0, -reach, 0)
            + part(0, 0, reach)
            + part(0, 0, -reach)
        )
        total = total + STENCIL[reach] * beside_all
    return total


def lateral_filter(field, table):
    count = field.shape[1]
    index = jnp.arange(count)
    phase = index[:, None] * index[None, :] % count
    angle = 2.0 * math.pi / count * phase.astype(jnp.float32)
    cosine = jnp.cos(angle)
    sine = jnp.sin(angle)
    real_part = jnp.einsum("xyz,yk->xzk", field, cosine, precision=lax.Precision.HIGHEST)
    imag_part = jnp.einsum("xyz,yk->xzk", field, sine, precision=lax.Precision.HIGHEST)
    weight = table[None, :, :]
    back = jnp.einsum("xzk,yk->xyz", real_part * weight, cosine, precision=lax.Precision.HIGHEST)
    back = back + jnp.einsum(
        "xzk,yk->xyz", imag_part * weight, sine, precision=lax.Precision.HIGHEST
    )
    return back / count


def shot_bits(n):
    bits = []
    k = 1
    while k < n:
        bits.append(k)
        k *= 2
    assert k == n
    return bits


def ag_step(held, k):
    n = lax.axis_size("shot")
    me = lax.axis_index("shot")
    theirs = lax.ppermute(held, "shot", [(i, i ^ k) for i in range(n)])
    low = (me // k) % 2 == 0
    pair = jnp.where(low, jnp.stack([held, theirs], axis=1), jnp.stack([theirs, held], axis=1))
    return pair.reshape((-1,) + held.shape[1:])


def rs_step(held, k, left):
    n = lax.axis_size("shot")
    me = lax.axis_index("shot")
    low = 2 ** left.index(k)
    high = held.shape[0] // (2 * low)
    split = held.reshape((high, 2, low) + held.shape[1:])
    mine = (me // k) % 2
    keep = lax.dynamic_index_in_dim(split, mine, axis=1, keepdims=False)
    send = lax.dynamic_index_in_dim(split, 1 - mine, axis=1, keepdims=False)
    got = lax.ppermute(send, "shot", [(i, i ^ k) for i in range(n)])
    return (keep + got).reshape((high * low,) + held.shape[1:])


def body(
    wave_prev,
    wave_now,
    velocity_code,
    perturb,
    gains,
    wavelet,
    source_index,
    receiver_index,
    absorb_width,
):
    shots, span_x, span_y, span_z = wave_now.shape
    n_shot = lax.axis_size("shot")
    me_shot = lax.axis_index("shot")
    bits = shot_bits(n_shot)
    start_x = lax.axis_index("space") * span_x
    total_x = span_x * lax.axis_size("space")
    speed_term = coefficient(velocity_code)
    positions = start_x.astype(jnp.float32) + jnp.arange(span_x, dtype=jnp.float32)
    absorber = damping(absorb_width, positions, total_x, span_y, span_z)
    cells = span_x * span_y * span_z
    offset = start_x * span_y * span_z
    source_local = source_index - offset
    source_owned = (source_local >= 0) & (source_local < cells)
    source_safe = jnp.clip(source_local, 0, cells - 1)
    plane = span_y * span_z
    sx = source_safe[0] // plane
    sy = (source_safe[0] // span_z) % span_y
    sz = source_safe[0] % span_z
    source_code = lax.dynamic_slice(velocity_code, (sx, sy, sz), (1, 1, 1)).reshape(1)
    source_gain = jnp.where(source_owned, coefficient(source_code), 0.0)
    barrier = lax.optimization_barrier

    hit = (
        (jnp.arange(span_x)[:, None, None] == sx)
        & (jnp.arange(span_y)[None, :, None] == sy)
        & (jnp.arange(span_z)[None, None, :] == sz)
    )

    def inject(field, moment):
        return field + jnp.where(hit, source_gain[0] * wavelet[0, moment], 0.0)

    def wave_step(current, prior, moment, last):
        drive = speed_term * laplace_x(with_halo(current))
        if last:
            return None, drive
        later = inject(2.0 * current - prior + drive - absorber * (current - prior), moment)
        return later, drive

    def born_second(born, field_model, drive):
        return (
            2.0 * born
            + speed_term * laplace_x(with_halo(born))
            - absorber * born
            + field_model * drive
        )

    slab = span_x // n_shot
    depth = perturb.shape[2]
    model_held = perturb.transpose(2, 0, 1).reshape(1, depth, span_x * span_y)
    gains_held = gains[None]
    st = {"w0": wave_now[0], "wp": wave_prev[0]}

    def task_wave(i):
        def run():
            last = i == 3
            cur, pri = (st["w0"], st["wp"]) if i == 0 else (st["w%d" % i], st["w%d" % (i - 1)])
            later, drive = wave_step(cur, pri, i, last)
            st["drive%d" % i] = drive
            if not last:
                st["w%d" % (i + 1)] = later
        return run

    def run_group(comm, compute):
        moved = [step(held, k) for held, step, k in comm]
        compute()
        keys = sorted(st.keys())
        out = barrier((moved, [st[n] for n in keys]))
        st.update(zip(keys, out[1]))
        return out[0]

    def nothing():
        return None

    def light_prep():
        task_wave(1)()
        st["light"] = st["drive0"] * st["drive0"] + st["drive1"] * st["drive1"]

    ag_bits = list(reversed(bits))
    tasks = [task_wave(0), light_prep]
    for i, k in enumerate(ag_bits[:-1]):
        model_held, gains_held = run_group(
            [(model_held, ag_step, k), (gains_held, ag_step, k)],
            tasks[i] if i < len(tasks) else nothing,
        )
    for i in range(len(bits) - 1, len(tasks)):
        tasks[i]()
    light_held = st["light"].reshape(n_shot, slab, span_y, span_z)
    light_order = bits[1:] + bits[:1]
    light_left = list(bits)
    model_held, gains_held, light_held = run_group(
        [
            (model_held, ag_step, ag_bits[-1]),
            (gains_held, ag_step, ag_bits[-1]),
            (light_held, lambda h, k: rs_step(h, k, light_left), light_order[0]),
        ],
        task_wave(2),
    )
    light_left.remove(light_order[0])

    def born_pass():
        model = model_held.reshape(span_z, span_x * span_y).T.reshape(span_x, span_y, span_z)
        st["born1"] = model * st["drive0"]
        st["born2"] = born_second(st["born1"], model, st["drive1"])

    light_rest = light_order[1:]
    (light_held,) = run_group([(light_held, lambda h, k: rs_step(h, k, light_left), light_rest[0])], born_pass)
    light_left.remove(light_rest[0])
    light_rest = light_rest[1:]
    born1, born2 = st["born1"], st["born2"]

    image = st["drive0"] * born1 + st["drive1"] * born2
    image_held = image.reshape(n_shot, slab, span_y, span_z)
    image_left = list(bits)
    tasks = [task_wave(3)]
    for i, k in enumerate(bits):
        comm = [(image_held, lambda h, kk: rs_step(h, kk, image_left), k)]
        if i < len(light_rest):
            comm.append((light_held, lambda h, kk: rs_step(h, kk, light_left), light_rest[i]))
        moved = run_group(comm, tasks[i] if i < len(tasks) else nothing)
        image_held = moved[0]
        image_left.remove(k)
        if i < len(light_rest):
            light_held = moved[1]
            light_left.remove(light_rest[i])
    for i in range(len(bits), len(tasks)):
        tasks[i]()

    table_all = gains_held.reshape(n_shot * gains.shape[0], gains.shape[1])
    filt_part = lateral_filter(image_held[0] / (light_held[0] + eps), table_all)
    filt_held = filt_part[None]
    for k in reversed(bits):
        filt_held = ag_step(filt_held, k)
    new_model = filt_held.reshape(span_x, span_y, span_z)
    filtered = lax.dynamic_slice_in_dim(new_model, me_shot * depth, depth, 2)

    b1 = new_model * st["drive2"]
    b2 = born_second(b1, new_model, st["drive3"])

    receiver_local = receiver_index[0] - offset
    receiver_owned = (receiver_local >= 0) & (receiver_local < cells)
    receiver_safe = jnp.clip(receiver_local, 0, cells - 1)
    row = receiver_safe // span_z
    rz = receiver_safe % span_z
    lane = jnp.arange(span_z)[None, :] == rz[:, None]

    def sample(field):
        rows = jnp.take(field.reshape(span_x * span_y, span_z), row, axis=0)
        picked = jnp.sum(jnp.where(lane, rows, 0.0), axis=1)
        return jnp.where(receiver_owned, picked, 0.0)

    records = jnp.stack([sample(b1), sample(b2)], axis=0)[None]
    traces = records + lax.ppermute(records, "space", [(0, 1), (1, 0)])
    return (filtered, b2[None], traces)


def solution(mesh):
    in_specs = (
        P(("dom", "shot"), "space", None, None),
        P(("dom", "shot"), "space", None, None),
        P(("dom", "space"), None, None),
        P(("dom", "space"), None, "shot"),
        P(("dom", "shot"), None),
        P(("dom", "shot"), None),
        P(("dom", "shot")),
        P(("dom", "shot"), None),
        P("dom"),
    )
    out_specs = (
        P(("dom", "space"), None, "shot"),
        P(("dom", "shot"), "space", None, None),
        P(("dom", "shot"), None, None),
    )
    return jax.shard_map(body, mesh=mesh, in_specs=in_specs, out_specs=out_specs, check_vma=False)
```

```python
import math

import jax
import jax.numpy as jnp
from jax import lax
from jax.sharding import PartitionSpec as P

STEPS_A = 2
STEPS_B = 2


STENCIL = (-205.0 / 72.0, 8.0 / 5.0, -1.0 / 5.0, 8.0 / 315.0, -1.0 / 560.0)
damp_peak = 0.5
eps = 1e-05
HALO = 4


def coefficient(levels):
    speed = 1500.0 + 15.0 * levels.astype(jnp.float32)
    ratio = 0.45 * speed / 5325.0
    return ratio * ratio


def ramp(position, count, lower, upper):
    low_part = jnp.maximum(lower - position, 0.0) / lower
    high_part = jnp.maximum(upper - (count - 1.0 - position), 0.0) / upper
    return low_part * low_part + high_part * high_part


def damping(widths, positions, count_x, count_y, count_z):
    edges = widths.astype(jnp.float32)
    along_x = ramp(positions, count_x, edges[0], edges[1])
    along_y = ramp(jnp.arange(count_y, dtype=jnp.float32), count_y, edges[2], edges[3])
    along_z = ramp(jnp.arange(count_z, dtype=jnp.float32), count_z, edges[4], edges[5])
    return damp_peak * (along_x[:, None, None] + along_y[None, :, None] + along_z[None, None, :])


def with_halo(x):
    size = lax.axis_size("space")
    length = x.shape[0]
    if size == 2:
        me = lax.axis_index("space")
        piece = lax.dynamic_slice_in_dim(x, (1 - me) * (length - HALO), HALO, 0)
        got = lax.ppermute(piece, "space", [(0, 1), (1, 0)])
        zeros = jnp.zeros((HALO,) + x.shape[1:], x.dtype)
        padded = jnp.concatenate([zeros, x, zeros], axis=0)
        return lax.dynamic_update_slice_in_dim(padded, got, (1 - me) * (length + HALO), 0)
    up = [(i, (i + 1) % size) for i in range(size - 1)]
    down = [(j, i) for i, j in up]
    before = lax.ppermute(x[length - HALO :], "space", up)
    after = lax.ppermute(x[:HALO], "space", down)
    return jnp.concatenate([before, x, after], axis=0)


def laplace_x(padded):
    width_x = padded.shape[0] - 8
    width_y = padded.shape[1]
    width_z = padded.shape[2]
    full = jnp.pad(padded, [(0, 0), (4, 4), (4, 4)])

    def part(move_x, move_y, move_z):
        return full[
            4 + move_x : 4 + move_x + width_x,
            4 + move_y : 4 + move_y + width_y,
            4 + move_z : 4 + move_z + width_z,
        ]

    total = 3.0 * STENCIL[0] * part(0, 0, 0)
    for reach in range(1, 5):
        beside_all = (
            part(reach, 0, 0)
            + part(-reach, 0, 0)
            + part(0, reach, 0)
            + part(0, -reach, 0)
            + part(0, 0, reach)
            + part(0, 0, -reach)
        )
        total = total + STENCIL[reach] * beside_all
    return total


def lateral_filter(field, table):
    count = field.shape[1]
    index = jnp.arange(count)
    phase = index[:, None] * index[None, :] % count
    angle = 2.0 * math.pi / count * phase.astype(jnp.float32)
    cosine = jnp.cos(angle)
    sine = jnp.sin(angle)
    real_part = jnp.einsum("xyz,yk->xzk", field, cosine, precision=lax.Precision.HIGHEST)
    imag_part = jnp.einsum("xyz,yk->xzk", field, sine, precision=lax.Precision.HIGHEST)
    weight = table[None, :, :]
    back = jnp.einsum("xzk,yk->xyz", real_part * weight, cosine, precision=lax.Precision.HIGHEST)
    back = back + jnp.einsum(
        "xzk,yk->xyz", imag_part * weight, sine, precision=lax.Precision.HIGHEST
    )
    return back / count


def shot_bits(n):
    bits = []
    k = 1
    while k < n:
        bits.append(k)
        k *= 2
    assert k == n
    return bits


def ag_step(held, k, done):
    n = lax.axis_size("shot")
    me = lax.axis_index("shot")
    theirs = lax.ppermute(held, "shot", [(i, i ^ k) for i in range(n)])
    low = 2 ** sum(1 for b in done if b < k)
    shape = (held.shape[0] // low, 1, low) + held.shape[1:]
    mine, other = held.reshape(shape), theirs.reshape(shape)
    first = (me // k) % 2 == 0
    pair = jnp.where(first, jnp.concatenate([mine, other], axis=1), jnp.concatenate([other, mine], axis=1))
    return pair.reshape((2 * held.shape[0],) + held.shape[1:])


def swap_first(order):
    return order[1:2] + order[:1] + order[2:]


def swap_last(order):
    return order[:-2] + order[-1:] + order[-2:-1] if len(order) > 1 else order


def chain(held, kind, order):
    return {"held": held, "kind": kind, "order": list(order), "i": 0, "bits": [] if kind == "ag" else sorted(order)}


def chain_step(c):
    k = c["order"][c["i"]]
    if c["kind"] == "ag":
        return ag_step(c["held"], k, c["bits"])
    return rs_step(c["held"], k, c["bits"])


def chain_commit(c, held):
    k = c["order"][c["i"]]
    c["held"] = held
    c["i"] += 1
    if c["kind"] == "ag":
        c["bits"].append(k)
    else:
        c["bits"].remove(k)


def rs_step(held, k, left):
    n = lax.axis_size("shot")
    me = lax.axis_index("shot")
    low = 2 ** left.index(k)
    high = held.shape[0] // (2 * low)
    split = held.reshape((high, 2, low) + held.shape[1:])
    mine = (me // k) % 2
    keep = lax.dynamic_index_in_dim(split, mine, axis=1, keepdims=False)
    send = lax.dynamic_index_in_dim(split, 1 - mine, axis=1, keepdims=False)
    got = lax.ppermute(send, "shot", [(i, i ^ k) for i in range(n)])
    return (keep + got).reshape((high * low,) + held.shape[1:])


def body(
    wave_prev,
    wave_now,
    velocity_code,
    perturb,
    gains,
    wavelet,
    source_index,
    receiver_index,
    absorb_width,
):
    shots, span_x, span_y, span_z = wave_now.shape
    n_shot = lax.axis_size("shot")
    me_shot = lax.axis_index("shot")
    bits = shot_bits(n_shot)
    start_x = lax.axis_index("space") * span_x
    total_x = span_x * lax.axis_size("space")
    speed_term = coefficient(velocity_code)
    positions = start_x.astype(jnp.float32) + jnp.arange(span_x, dtype=jnp.float32)
    absorber = damping(absorb_width, positions, total_x, span_y, span_z)
    cells = span_x * span_y * span_z
    offset = start_x * span_y * span_z
    source_local = source_index - offset
    source_owned = (source_local >= 0) & (source_local < cells)
    source_safe = jnp.clip(source_local, 0, cells - 1)
    plane = span_y * span_z
    sx = source_safe[0] // plane
    sy = (source_safe[0] // span_z) % span_y
    sz = source_safe[0] % span_z
    source_code = lax.dynamic_slice(velocity_code, (sx, sy, sz), (1, 1, 1)).reshape(1)
    source_gain = jnp.where(source_owned, coefficient(source_code), 0.0)
    barrier = lax.optimization_barrier

    hit = (
        (jnp.arange(span_x)[:, None, None] == sx)
        & (jnp.arange(span_y)[None, :, None] == sy)
        & (jnp.arange(span_z)[None, None, :] == sz)
    )

    def inject(field, moment):
        return field + jnp.where(hit, source_gain[0] * wavelet[0, moment], 0.0)

    def wave_step(current, prior, moment, last):
        drive = speed_term * laplace_x(with_halo(current))
        if last:
            return None, drive
        later = inject(2.0 * current - prior + drive - absorber * (current - prior), moment)
        return later, drive

    def born_second(born, field_model, drive):
        return (
            2.0 * born
            + speed_term * laplace_x(with_halo(born))
            - absorber * born
            + field_model * drive
        )

    slab = span_x // n_shot
    depth = perturb.shape[2]
    model_held = perturb.transpose(2, 0, 1).reshape(1, depth, span_x * span_y)
    gains_held = gains[None]
    st = {"w0": wave_now[0], "wp": wave_prev[0]}

    def task_wave(i):
        def run():
            last = i == 3
            cur, pri = (st["w0"], st["wp"]) if i == 0 else (st["w%d" % i], st["w%d" % (i - 1)])
            later, drive = wave_step(cur, pri, i, last)
            st["drive%d" % i] = drive
            if not last:
                st["w%d" % (i + 1)] = later
        return run

    def run_group(chains, compute):
        chains = [c for c in chains if c["i"] < len(c["order"])]
        moved = [chain_step(c) for c in chains]
        compute()
        keys = sorted(st.keys())
        out = barrier((moved, [st[n] for n in keys]))
        st.update(zip(keys, out[1]))
        for c, held in zip(chains, out[0]):
            chain_commit(c, held)

    def nothing():
        return None

    def light_prep():
        task_wave(1)()
        st["light"] = st["drive0"] * st["drive0"] + st["drive1"] * st["drive1"]

    def halves(x, axis):
        h = x.shape[axis] // 2
        return lax.slice_in_dim(x, 0, h, axis=axis), lax.slice_in_dim(x, h, x.shape[axis], axis=axis)

    far_first = list(reversed(bits))
    near_first = list(bits)

    half_a, half_b = halves(model_held, 1)
    model_a = chain(half_a, "ag", far_first)
    model_b = chain(half_b, "ag", swap_last(far_first))
    gains_c = chain(gains_held, "ag", far_first)
    tasks = [task_wave(0), light_prep, task_wave(2)]
    for i in range(len(bits)):
        run_group([model_a, model_b, gains_c], tasks[i] if i < len(tasks) else nothing)
    for i in range(len(bits), len(tasks)):
        tasks[i]()
    model_held = jnp.concatenate([model_a["held"], model_b["held"]], axis=1)
    gains_held = gains_c["held"]
    light_a, light_b = halves(st["light"].reshape(n_shot, slab, span_y, span_z), 2)
    light_a = chain(light_a, "rs", near_first)
    light_b = chain(light_b, "rs", swap_first(near_first))

    def born_pass():
        model = model_held.reshape(span_z, span_x * span_y).T.reshape(span_x, span_y, span_z)
        st["born1"] = model * st["drive0"]
        st["born2"] = born_second(st["born1"], model, st["drive1"])

    run_group([light_a, light_b], born_pass)
    born1, born2 = st["born1"], st["born2"]

    image = st["drive0"] * born1 + st["drive1"] * born2
    image_a, image_b = halves(image.reshape(n_shot, slab, span_y, span_z), 2)
    image_a = chain(image_a, "rs", near_first)
    image_b = chain(image_b, "rs", swap_first(near_first))
    tasks = [task_wave(3)]
    for i in range(len(bits)):
        run_group([image_a, image_b, light_a, light_b], tasks[i] if i < len(tasks) else nothing)
    for i in range(len(bits), len(tasks)):
        tasks[i]()
    image_part = jnp.concatenate([image_a["held"][0], image_b["held"][0]], axis=1)
    light_part = jnp.concatenate([light_a["held"][0], light_b["held"][0]], axis=1)

    table_all = gains_held.reshape(n_shot * gains.shape[0], gains.shape[1])
    filt_part = lateral_filter(image_part / (light_part + eps), table_all)
    part_a, part_b = halves(filt_part[None], 2)
    filt_a = chain(part_a, "ag", far_first)
    filt_b = chain(part_b, "ag", swap_last(far_first))
    for i in range(len(bits)):
        run_group([filt_a, filt_b], nothing)
    new_model = jnp.concatenate([filt_a["held"], filt_b["held"]], axis=2).reshape(span_x, span_y, span_z)
    filtered = lax.dynamic_slice_in_dim(new_model, me_shot * depth, depth, 2)

    b1 = new_model * st["drive2"]
    b2 = born_second(b1, new_model, st["drive3"])

    receiver_local = receiver_index[0] - offset
    receiver_owned = (receiver_local >= 0) & (receiver_local < cells)
    receiver_safe = jnp.clip(receiver_local, 0, cells - 1)
    row = receiver_safe // span_z
    rz = receiver_safe % span_z
    lane = jnp.arange(span_z)[None, :] == rz[:, None]

    def sample(field):
        rows = jnp.take(field.reshape(span_x * span_y, span_z), row, axis=0)
        picked = jnp.sum(jnp.where(lane, rows, 0.0), axis=1)
        return jnp.where(receiver_owned, picked, 0.0)

    records = jnp.stack([sample(b1), sample(b2)], axis=0)[None]
    traces = records + lax.ppermute(records, "space", [(0, 1), (1, 0)])
    return (filtered, b2[None], traces)


def solution(mesh):
    in_specs = (
        P(("dom", "shot"), "space", None, None),
        P(("dom", "shot"), "space", None, None),
        P(("dom", "space"), None, None),
        P(("dom", "space"), None, "shot"),
        P(("dom", "shot"), None),
        P(("dom", "shot"), None),
        P(("dom", "shot")),
        P(("dom", "shot"), None),
        P("dom"),
    )
    out_specs = (
        P(("dom", "space"), None, "shot"),
        P(("dom", "shot"), "space", None, None),
        P(("dom", "shot"), None, None),
    )
    return jax.shard_map(body, mesh=mesh, in_specs=in_specs, out_specs=out_specs, check_vma=False)
```

```python
import math

import jax
import jax.numpy as jnp
from jax import lax
from jax.sharding import PartitionSpec as P

STEPS_A = 2
STEPS_B = 2


STENCIL = (-205.0 / 72.0, 8.0 / 5.0, -1.0 / 5.0, 8.0 / 315.0, -1.0 / 560.0)
damp_peak = 0.5
eps = 1e-05
HALO = 4


def coefficient(levels):
    speed = 1500.0 + 15.0 * levels.astype(jnp.float32)
    ratio = 0.45 * speed / 5325.0
    return ratio * ratio


def ramp(position, count, lower, upper):
    low_part = jnp.maximum(lower - position, 0.0) / lower
    high_part = jnp.maximum(upper - (count - 1.0 - position), 0.0) / upper
    return low_part * low_part + high_part * high_part


def damping(widths, positions, count_x, count_y, count_z):
    edges = widths.astype(jnp.float32)
    longest = max(positions.shape[0], count_y, count_z)
    line = jnp.arange(longest, dtype=jnp.float32)
    x_line = jnp.pad(positions, (0, longest - positions.shape[0]))
    place = jnp.stack([x_line, line, line])
    count = jnp.stack([jnp.asarray(count_x, jnp.float32), jnp.float32(count_y), jnp.float32(count_z)])[:, None]
    lower = jnp.stack([edges[0], edges[2], edges[4]])[:, None]
    upper = jnp.stack([edges[1], edges[3], edges[5]])[:, None]
    ramps = ramp(place, count, lower, upper)
    along_x = ramps[0, : positions.shape[0]]
    along_y = ramps[1, :count_y]
    along_z = ramps[2, :count_z]
    return damp_peak * (along_x[:, None, None] + along_y[None, :, None] + along_z[None, None, :])


def with_halo(x):
    size = lax.axis_size("space")
    length = x.shape[0]
    if size == 2:
        me = lax.axis_index("space")
        piece = lax.dynamic_slice_in_dim(x, (1 - me) * (length - HALO), HALO, 0)
        got = lax.ppermute(piece, "space", [(0, 1), (1, 0)])
        zeros = jnp.zeros((HALO,) + x.shape[1:], x.dtype)
        padded = jnp.concatenate([zeros, x, zeros], axis=0)
        return lax.dynamic_update_slice_in_dim(padded, got, (1 - me) * (length + HALO), 0)
    up = [(i, (i + 1) % size) for i in range(size - 1)]
    down = [(j, i) for i, j in up]
    before = lax.ppermute(x[length - HALO :], "space", up)
    after = lax.ppermute(x[:HALO], "space", down)
    return jnp.concatenate([before, x, after], axis=0)


def laplace_x(padded):
    width_x = padded.shape[0] - 8
    width_y = padded.shape[1]
    width_z = padded.shape[2]
    full = jnp.pad(padded, [(0, 0), (4, 4), (4, 4)])

    def part(move_x, move_y, move_z):
        return full[
            4 + move_x : 4 + move_x + width_x,
            4 + move_y : 4 + move_y + width_y,
            4 + move_z : 4 + move_z + width_z,
        ]

    total = 3.0 * STENCIL[0] * part(0, 0, 0)
    for reach in range(1, 5):
        beside_all = (
            part(reach, 0, 0)
            + part(-reach, 0, 0)
            + part(0, reach, 0)
            + part(0, -reach, 0)
            + part(0, 0, reach)
            + part(0, 0, -reach)
        )
        total = total + STENCIL[reach] * beside_all
    return total


def lateral_filter(field, table):
    count = field.shape[1]
    index = jnp.arange(count)
    phase = index[:, None] * index[None, :] % count
    angle = 2.0 * math.pi / count * phase.astype(jnp.float32)
    cosine = jnp.cos(angle)
    sine = jnp.sin(angle)
    real_part = jnp.einsum("xyz,yk->xzk", field, cosine, precision=lax.Precision.HIGHEST)
    imag_part = jnp.einsum("xyz,yk->xzk", field, sine, precision=lax.Precision.HIGHEST)
    weight = table[None, :, :]
    back = jnp.einsum("xzk,yk->xyz", real_part * weight, cosine, precision=lax.Precision.HIGHEST)
    back = back + jnp.einsum(
        "xzk,yk->xyz", imag_part * weight, sine, precision=lax.Precision.HIGHEST
    )
    return back / count


def shot_bits(n):
    bits = []
    k = 1
    while k < n:
        bits.append(k)
        k *= 2
    assert k == n
    return bits


def ag_step(held, k, done):
    n = lax.axis_size("shot")
    me = lax.axis_index("shot")
    theirs = lax.ppermute(held, "shot", [(i, i ^ k) for i in range(n)])
    low = 2 ** sum(1 for b in done if b < k)
    shape = (held.shape[0] // low, 1, low) + held.shape[1:]
    mine, other = held.reshape(shape), theirs.reshape(shape)
    first = (me // k) % 2 == 0
    pair = jnp.where(first, jnp.concatenate([mine, other], axis=1), jnp.concatenate([other, mine], axis=1))
    return pair.reshape((2 * held.shape[0],) + held.shape[1:])


def swap_first(order):
    return order[1:2] + order[:1] + order[2:]


def swap_last(order):
    return order[:-2] + order[-1:] + order[-2:-1] if len(order) > 1 else order


def chain(held, kind, order, bits=None):
    if bits is None:
        bits = [] if kind == "ag" else sorted(order)
    return {"held": held, "kind": kind, "order": list(order), "i": 0, "bits": list(bits)}


def chain_step(c):
    k = c["order"][c["i"]]
    if c["kind"] == "ag":
        return ag_step(c["held"], k, c["bits"])
    return rs_step(c["held"], k, c["bits"])


def chain_commit(c, held):
    k = c["order"][c["i"]]
    c["held"] = held
    c["i"] += 1
    if c["kind"] == "ag":
        c["bits"].append(k)
    else:
        c["bits"].remove(k)


def rs_step(held, k, left):
    n = lax.axis_size("shot")
    me = lax.axis_index("shot")
    low = 2 ** left.index(k)
    high = held.shape[0] // (2 * low)
    split = held.reshape((high, 2, low) + held.shape[1:])
    mine = (me // k) % 2
    keep = lax.dynamic_index_in_dim(split, mine, axis=1, keepdims=False)
    send = lax.dynamic_index_in_dim(split, 1 - mine, axis=1, keepdims=False)
    got = lax.ppermute(send, "shot", [(i, i ^ k) for i in range(n)])
    return (keep + got).reshape((high * low,) + held.shape[1:])


def body(
    wave_prev,
    wave_now,
    velocity_code,
    perturb,
    gains,
    wavelet,
    source_index,
    receiver_index,
    absorb_width,
):
    shots, span_x, span_y, span_z = wave_now.shape
    n_shot = lax.axis_size("shot")
    me_shot = lax.axis_index("shot")
    bits = shot_bits(n_shot)
    start_x = lax.axis_index("space") * span_x
    total_x = span_x * lax.axis_size("space")
    speed_term = coefficient(velocity_code)
    positions = start_x.astype(jnp.float32) + jnp.arange(span_x, dtype=jnp.float32)
    absorber = damping(absorb_width, positions, total_x, span_y, span_z)
    cells = span_x * span_y * span_z
    offset = start_x * span_y * span_z
    source_local = source_index - offset
    source_owned = (source_local >= 0) & (source_local < cells)
    source_safe = jnp.clip(source_local, 0, cells - 1)
    plane = span_y * span_z
    sx = source_safe[0] // plane
    sy = (source_safe[0] // span_z) % span_y
    sz = source_safe[0] % span_z
    source_code = lax.dynamic_slice(velocity_code, (sx, sy, sz), (1, 1, 1)).reshape(1)
    source_gain = jnp.where(source_owned, coefficient(source_code), 0.0)
    barrier = lax.optimization_barrier

    hit = (
        (jnp.arange(span_x)[:, None, None] == sx)
        & (jnp.arange(span_y)[None, :, None] == sy)
        & (jnp.arange(span_z)[None, None, :] == sz)
    )

    def inject(field, moment):
        return field + jnp.where(hit, source_gain[0] * wavelet[0, moment], 0.0)

    def wave_step(current, prior, moment, last):
        drive = speed_term * laplace_x(with_halo(current))
        if last:
            return None, drive
        later = inject(2.0 * current - prior + drive - absorber * (current - prior), moment)
        return later, drive

    def born_second(born, field_model, drive):
        return (
            2.0 * born
            + speed_term * laplace_x(with_halo(born))
            - absorber * born
            + field_model * drive
        )

    slab = span_x // n_shot
    depth = perturb.shape[2]
    model_held = perturb.transpose(2, 0, 1).reshape(1, depth, span_x * span_y)
    gains_held = gains[None]
    st = {"w0": wave_now[0], "wp": wave_prev[0]}

    def task_wave(i):
        def run():
            last = i == 3
            cur, pri = (st["w0"], st["wp"]) if i == 0 else (st["w%d" % i], st["w%d" % (i - 1)])
            later, drive = wave_step(cur, pri, i, last)
            st["drive%d" % i] = drive
            if not last:
                st["w%d" % (i + 1)] = later
        return run

    def run_group(chains, compute):
        chains = [c for c in chains if c["i"] < len(c["order"])]
        moved = [chain_step(c) for c in chains]
        compute()
        keys = sorted(st.keys())
        out = barrier((moved, [st[n] for n in keys]))
        st.update(zip(keys, out[1]))
        for c, held in zip(chains, out[0]):
            chain_commit(c, held)

    def nothing():
        return None

    def light_prep():
        task_wave(1)()
        st["light"] = st["drive0"] * st["drive0"] + st["drive1"] * st["drive1"]

    def halves(x, axis):
        h = x.shape[axis] // 2
        return lax.slice_in_dim(x, 0, h, axis=axis), lax.slice_in_dim(x, h, x.shape[axis], axis=axis)

    far_first = list(reversed(bits))
    near_first = list(bits)

    top = far_first[0]
    model_c = chain(model_held, "ag", far_first[:1])
    gains_c = chain(gains_held, "ag", far_first)
    tasks = [task_wave(0), light_prep, task_wave(2)]
    run_group([model_c, gains_c], tasks[0])
    half_a, half_b = halves(model_c["held"], 1)
    model_a = chain(half_a, "ag", far_first[1:], [top])
    model_b = chain(half_b, "ag", swap_first(far_first[1:]), [top])
    for i in range(1, len(bits)):
        run_group([model_a, model_b, gains_c], tasks[i] if i < len(tasks) else nothing)
    for i in range(len(bits), len(tasks)):
        tasks[i]()
    model_held = jnp.concatenate([model_a["held"], model_b["held"]], axis=1)
    gains_held = gains_c["held"]
    light_a, light_b = halves(st["light"].reshape(n_shot, slab, span_y, span_z), 2)
    light_a = chain(light_a, "rs", near_first[:-1], near_first)
    light_b = chain(light_b, "rs", swap_first(near_first[:-1]), near_first)

    def born_pass():
        model = model_held.reshape(span_z, span_x * span_y).T.reshape(span_x, span_y, span_z)
        st["born1"] = model * st["drive0"]
        st["born2"] = born_second(st["born1"], model, st["drive1"])

    run_group([light_a, light_b], born_pass)
    born1, born2 = st["born1"], st["born2"]

    image = st["drive0"] * born1 + st["drive1"] * born2
    image_a, image_b = halves(image.reshape(n_shot, slab, span_y, span_z), 2)
    image_a = chain(image_a, "rs", near_first[:-1], near_first)
    image_b = chain(image_b, "rs", swap_first(near_first[:-1]), near_first)
    tasks = [task_wave(3)]
    for i in range(len(bits) - 1):
        run_group([image_a, image_b, light_a, light_b], tasks[i] if i < len(tasks) else nothing)
    for i in range(len(bits) - 1, len(tasks)):
        tasks[i]()
    both = jnp.concatenate(
        [
            jnp.concatenate([image_a["held"], image_b["held"]], axis=2),
            jnp.concatenate([light_a["held"], light_b["held"]], axis=2),
        ],
        axis=1,
    )
    last = chain(both, "rs", near_first[-1:], near_first[-1:])
    run_group([last], nothing)
    image_part = last["held"][0, :slab]
    light_part = last["held"][0, slab:]

    table_all = gains_held.reshape(n_shot * gains.shape[0], gains.shape[1])
    filt_part = lateral_filter(image_part / (light_part + eps), table_all)
    filt_c = chain(filt_part[None], "ag", far_first[:1])
    run_group([filt_c], nothing)
    part_a, part_b = halves(filt_c["held"], 2)
    filt_a = chain(part_a, "ag", far_first[1:], [top])
    filt_b = chain(part_b, "ag", swap_first(far_first[1:]), [top])
    for i in range(1, len(bits)):
        run_group([filt_a, filt_b], nothing)
    new_model = jnp.concatenate([filt_a["held"], filt_b["held"]], axis=2).reshape(span_x, span_y, span_z)
    filtered = lax.dynamic_slice_in_dim(new_model, me_shot * depth, depth, 2)

    b1 = new_model * st["drive2"]
    b2 = born_second(b1, new_model, st["drive3"])

    receiver_local = receiver_index[0] - offset
    receiver_owned = (receiver_local >= 0) & (receiver_local < cells)
    receiver_safe = jnp.clip(receiver_local, 0, cells - 1)
    row = receiver_safe // span_z
    rz = receiver_safe % span_z
    lane = jnp.arange(span_z)[None, :] == rz[:, None]

    def sample(field):
        rows = jnp.take(field.reshape(span_x * span_y, span_z), row, axis=0)
        picked = jnp.sum(jnp.where(lane, rows, 0.0), axis=1)
        return jnp.where(receiver_owned, picked, 0.0)

    records = jnp.stack([sample(b1), sample(b2)], axis=0)[None]
    traces = records + lax.ppermute(records, "space", [(0, 1), (1, 0)])
    return (filtered, b2[None], traces)


def solution(mesh):
    in_specs = (
        P(("dom", "shot"), "space", None, None),
        P(("dom", "shot"), "space", None, None),
        P(("dom", "space"), None, None),
        P(("dom", "space"), None, "shot"),
        P(("dom", "shot"), None),
        P(("dom", "shot"), None),
        P(("dom", "shot")),
        P(("dom", "shot"), None),
        P("dom"),
    )
    out_specs = (
        P(("dom", "space"), None, "shot"),
        P(("dom", "shot"), "space", None, None),
        P(("dom", "shot"), None, None),
    )
    return jax.shard_map(body, mesh=mesh, in_specs=in_specs, out_specs=out_specs, check_vma=False)
```

```python
import math

import jax
import jax.numpy as jnp
from jax import lax
from jax.sharding import PartitionSpec as P

STEPS_A = 2
STEPS_B = 2


STENCIL = (-205.0 / 72.0, 8.0 / 5.0, -1.0 / 5.0, 8.0 / 315.0, -1.0 / 560.0)
damp_peak = 0.5
eps = 1e-05
HALO = 4


def coefficient(levels):
    speed = 1500.0 + 15.0 * levels.astype(jnp.float32)
    ratio = 0.45 * speed / 5325.0
    return ratio * ratio


def ramp(position, count, lower, upper):
    low_part = jnp.maximum(lower - position, 0.0) / lower
    high_part = jnp.maximum(upper - (count - 1.0 - position), 0.0) / upper
    return low_part * low_part + high_part * high_part


def damping(widths, positions, count_x, count_y, count_z):
    edges = widths.astype(jnp.float32)
    longest = max(positions.shape[0], count_y, count_z)
    line = jnp.arange(longest, dtype=jnp.float32)
    x_line = jnp.pad(positions, (0, longest - positions.shape[0]))
    place = jnp.stack([x_line, line, line])
    count = jnp.stack([jnp.asarray(count_x, jnp.float32), jnp.float32(count_y), jnp.float32(count_z)])[:, None]
    lower = jnp.stack([edges[0], edges[2], edges[4]])[:, None]
    upper = jnp.stack([edges[1], edges[3], edges[5]])[:, None]
    ramps = ramp(place, count, lower, upper)
    along_x = ramps[0, : positions.shape[0]]
    along_y = ramps[1, :count_y]
    along_z = ramps[2, :count_z]
    return damp_peak * (along_x[:, None, None] + along_y[None, :, None] + along_z[None, None, :])


def with_halo(x):
    size = lax.axis_size("space")
    length = x.shape[0]
    if size == 2:
        me = lax.axis_index("space")
        piece = lax.dynamic_slice_in_dim(x, (1 - me) * (length - HALO), HALO, 0)
        got = lax.ppermute(piece, "space", [(0, 1), (1, 0)])
        zeros = jnp.zeros((HALO,) + x.shape[1:], x.dtype)
        padded = jnp.concatenate([zeros, x, zeros], axis=0)
        return lax.dynamic_update_slice_in_dim(padded, got, (1 - me) * (length + HALO), 0)
    up = [(i, (i + 1) % size) for i in range(size - 1)]
    down = [(j, i) for i, j in up]
    before = lax.ppermute(x[length - HALO :], "space", up)
    after = lax.ppermute(x[:HALO], "space", down)
    return jnp.concatenate([before, x, after], axis=0)


def laplace_x(padded):
    width_x = padded.shape[0] - 8
    width_y = padded.shape[1]
    width_z = padded.shape[2]
    full = jnp.pad(padded, [(0, 0), (4, 4), (4, 4)])

    def part(move_x, move_y, move_z):
        return full[
            4 + move_x : 4 + move_x + width_x,
            4 + move_y : 4 + move_y + width_y,
            4 + move_z : 4 + move_z + width_z,
        ]

    total = 3.0 * STENCIL[0] * part(0, 0, 0)
    for reach in range(1, 5):
        beside_all = (
            part(reach, 0, 0)
            + part(-reach, 0, 0)
            + part(0, reach, 0)
            + part(0, -reach, 0)
            + part(0, 0, reach)
            + part(0, 0, -reach)
        )
        total = total + STENCIL[reach] * beside_all
    return total


def lateral_filter(field, table):
    count = field.shape[1]
    index = jnp.arange(count)
    phase = index[:, None] * index[None, :] % count
    angle = 2.0 * math.pi / count * phase.astype(jnp.float32)
    cosine = jnp.cos(angle)
    sine = jnp.sin(angle)
    real_part = jnp.einsum("xyz,yk->xzk", field, cosine, precision=lax.Precision.HIGHEST)
    imag_part = jnp.einsum("xyz,yk->xzk", field, sine, precision=lax.Precision.HIGHEST)
    weight = table[None, :, :]
    back = jnp.einsum("xzk,yk->xyz", real_part * weight, cosine, precision=lax.Precision.HIGHEST)
    back = back + jnp.einsum(
        "xzk,yk->xyz", imag_part * weight, sine, precision=lax.Precision.HIGHEST
    )
    return back / count


def shot_bits(n):
    bits = []
    k = 1
    while k < n:
        bits.append(k)
        k *= 2
    assert k == n
    return bits


def ag_step(held, k, done):
    n = lax.axis_size("shot")
    me = lax.axis_index("shot")
    theirs = lax.ppermute(held, "shot", [(i, i ^ k) for i in range(n)])
    low = 2 ** sum(1 for b in done if b < k)
    shape = (held.shape[0] // low, 1, low) + held.shape[1:]
    mine, other = held.reshape(shape), theirs.reshape(shape)
    first = (me // k) % 2 == 0
    pair = jnp.where(first, jnp.concatenate([mine, other], axis=1), jnp.concatenate([other, mine], axis=1))
    return pair.reshape((2 * held.shape[0],) + held.shape[1:])


def swap_first(order):
    return order[1:2] + order[:1] + order[2:]


def swap_last(order):
    return order[:-2] + order[-1:] + order[-2:-1] if len(order) > 1 else order


def chain(held, kind, order, bits=None):
    if bits is None:
        bits = [] if kind == "ag" else sorted(order)
    return {"held": held, "kind": kind, "order": list(order), "i": 0, "bits": list(bits)}


def chain_step(c):
    k = c["order"][c["i"]]
    if c["kind"] == "ag":
        return ag_step(c["held"], k, c["bits"])
    return rs_step(c["held"], k, c["bits"])


def chain_commit(c, held):
    k = c["order"][c["i"]]
    c["held"] = held
    c["i"] += 1
    if c["kind"] == "ag":
        c["bits"].append(k)
    else:
        c["bits"].remove(k)


def rs_step(held, k, left):
    n = lax.axis_size("shot")
    me = lax.axis_index("shot")
    low = 2 ** left.index(k)
    high = held.shape[0] // (2 * low)
    split = held.reshape((high, 2, low) + held.shape[1:])
    mine = (me // k) % 2
    keep = lax.dynamic_index_in_dim(split, mine, axis=1, keepdims=False)
    send = lax.dynamic_index_in_dim(split, 1 - mine, axis=1, keepdims=False)
    got = lax.ppermute(send, "shot", [(i, i ^ k) for i in range(n)])
    return (keep + got).reshape((high * low,) + held.shape[1:])


def body(
    wave_prev,
    wave_now,
    velocity_code,
    perturb,
    gains,
    wavelet,
    source_index,
    receiver_index,
    absorb_width,
):
    shots, span_x, span_y, span_z = wave_now.shape
    n_shot = lax.axis_size("shot")
    me_shot = lax.axis_index("shot")
    bits = shot_bits(n_shot)
    start_x = lax.axis_index("space") * span_x
    total_x = span_x * lax.axis_size("space")
    speed_term = coefficient(velocity_code)
    positions = start_x.astype(jnp.float32) + jnp.arange(span_x, dtype=jnp.float32)
    absorber = damping(absorb_width, positions, total_x, span_y, span_z)
    cells = span_x * span_y * span_z
    offset = start_x * span_y * span_z
    source_local = source_index - offset
    source_owned = (source_local >= 0) & (source_local < cells)
    source_safe = jnp.clip(source_local, 0, cells - 1)
    plane = span_y * span_z
    sx = source_safe[0] // plane
    sy = (source_safe[0] // span_z) % span_y
    sz = source_safe[0] % span_z
    source_code = lax.dynamic_slice(velocity_code, (sx, sy, sz), (1, 1, 1)).reshape(1)
    source_gain = jnp.where(source_owned, coefficient(source_code), 0.0)
    barrier = lax.optimization_barrier

    hit = (
        (jnp.arange(span_x)[:, None, None] == sx)
        & (jnp.arange(span_y)[None, :, None] == sy)
        & (jnp.arange(span_z)[None, None, :] == sz)
    )

    def inject(field, moment):
        return field + jnp.where(hit, source_gain[0] * wavelet[0, moment], 0.0)

    def wave_step(current, prior, moment, last):
        drive = speed_term * laplace_x(with_halo(current))
        if last:
            return None, drive
        later = inject(2.0 * current - prior + drive - absorber * (current - prior), moment)
        return later, drive

    def born_second(born, field_model, drive):
        return (
            2.0 * born
            + speed_term * laplace_x(with_halo(born))
            - absorber * born
            + field_model * drive
        )

    slab = span_x // n_shot
    depth = perturb.shape[2]
    model_held = perturb.transpose(2, 0, 1).reshape(1, depth, span_x * span_y)
    gains_held = gains[None]
    st = {"w0": wave_now[0], "wp": wave_prev[0]}

    def task_wave(i):
        def run():
            last = i == 3
            cur, pri = (st["w0"], st["wp"]) if i == 0 else (st["w%d" % i], st["w%d" % (i - 1)])
            later, drive = wave_step(cur, pri, i, last)
            st["drive%d" % i] = drive
            if not last:
                st["w%d" % (i + 1)] = later
        return run

    def run_group(chains, compute):
        chains = [c for c in chains if c["i"] < len(c["order"])]
        moved = [chain_step(c) for c in chains]
        compute()
        keys = sorted(st.keys())
        out = barrier((moved, [st[n] for n in keys]))
        st.update(zip(keys, out[1]))
        for c, held in zip(chains, out[0]):
            chain_commit(c, held)

    def nothing():
        return None

    def light_prep():
        task_wave(1)()
        st["light"] = st["drive0"] * st["drive0"] + st["drive1"] * st["drive1"]

    def halves(x, axis):
        h = x.shape[axis] // 2
        return lax.slice_in_dim(x, 0, h, axis=axis), lax.slice_in_dim(x, h, x.shape[axis], axis=axis)

    far_first = list(reversed(bits))
    near_first = list(bits)

    top = far_first[0]
    model_c = chain(model_held, "ag", far_first[:1])
    gains_c = chain(gains_held, "ag", far_first)
    tasks = [task_wave(0), light_prep, task_wave(2)]
    run_group([model_c, gains_c], tasks[0])
    half_a, half_b = halves(model_c["held"], 1)
    model_a = chain(half_a, "ag", far_first[1:], [top])
    model_b = chain(half_b, "ag", swap_first(far_first[1:]), [top])
    for i in range(1, len(bits)):
        run_group([model_a, model_b, gains_c], tasks[i] if i < len(tasks) else nothing)
    for i in range(len(bits), len(tasks)):
        tasks[i]()
    model_held = jnp.concatenate([model_a["held"], model_b["held"]], axis=1)
    gains_held = gains_c["held"]
    light_a, light_b = halves(st["light"].reshape(n_shot, slab, span_y, span_z), 2)
    light_a = chain(light_a, "rs", near_first[:-1], near_first)
    light_b = chain(light_b, "rs", swap_first(near_first[:-1]), near_first)

    def born_pass():
        model = model_held.reshape(span_z, span_x * span_y).T.reshape(span_x, span_y, span_z)
        st["born1"] = model * st["drive0"]
        st["born2"] = born_second(st["born1"], model, st["drive1"])

    run_group([light_a, light_b], born_pass)
    born1, born2 = st["born1"], st["born2"]

    image = st["drive0"] * born1 + st["drive1"] * born2
    image_a, image_b = halves(image.reshape(n_shot, slab, span_y, span_z), 2)
    image_a = chain(image_a, "rs", near_first[:-1], near_first)
    image_b = chain(image_b, "rs", swap_first(near_first[:-1]), near_first)
    tasks = [task_wave(3)]
    light_c = None
    for i in range(len(bits) - 1):
        group = [image_a, image_b]
        if light_a["i"] < len(light_a["order"]):
            group += [light_a, light_b]
        elif light_c is None:
            light_c = chain(
                jnp.concatenate([light_a["held"], light_b["held"]], axis=2), "rs", near_first[-1:], near_first[-1:]
            )
            group.append(light_c)
        run_group(group, tasks[i] if i < len(tasks) else nothing)
    for i in range(len(bits) - 1, len(tasks)):
        tasks[i]()
    if light_c is None:
        light_c = chain(
            jnp.concatenate([light_a["held"], light_b["held"]], axis=2), "rs", near_first[-1:], near_first[-1:]
        )
    last = chain(
        jnp.concatenate([image_a["held"], image_b["held"]], axis=2), "rs", near_first[-1:], near_first[-1:]
    )
    run_group([last, light_c], nothing)
    image_part = last["held"][0]
    light_part = light_c["held"][0]

    table_all = gains_held.reshape(n_shot * gains.shape[0], gains.shape[1])
    filt_part = lateral_filter(image_part / (light_part + eps), table_all)
    filt_c = chain(filt_part[None], "ag", far_first[:1])
    run_group([filt_c], nothing)
    part_a, part_b = halves(filt_c["held"], 2)
    filt_a = chain(part_a, "ag", far_first[1:], [top])
    filt_b = chain(part_b, "ag", swap_first(far_first[1:]), [top])
    for i in range(1, len(bits)):
        run_group([filt_a, filt_b], nothing)
    new_model = jnp.concatenate([filt_a["held"], filt_b["held"]], axis=2).reshape(span_x, span_y, span_z)
    filtered = lax.dynamic_slice_in_dim(new_model, me_shot * depth, depth, 2)

    b1 = new_model * st["drive2"]
    b2 = born_second(b1, new_model, st["drive3"])

    receiver_local = receiver_index[0] - offset
    receiver_owned = (receiver_local >= 0) & (receiver_local < cells)
    receiver_safe = jnp.clip(receiver_local, 0, cells - 1)
    row = receiver_safe // span_z
    rz = receiver_safe % span_z
    lane = jnp.arange(span_z)[None, :] == rz[:, None]

    def sample(field):
        rows = jnp.take(field.reshape(span_x * span_y, span_z), row, axis=0)
        picked = jnp.sum(jnp.where(lane, rows, 0.0), axis=1)
        return jnp.where(receiver_owned, picked, 0.0)

    records = jnp.stack([sample(b1), sample(b2)], axis=0)[None]
    traces = records + lax.ppermute(records, "space", [(0, 1), (1, 0)])
    return (filtered, b2[None], traces)


def solution(mesh):
    in_specs = (
        P(("dom", "shot"), "space", None, None),
        P(("dom", "shot"), "space", None, None),
        P(("dom", "space"), None, None),
        P(("dom", "space"), None, "shot"),
        P(("dom", "shot"), None),
        P(("dom", "shot"), None),
        P(("dom", "shot")),
        P(("dom", "shot"), None),
        P("dom"),
    )
    out_specs = (
        P(("dom", "space"), None, "shot"),
        P(("dom", "shot"), "space", None, None),
        P(("dom", "shot"), None, None),
    )
    return jax.shard_map(body, mesh=mesh, in_specs=in_specs, out_specs=out_specs, check_vma=False)
```

```python
import math

import jax
import jax.numpy as jnp
from jax import lax
from jax.sharding import PartitionSpec as P

STEPS_A = 2
STEPS_B = 2


STENCIL = (-205.0 / 72.0, 8.0 / 5.0, -1.0 / 5.0, 8.0 / 315.0, -1.0 / 560.0)
damp_peak = 0.5
eps = 1e-05
HALO = 4


def coefficient(levels):
    speed = 1500.0 + 15.0 * levels.astype(jnp.float32)
    ratio = 0.45 * speed / 5325.0
    return ratio * ratio


def ramp(position, count, lower, upper):
    low_part = jnp.maximum(lower - position, 0.0) / lower
    high_part = jnp.maximum(upper - (count - 1.0 - position), 0.0) / upper
    return low_part * low_part + high_part * high_part


def damping(widths, positions, count_x, count_y, count_z):
    edges = widths.astype(jnp.float32)
    longest = max(positions.shape[0], count_y, count_z)
    line = jnp.arange(longest, dtype=jnp.float32)
    x_line = jnp.pad(positions, (0, longest - positions.shape[0]))
    place = jnp.stack([x_line, line, line])
    count = jnp.stack([jnp.asarray(count_x, jnp.float32), jnp.float32(count_y), jnp.float32(count_z)])[:, None]
    lower = jnp.stack([edges[0], edges[2], edges[4]])[:, None]
    upper = jnp.stack([edges[1], edges[3], edges[5]])[:, None]
    ramps = ramp(place, count, lower, upper)
    along_x = ramps[0, : positions.shape[0]]
    along_y = ramps[1, :count_y]
    along_z = ramps[2, :count_z]
    return damp_peak * (along_x[:, None, None] + along_y[None, :, None] + along_z[None, None, :])


def with_halo(x):
    size = lax.axis_size("space")
    length = x.shape[0]
    if size == 2:
        me = lax.axis_index("space")
        piece = lax.dynamic_slice_in_dim(x, (1 - me) * (length - HALO), HALO, 0)
        got = lax.ppermute(piece, "space", [(0, 1), (1, 0)])
        zeros = jnp.zeros((HALO,) + x.shape[1:], x.dtype)
        padded = jnp.concatenate([zeros, x, zeros], axis=0)
        return lax.dynamic_update_slice_in_dim(padded, got, (1 - me) * (length + HALO), 0)
    up = [(i, (i + 1) % size) for i in range(size - 1)]
    down = [(j, i) for i, j in up]
    before = lax.ppermute(x[length - HALO :], "space", up)
    after = lax.ppermute(x[:HALO], "space", down)
    return jnp.concatenate([before, x, after], axis=0)


def laplace_x(padded):
    width_x = padded.shape[0] - 8
    width_y = padded.shape[1]
    width_z = padded.shape[2]
    full = jnp.pad(padded, [(0, 0), (4, 4), (4, 4)])

    def part(move_x, move_y, move_z):
        return full[
            4 + move_x : 4 + move_x + width_x,
            4 + move_y : 4 + move_y + width_y,
            4 + move_z : 4 + move_z + width_z,
        ]

    total = 3.0 * STENCIL[0] * part(0, 0, 0)
    for reach in range(1, 5):
        beside_all = (
            part(reach, 0, 0)
            + part(-reach, 0, 0)
            + part(0, reach, 0)
            + part(0, -reach, 0)
            + part(0, 0, reach)
            + part(0, 0, -reach)
        )
        total = total + STENCIL[reach] * beside_all
    return total


def lateral_filter(field, table):
    count = field.shape[1]
    index = jnp.arange(count)
    phase = index[:, None] * index[None, :] % count
    angle = 2.0 * math.pi / count * phase.astype(jnp.float32)
    cosine = jnp.cos(angle)
    sine = jnp.sin(angle)
    real_part = jnp.einsum("xyz,yk->xzk", field, cosine, precision=lax.Precision.HIGHEST)
    imag_part = jnp.einsum("xyz,yk->xzk", field, sine, precision=lax.Precision.HIGHEST)
    weight = table[None, :, :]
    back = jnp.einsum("xzk,yk->xyz", real_part * weight, cosine, precision=lax.Precision.HIGHEST)
    back = back + jnp.einsum(
        "xzk,yk->xyz", imag_part * weight, sine, precision=lax.Precision.HIGHEST
    )
    return back / count


def shot_bits(n):
    bits = []
    k = 1
    while k < n:
        bits.append(k)
        k *= 2
    assert k == n
    return bits


def ag_step(held, k, done):
    n = lax.axis_size("shot")
    me = lax.axis_index("shot")
    theirs = lax.ppermute(held, "shot", [(i, i ^ k) for i in range(n)])
    low = 2 ** sum(1 for b in done if b < k)
    shape = (held.shape[0] // low, 1, low) + held.shape[1:]
    mine, other = held.reshape(shape), theirs.reshape(shape)
    first = (me // k) % 2 == 0
    pair = jnp.where(first, jnp.concatenate([mine, other], axis=1), jnp.concatenate([other, mine], axis=1))
    return pair.reshape((2 * held.shape[0],) + held.shape[1:])


def swap_first(order):
    return order[1:2] + order[:1] + order[2:]


def swap_last(order):
    return order[:-2] + order[-1:] + order[-2:-1] if len(order) > 1 else order


def chain(held, kind, order, bits=None):
    if bits is None:
        bits = [] if kind == "ag" else sorted(order)
    return {"held": held, "kind": kind, "order": list(order), "i": 0, "bits": list(bits)}


def swap_sum(held, k):
    n = lax.axis_size("shot")
    return held + lax.ppermute(held, "shot", [(i, i ^ k) for i in range(n)])


def chain_step(c):
    k = c["order"][c["i"]]
    if c["kind"] == "sum":
        return swap_sum(c["held"], k)
    if c["kind"] == "ag":
        return ag_step(c["held"], k, c["bits"])
    return rs_step(c["held"], k, c["bits"])


def chain_commit(c, held):
    k = c["order"][c["i"]]
    c["held"] = held
    c["i"] += 1
    if c["kind"] == "ag":
        c["bits"].append(k)
    elif c["kind"] == "rs":
        c["bits"].remove(k)


def rs_step(held, k, left):
    n = lax.axis_size("shot")
    me = lax.axis_index("shot")
    low = 2 ** left.index(k)
    high = held.shape[0] // (2 * low)
    split = held.reshape((high, 2, low) + held.shape[1:])
    mine = (me // k) % 2
    keep = lax.dynamic_index_in_dim(split, mine, axis=1, keepdims=False)
    send = lax.dynamic_index_in_dim(split, 1 - mine, axis=1, keepdims=False)
    got = lax.ppermute(send, "shot", [(i, i ^ k) for i in range(n)])
    return (keep + got).reshape((high * low,) + held.shape[1:])


def body(
    wave_prev,
    wave_now,
    velocity_code,
    perturb,
    gains,
    wavelet,
    source_index,
    receiver_index,
    absorb_width,
):
    shots, span_x, span_y, span_z = wave_now.shape
    n_shot = lax.axis_size("shot")
    me_shot = lax.axis_index("shot")
    bits = shot_bits(n_shot)
    start_x = lax.axis_index("space") * span_x
    total_x = span_x * lax.axis_size("space")
    speed_term = coefficient(velocity_code)
    positions = start_x.astype(jnp.float32) + jnp.arange(span_x, dtype=jnp.float32)
    absorber = damping(absorb_width, positions, total_x, span_y, span_z)
    cells = span_x * span_y * span_z
    offset = start_x * span_y * span_z
    source_local = source_index - offset
    source_owned = (source_local >= 0) & (source_local < cells)
    source_safe = jnp.clip(source_local, 0, cells - 1)
    plane = span_y * span_z
    sx = source_safe[0] // plane
    sy = (source_safe[0] // span_z) % span_y
    sz = source_safe[0] % span_z
    source_code = lax.dynamic_slice(velocity_code, (sx, sy, sz), (1, 1, 1)).reshape(1)
    source_gain = jnp.where(source_owned, coefficient(source_code), 0.0)
    barrier = lax.optimization_barrier

    hit = (
        (jnp.arange(span_x)[:, None, None] == sx)
        & (jnp.arange(span_y)[None, :, None] == sy)
        & (jnp.arange(span_z)[None, None, :] == sz)
    )

    def inject(field, moment):
        return field + jnp.where(hit, source_gain[0] * wavelet[0, moment], 0.0)

    def wave_step(current, prior, moment, last):
        drive = speed_term * laplace_x(with_halo(current))
        if last:
            return None, drive
        later = inject(2.0 * current - prior + drive - absorber * (current - prior), moment)
        return later, drive

    def born_second(born, field_model, drive):
        return (
            2.0 * born
            + speed_term * laplace_x(with_halo(born))
            - absorber * born
            + field_model * drive
        )

    slab = span_x // n_shot
    depth = perturb.shape[2]
    model_held = perturb.transpose(2, 0, 1).reshape(1, depth, span_x * span_y)
    gains_held = gains[None]
    st = {"w0": wave_now[0], "wp": wave_prev[0]}

    def task_wave(i):
        def run():
            last = i == 3
            cur, pri = (st["w0"], st["wp"]) if i == 0 else (st["w%d" % i], st["w%d" % (i - 1)])
            later, drive = wave_step(cur, pri, i, last)
            st["drive%d" % i] = drive
            if not last:
                st["w%d" % (i + 1)] = later
        return run

    def run_group(chains, compute):
        chains = [c for c in chains if c["i"] < len(c["order"])]
        moved = [chain_step(c) for c in chains]
        compute()
        keys = sorted(st.keys())
        out = barrier((moved, [st[n] for n in keys]))
        st.update(zip(keys, out[1]))
        for c, held in zip(chains, out[0]):
            chain_commit(c, held)

    def nothing():
        return None

    def light_prep():
        task_wave(1)()
        st["light"] = st["drive0"] * st["drive0"] + st["drive1"] * st["drive1"]

    def halves(x, axis):
        h = x.shape[axis] // 2
        return lax.slice_in_dim(x, 0, h, axis=axis), lax.slice_in_dim(x, h, x.shape[axis], axis=axis)

    far_first = list(reversed(bits))
    near_first = list(bits)

    top = far_first[0]
    model_c = chain(model_held, "ag", far_first[:1])
    gains_c = chain(gains_held, "ag", far_first)
    tasks = [task_wave(0), light_prep, task_wave(2)]
    run_group([model_c, gains_c], tasks[0])
    half_a, half_b = halves(model_c["held"], 1)
    model_a = chain(half_a, "ag", far_first[1:], [top])
    model_b = chain(half_b, "ag", swap_first(far_first[1:]), [top])
    for i in range(1, len(bits)):
        run_group([model_a, model_b, gains_c], tasks[i] if i < len(tasks) else nothing)
    for i in range(len(bits), len(tasks)):
        tasks[i]()
    model_held = jnp.concatenate([model_a["held"], model_b["held"]], axis=1)
    gains_held = gains_c["held"]
    light_a, light_b = halves(st["light"].reshape(n_shot, slab, span_y, span_z), 2)
    light_a = chain(light_a, "rs", near_first[:-1], near_first)
    light_b = chain(light_b, "rs", swap_first(near_first[:-1]), near_first)

    def born_pass():
        model = model_held.reshape(span_z, span_x * span_y).T.reshape(span_x, span_y, span_z)
        st["born1"] = model * st["drive0"]
        st["born2"] = born_second(st["born1"], model, st["drive1"])

    run_group([light_a, light_b], born_pass)
    born1, born2 = st["born1"], st["born2"]

    image = st["drive0"] * born1 + st["drive1"] * born2
    image_a, image_b = halves(image.reshape(n_shot, slab, span_y, span_z), 2)
    image_a = chain(image_a, "rs", near_first[:-1], near_first)
    image_b = chain(image_b, "rs", swap_first(near_first[:-1]), near_first)
    tasks = [task_wave(3)]
    light_c = None
    for i in range(len(bits) - 1):
        group = [image_a, image_b]
        if light_a["i"] < len(light_a["order"]):
            group += [light_a, light_b]
        elif light_c is None:
            light_c = chain(jnp.concatenate([light_a["held"], light_b["held"]], axis=2), "sum", near_first[-1:])
            group.append(light_c)
        run_group(group, tasks[i] if i < len(tasks) else nothing)
    for i in range(len(bits) - 1, len(tasks)):
        tasks[i]()
    if light_c is None:
        light_c = chain(jnp.concatenate([light_a["held"], light_b["held"]], axis=2), "sum", near_first[-1:])
    last = chain(jnp.concatenate([image_a["held"], image_b["held"]], axis=2), "sum", near_first[-1:])
    run_group([last, light_c], nothing)
    image_part = last["held"].reshape((-1,) + last["held"].shape[2:])
    light_part = light_c["held"].reshape((-1,) + light_c["held"].shape[2:])

    table_all = gains_held.reshape(n_shot * gains.shape[0], gains.shape[1])
    filt_part = lateral_filter(image_part / (light_part + eps), table_all)
    pair_held = filt_part.reshape((2, slab) + filt_part.shape[1:])
    part_a, part_b = halves(pair_held, 2)
    filt_a = chain(part_a, "ag", far_first[1:], [top])
    filt_b = chain(part_b, "ag", swap_first(far_first[1:]), [top])
    for i in range(1, len(bits)):
        run_group([filt_a, filt_b], nothing)
    new_model = jnp.concatenate([filt_a["held"], filt_b["held"]], axis=2).reshape(span_x, span_y, span_z)
    filtered = lax.dynamic_slice_in_dim(new_model, me_shot * depth, depth, 2)

    b1 = new_model * st["drive2"]
    b2 = born_second(b1, new_model, st["drive3"])

    receiver_local = receiver_index[0] - offset
    receiver_owned = (receiver_local >= 0) & (receiver_local < cells)
    receiver_safe = jnp.clip(receiver_local, 0, cells - 1)
    row = receiver_safe // span_z
    rz = receiver_safe % span_z
    lane = jnp.arange(span_z)[None, :] == rz[:, None]

    def sample(field):
        rows = jnp.take(field.reshape(span_x * span_y, span_z), row, axis=0)
        picked = jnp.sum(jnp.where(lane, rows, 0.0), axis=1)
        return jnp.where(receiver_owned, picked, 0.0)

    records = jnp.stack([sample(b1), sample(b2)], axis=0)[None]
    traces = records + lax.ppermute(records, "space", [(0, 1), (1, 0)])
    return (filtered, b2[None], traces)


def solution(mesh):
    in_specs = (
        P(("dom", "shot"), "space", None, None),
        P(("dom", "shot"), "space", None, None),
        P(("dom", "space"), None, None),
        P(("dom", "space"), None, "shot"),
        P(("dom", "shot"), None),
        P(("dom", "shot"), None),
        P(("dom", "shot")),
        P(("dom", "shot"), None),
        P("dom"),
    )
    out_specs = (
        P(("dom", "space"), None, "shot"),
        P(("dom", "shot"), "space", None, None),
        P(("dom", "shot"), None, None),
    )
    return jax.shard_map(body, mesh=mesh, in_specs=in_specs, out_specs=out_specs, check_vma=False)
```

```python
import math

import jax
import jax.numpy as jnp
from jax import lax
from jax.sharding import PartitionSpec as P

STEPS_A = 2
STEPS_B = 2


STENCIL = (-205.0 / 72.0, 8.0 / 5.0, -1.0 / 5.0, 8.0 / 315.0, -1.0 / 560.0)
damp_peak = 0.5
eps = 1e-05
HALO = 4


def coefficient(levels):
    speed = 1500.0 + 15.0 * levels.astype(jnp.float32)
    ratio = 0.45 * speed / 5325.0
    return ratio * ratio


def ramp(position, count, lower, upper):
    low_part = jnp.maximum(lower - position, 0.0) / lower
    high_part = jnp.maximum(upper - (count - 1.0 - position), 0.0) / upper
    return low_part * low_part + high_part * high_part


def damping(widths, positions, count_x, count_y, count_z):
    edges = widths.astype(jnp.float32)
    longest = max(positions.shape[0], count_y, count_z)
    line = jnp.arange(longest, dtype=jnp.float32)
    x_line = jnp.pad(positions, (0, longest - positions.shape[0]))
    place = jnp.stack([x_line, line, line])
    count = jnp.stack([jnp.asarray(count_x, jnp.float32), jnp.float32(count_y), jnp.float32(count_z)])[:, None]
    lower = jnp.stack([edges[0], edges[2], edges[4]])[:, None]
    upper = jnp.stack([edges[1], edges[3], edges[5]])[:, None]
    ramps = ramp(place, count, lower, upper)
    along_x = ramps[0, : positions.shape[0]]
    along_y = ramps[1, :count_y]
    along_z = ramps[2, :count_z]
    return damp_peak * (along_x[:, None, None] + along_y[None, :, None] + along_z[None, None, :])


def with_halo(x):
    size = lax.axis_size("space")
    length = x.shape[0]
    if size == 2:
        me = lax.axis_index("space")
        piece = lax.dynamic_slice_in_dim(x, (1 - me) * (length - HALO), HALO, 0)
        got = lax.ppermute(piece, "space", [(0, 1), (1, 0)])
        zeros = jnp.zeros((HALO,) + x.shape[1:], x.dtype)
        padded = jnp.concatenate([zeros, x, zeros], axis=0)
        return lax.dynamic_update_slice_in_dim(padded, got, (1 - me) * (length + HALO), 0)
    up = [(i, (i + 1) % size) for i in range(size - 1)]
    down = [(j, i) for i, j in up]
    before = lax.ppermute(x[length - HALO :], "space", up)
    after = lax.ppermute(x[:HALO], "space", down)
    return jnp.concatenate([before, x, after], axis=0)


def laplace_x(padded):
    width_x = padded.shape[0] - 8
    width_y = padded.shape[1]
    width_z = padded.shape[2]
    full = jnp.pad(padded, [(0, 0), (4, 4), (4, 4)])

    def part(move_x, move_y, move_z):
        return full[
            4 + move_x : 4 + move_x + width_x,
            4 + move_y : 4 + move_y + width_y,
            4 + move_z : 4 + move_z + width_z,
        ]

    total = 3.0 * STENCIL[0] * part(0, 0, 0)
    for reach in range(1, 5):
        beside_all = (
            part(reach, 0, 0)
            + part(-reach, 0, 0)
            + part(0, reach, 0)
            + part(0, -reach, 0)
            + part(0, 0, reach)
            + part(0, 0, -reach)
        )
        total = total + STENCIL[reach] * beside_all
    return total


def lateral_filter(field, table):
    count = field.shape[1]
    index = jnp.arange(count)
    phase = index[:, None] * index[None, :] % count
    angle = 2.0 * math.pi / count * phase.astype(jnp.float32)
    cosine = jnp.cos(angle)
    sine = jnp.sin(angle)
    real_part = jnp.einsum("xyz,yk->xzk", field, cosine, precision=lax.Precision.HIGHEST)
    imag_part = jnp.einsum("xyz,yk->xzk", field, sine, precision=lax.Precision.HIGHEST)
    weight = table[None, :, :]
    back = jnp.einsum("xzk,yk->xyz", real_part * weight, cosine, precision=lax.Precision.HIGHEST)
    back = back + jnp.einsum(
        "xzk,yk->xyz", imag_part * weight, sine, precision=lax.Precision.HIGHEST
    )
    return back / count


def shot_bits(n):
    bits = []
    k = 1
    while k < n:
        bits.append(k)
        k *= 2
    assert k == n
    return bits


def ag_step(held, k, done):
    n = lax.axis_size("shot")
    me = lax.axis_index("shot")
    theirs = lax.ppermute(held, "shot", [(i, i ^ k) for i in range(n)])
    low = 2 ** sum(1 for b in done if b < k)
    shape = (held.shape[0] // low, 1, low) + held.shape[1:]
    mine, other = held.reshape(shape), theirs.reshape(shape)
    first = (me // k) % 2 == 0
    pair = jnp.where(first, jnp.concatenate([mine, other], axis=1), jnp.concatenate([other, mine], axis=1))
    return pair.reshape((2 * held.shape[0],) + held.shape[1:])


def swap_first(order):
    return order[1:2] + order[:1] + order[2:]


def swap_last(order):
    return order[:-2] + order[-1:] + order[-2:-1] if len(order) > 1 else order


def chain(held, kind, order, bits=None):
    if bits is None:
        bits = [] if kind == "ag" else sorted(order)
    return {"held": held, "kind": kind, "order": list(order), "i": 0, "bits": list(bits)}


def chain_step(c):
    k = c["order"][c["i"]]
    if c["kind"] == "ag":
        return ag_step(c["held"], k, c["bits"])
    return rs_step(c["held"], k, c["bits"])


def chain_commit(c, held):
    k = c["order"][c["i"]]
    c["held"] = held
    c["i"] += 1
    if c["kind"] == "ag":
        c["bits"].append(k)
    else:
        c["bits"].remove(k)


def rs_step(held, k, left):
    n = lax.axis_size("shot")
    me = lax.axis_index("shot")
    low = 2 ** left.index(k)
    high = held.shape[0] // (2 * low)
    split = held.reshape((high, 2, low) + held.shape[1:])
    mine = (me // k) % 2
    keep = lax.dynamic_index_in_dim(split, mine, axis=1, keepdims=False)
    send = lax.dynamic_index_in_dim(split, 1 - mine, axis=1, keepdims=False)
    got = lax.ppermute(send, "shot", [(i, i ^ k) for i in range(n)])
    return (keep + got).reshape((high * low,) + held.shape[1:])


def body(
    wave_prev,
    wave_now,
    velocity_code,
    perturb,
    gains,
    wavelet,
    source_index,
    receiver_index,
    absorb_width,
):
    shots, span_x, span_y, span_z = wave_now.shape
    n_shot = lax.axis_size("shot")
    me_shot = lax.axis_index("shot")
    bits = shot_bits(n_shot)
    start_x = lax.axis_index("space") * span_x
    total_x = span_x * lax.axis_size("space")
    speed_term = coefficient(velocity_code)
    positions = start_x.astype(jnp.float32) + jnp.arange(span_x, dtype=jnp.float32)
    absorber = damping(absorb_width, positions, total_x, span_y, span_z)
    cells = span_x * span_y * span_z
    offset = start_x * span_y * span_z
    source_local = source_index - offset
    source_owned = (source_local >= 0) & (source_local < cells)
    source_safe = jnp.clip(source_local, 0, cells - 1)
    plane = span_y * span_z
    sx = source_safe[0] // plane
    sy = (source_safe[0] // span_z) % span_y
    sz = source_safe[0] % span_z
    source_code = lax.dynamic_slice(velocity_code, (sx, sy, sz), (1, 1, 1)).reshape(1)
    source_gain = jnp.where(source_owned, coefficient(source_code), 0.0)
    barrier = lax.optimization_barrier

    hit = (
        (jnp.arange(span_x)[:, None, None] == sx)
        & (jnp.arange(span_y)[None, :, None] == sy)
        & (jnp.arange(span_z)[None, None, :] == sz)
    )

    def inject(field, moment):
        return field + jnp.where(hit, source_gain[0] * wavelet[0, moment], 0.0)

    def wave_step(current, prior, moment, last):
        drive = speed_term * laplace_x(with_halo(current))
        if last:
            return None, drive
        later = inject(2.0 * current - prior + drive - absorber * (current - prior), moment)
        return later, drive

    def born_second(born, field_model, drive):
        return (
            2.0 * born
            + speed_term * laplace_x(with_halo(born))
            - absorber * born
            + field_model * drive
        )

    slab = span_x // n_shot
    depth = perturb.shape[2]
    model_held = perturb.transpose(2, 0, 1).reshape(1, depth, span_x * span_y)
    gains_held = gains[None]
    st = {"w0": wave_now[0], "wp": wave_prev[0]}

    def task_wave(i):
        def run():
            last = i == 3
            cur, pri = (st["w0"], st["wp"]) if i == 0 else (st["w%d" % i], st["w%d" % (i - 1)])
            later, drive = wave_step(cur, pri, i, last)
            st["drive%d" % i] = drive
            if not last:
                st["w%d" % (i + 1)] = later
        return run

    def run_group(chains, compute):
        chains = [c for c in chains if c["i"] < len(c["order"])]
        moved = [chain_step(c) for c in chains]
        compute()
        keys = sorted(st.keys())
        out = barrier((moved, [st[n] for n in keys]))
        st.update(zip(keys, out[1]))
        for c, held in zip(chains, out[0]):
            chain_commit(c, held)

    def nothing():
        return None

    def light_prep():
        task_wave(1)()
        st["light"] = st["drive0"] * st["drive0"] + st["drive1"] * st["drive1"]

    def halves(x, axis):
        h = x.shape[axis] // 2
        return lax.slice_in_dim(x, 0, h, axis=axis), lax.slice_in_dim(x, h, x.shape[axis], axis=axis)

    far_first = list(reversed(bits))
    near_first = list(bits)

    top = far_first[0]
    model_c = chain(model_held, "ag", far_first[:1])
    gains_c = chain(gains_held, "ag", far_first)
    tasks = [task_wave(0), light_prep, task_wave(2)]
    run_group([model_c], tasks[0])
    half_a, half_b = halves(model_c["held"], 1)
    model_a = chain(half_a, "ag", far_first[1:], [top])
    model_b = chain(half_b, "ag", swap_first(far_first[1:]), [top])
    for i in range(1, len(bits)):
        run_group([model_a, model_b, gains_c], tasks[i] if i < len(tasks) else nothing)
    for i in range(len(bits), len(tasks)):
        tasks[i]()
    model_held = jnp.concatenate([model_a["held"], model_b["held"]], axis=1)
    light_a, light_b = halves(st["light"].reshape(n_shot, slab, span_y, span_z), 2)
    light_a = chain(light_a, "rs", near_first[:-1], near_first)
    light_b = chain(light_b, "rs", swap_first(near_first[:-1]), near_first)

    def born_pass():
        model = model_held.reshape(span_z, span_x * span_y).T.reshape(span_x, span_y, span_z)
        st["born1"] = model * st["drive0"]
        st["born2"] = born_second(st["born1"], model, st["drive1"])

    run_group([light_a, light_b, gains_c], born_pass)
    born1, born2 = st["born1"], st["born2"]
    gains_held = gains_c["held"]

    image = st["drive0"] * born1 + st["drive1"] * born2
    image_a, image_b = halves(image.reshape(n_shot, slab, span_y, span_z), 2)
    image_a = chain(image_a, "rs", near_first[:-1], near_first)
    image_b = chain(image_b, "rs", swap_first(near_first[:-1]), near_first)
    tasks = [task_wave(3)]
    light_c = None
    for i in range(len(bits) - 1):
        group = [image_a, image_b]
        if light_a["i"] < len(light_a["order"]):
            group += [light_a, light_b]
        elif light_c is None:
            light_c = chain(
                jnp.concatenate([light_a["held"], light_b["held"]], axis=2), "rs", near_first[-1:], near_first[-1:]
            )
            group.append(light_c)
        run_group(group, tasks[i] if i < len(tasks) else nothing)
    for i in range(len(bits) - 1, len(tasks)):
        tasks[i]()
    if light_c is None:
        light_c = chain(
            jnp.concatenate([light_a["held"], light_b["held"]], axis=2), "rs", near_first[-1:], near_first[-1:]
        )
    last = chain(
        jnp.concatenate([image_a["held"], image_b["held"]], axis=2), "rs", near_first[-1:], near_first[-1:]
    )
    run_group([last, light_c], nothing)
    image_part = last["held"][0]
    light_part = light_c["held"][0]

    table_all = gains_held.reshape(n_shot * gains.shape[0], gains.shape[1])
    filt_part = lateral_filter(image_part / (light_part + eps), table_all)
    filt_c = chain(filt_part[None], "ag", far_first[:1])
    run_group([filt_c], nothing)
    part_a, part_b = halves(filt_c["held"], 2)
    filt_a = chain(part_a, "ag", far_first[1:], [top])
    filt_b = chain(part_b, "ag", swap_first(far_first[1:]), [top])
    for i in range(1, len(bits)):
        run_group([filt_a, filt_b], nothing)
    new_model = jnp.concatenate([filt_a["held"], filt_b["held"]], axis=2).reshape(span_x, span_y, span_z)
    filtered = lax.dynamic_slice_in_dim(new_model, me_shot * depth, depth, 2)

    b1 = new_model * st["drive2"]
    b1_padded = with_halo(b1)
    filtered, b1_padded = barrier((filtered, b1_padded))
    b2 = (
        2.0 * b1
        + speed_term * laplace_x(b1_padded)
        - absorber * b1
        + new_model * st["drive3"]
    )

    receiver_local = receiver_index[0] - offset
    receiver_owned = (receiver_local >= 0) & (receiver_local < cells)
    receiver_safe = jnp.clip(receiver_local, 0, cells - 1)
    row = receiver_safe // span_z
    rz = receiver_safe % span_z
    lane = jnp.arange(span_z)[None, :] == rz[:, None]

    def sample(field):
        rows = jnp.take(field.reshape(span_x * span_y, span_z), row, axis=0)
        picked = jnp.sum(jnp.where(lane, rows, 0.0), axis=1)
        return jnp.where(receiver_owned, picked, 0.0)

    records = jnp.stack([sample(b1), sample(b2)], axis=0)[None]
    traces = records + lax.ppermute(records, "space", [(0, 1), (1, 0)])
    return (filtered, b2[None], traces)


def solution(mesh):
    in_specs = (
        P(("dom", "shot"), "space", None, None),
        P(("dom", "shot"), "space", None, None),
        P(("dom", "space"), None, None),
        P(("dom", "space"), None, "shot"),
        P(("dom", "shot"), None),
        P(("dom", "shot"), None),
        P(("dom", "shot")),
        P(("dom", "shot"), None),
        P("dom"),
    )
    out_specs = (
        P(("dom", "space"), None, "shot"),
        P(("dom", "shot"), "space", None, None),
        P(("dom", "shot"), None, None),
    )
    return jax.shard_map(body, mesh=mesh, in_specs=in_specs, out_specs=out_specs, check_vma=False)
```

```python
import math

import jax
import jax.numpy as jnp
from jax import lax
from jax.sharding import PartitionSpec as P

STEPS_A = 2
STEPS_B = 2


STENCIL = (-205.0 / 72.0, 8.0 / 5.0, -1.0 / 5.0, 8.0 / 315.0, -1.0 / 560.0)
damp_peak = 0.5
eps = 1e-05
HALO = 4


def coefficient(levels):
    speed = 1500.0 + 15.0 * levels.astype(jnp.float32)
    ratio = 0.45 * speed / 5325.0
    return ratio * ratio


def ramp(position, count, lower, upper):
    low_part = jnp.maximum(lower - position, 0.0) / lower
    high_part = jnp.maximum(upper - (count - 1.0 - position), 0.0) / upper
    return low_part * low_part + high_part * high_part


def damping(widths, positions, count_x, count_y, count_z):
    edges = widths.astype(jnp.float32)
    longest = max(positions.shape[0], count_y, count_z)
    line = jnp.arange(longest, dtype=jnp.float32)
    x_line = jnp.pad(positions, (0, longest - positions.shape[0]))
    place = jnp.stack([x_line, line, line])
    count = jnp.stack([jnp.asarray(count_x, jnp.float32), jnp.float32(count_y), jnp.float32(count_z)])[:, None]
    lower = jnp.stack([edges[0], edges[2], edges[4]])[:, None]
    upper = jnp.stack([edges[1], edges[3], edges[5]])[:, None]
    ramps = ramp(place, count, lower, upper)
    along_x = ramps[0, : positions.shape[0]]
    along_y = ramps[1, :count_y]
    along_z = ramps[2, :count_z]
    return damp_peak * (along_x[:, None, None] + along_y[None, :, None] + along_z[None, None, :])


def with_halo(x):
    size = lax.axis_size("space")
    length = x.shape[0]
    if size == 2:
        me = lax.axis_index("space")
        piece = lax.dynamic_slice_in_dim(x, (1 - me) * (length - HALO), HALO, 0)
        got = lax.ppermute(piece, "space", [(0, 1), (1, 0)])
        zeros = jnp.zeros((HALO,) + x.shape[1:], x.dtype)
        padded = jnp.concatenate([zeros, x, zeros], axis=0)
        return lax.dynamic_update_slice_in_dim(padded, got, (1 - me) * (length + HALO), 0)
    up = [(i, (i + 1) % size) for i in range(size - 1)]
    down = [(j, i) for i, j in up]
    before = lax.ppermute(x[length - HALO :], "space", up)
    after = lax.ppermute(x[:HALO], "space", down)
    return jnp.concatenate([before, x, after], axis=0)


def laplace_x(padded):
    width_x = padded.shape[0] - 8
    width_y = padded.shape[1]
    width_z = padded.shape[2]
    full = jnp.pad(padded, [(0, 0), (4, 4), (4, 4)])

    def part(move_x, move_y, move_z):
        return full[
            4 + move_x : 4 + move_x + width_x,
            4 + move_y : 4 + move_y + width_y,
            4 + move_z : 4 + move_z + width_z,
        ]

    total = 3.0 * STENCIL[0] * part(0, 0, 0)
    for reach in range(1, 5):
        beside_all = (
            part(reach, 0, 0)
            + part(-reach, 0, 0)
            + part(0, reach, 0)
            + part(0, -reach, 0)
            + part(0, 0, reach)
            + part(0, 0, -reach)
        )
        total = total + STENCIL[reach] * beside_all
    return total


def lateral_filter(field, table):
    count = field.shape[1]
    index = jnp.arange(count)
    phase = index[:, None] * index[None, :] % count
    angle = 2.0 * math.pi / count * phase.astype(jnp.float32)
    cosine = jnp.cos(angle)
    sine = jnp.sin(angle)
    real_part = jnp.einsum("xyz,yk->xzk", field, cosine, precision=lax.Precision.HIGHEST)
    imag_part = jnp.einsum("xyz,yk->xzk", field, sine, precision=lax.Precision.HIGHEST)
    weight = table[None, :, :]
    back = jnp.einsum("xzk,yk->xyz", real_part * weight, cosine, precision=lax.Precision.HIGHEST)
    back = back + jnp.einsum(
        "xzk,yk->xyz", imag_part * weight, sine, precision=lax.Precision.HIGHEST
    )
    return back / count


def shot_bits(n):
    bits = []
    k = 1
    while k < n:
        bits.append(k)
        k *= 2
    assert k == n
    return bits


def ag_step(held, k, done):
    n = lax.axis_size("shot")
    me = lax.axis_index("shot")
    theirs = lax.ppermute(held, "shot", [(i, i ^ k) for i in range(n)])
    low = 2 ** sum(1 for b in done if b < k)
    shape = (held.shape[0] // low, 1, low) + held.shape[1:]
    mine, other = held.reshape(shape), theirs.reshape(shape)
    first = (me // k) % 2 == 0
    pair = jnp.where(first, jnp.concatenate([mine, other], axis=1), jnp.concatenate([other, mine], axis=1))
    return pair.reshape((2 * held.shape[0],) + held.shape[1:])


def swap_first(order):
    return order[1:2] + order[:1] + order[2:]


def swap_last(order):
    return order[:-2] + order[-1:] + order[-2:-1] if len(order) > 1 else order


def chain(held, kind, order, bits=None):
    if bits is None:
        bits = [] if kind == "ag" else sorted(order)
    return {"held": held, "kind": kind, "order": list(order), "i": 0, "bits": list(bits)}


def chain_step(c):
    k = c["order"][c["i"]]
    if c["kind"] == "ag":
        return ag_step(c["held"], k, c["bits"])
    return rs_step(c["held"], k, c["bits"])


def chain_commit(c, held):
    k = c["order"][c["i"]]
    c["held"] = held
    c["i"] += 1
    if c["kind"] == "ag":
        c["bits"].append(k)
    else:
        c["bits"].remove(k)


def rs_step(held, k, left):
    n = lax.axis_size("shot")
    me = lax.axis_index("shot")
    low = 2 ** left.index(k)
    high = held.shape[0] // (2 * low)
    split = held.reshape((high, 2, low) + held.shape[1:])
    mine = (me // k) % 2
    keep = lax.dynamic_index_in_dim(split, mine, axis=1, keepdims=False)
    send = lax.dynamic_index_in_dim(split, 1 - mine, axis=1, keepdims=False)
    got = lax.ppermute(send, "shot", [(i, i ^ k) for i in range(n)])
    return (keep + got).reshape((high * low,) + held.shape[1:])


def body(
    wave_prev,
    wave_now,
    velocity_code,
    perturb,
    gains,
    wavelet,
    source_index,
    receiver_index,
    absorb_width,
):
    shots, span_x, span_y, span_z = wave_now.shape
    n_shot = lax.axis_size("shot")
    me_shot = lax.axis_index("shot")
    bits = shot_bits(n_shot)
    start_x = lax.axis_index("space") * span_x
    total_x = span_x * lax.axis_size("space")
    speed_term = coefficient(velocity_code)
    positions = start_x.astype(jnp.float32) + jnp.arange(span_x, dtype=jnp.float32)
    absorber = damping(absorb_width, positions, total_x, span_y, span_z)
    cells = span_x * span_y * span_z
    offset = start_x * span_y * span_z
    source_local = source_index - offset
    source_owned = (source_local >= 0) & (source_local < cells)
    source_safe = jnp.clip(source_local, 0, cells - 1)
    plane = span_y * span_z
    sx = source_safe[0] // plane
    sy = (source_safe[0] // span_z) % span_y
    sz = source_safe[0] % span_z
    source_code = lax.dynamic_slice(velocity_code, (sx, sy, sz), (1, 1, 1)).reshape(1)
    source_gain = jnp.where(source_owned, coefficient(source_code), 0.0)
    barrier = lax.optimization_barrier

    hit = (
        (jnp.arange(span_x)[:, None, None] == sx)
        & (jnp.arange(span_y)[None, :, None] == sy)
        & (jnp.arange(span_z)[None, None, :] == sz)
    )

    def inject(field, moment):
        return field + jnp.where(hit, source_gain[0] * wavelet[0, moment], 0.0)

    def wave_step(current, prior, moment, last):
        drive = speed_term * laplace_x(with_halo(current))
        if last:
            return None, drive
        later = inject(2.0 * current - prior + drive - absorber * (current - prior), moment)
        return later, drive

    def born_second(born, field_model, drive):
        return (
            2.0 * born
            + speed_term * laplace_x(with_halo(born))
            - absorber * born
            + field_model * drive
        )

    slab = span_x // n_shot
    depth = perturb.shape[2]
    model_held = perturb.transpose(2, 0, 1).reshape(1, depth, span_x * span_y)
    gains_held = gains[None]
    st = {"w0": wave_now[0], "wp": wave_prev[0]}

    def task_wave(i):
        def run():
            last = i == 3
            cur, pri = (st["w0"], st["wp"]) if i == 0 else (st["w%d" % i], st["w%d" % (i - 1)])
            later, drive = wave_step(cur, pri, i, last)
            st["drive%d" % i] = drive
            if not last:
                st["w%d" % (i + 1)] = later
        return run

    def run_group(chains, compute):
        chains = [c for c in chains if c["i"] < len(c["order"])]
        moved = [chain_step(c) for c in chains]
        compute()
        keys = sorted(st.keys())
        out = barrier((moved, [st[n] for n in keys]))
        st.update(zip(keys, out[1]))
        for c, held in zip(chains, out[0]):
            chain_commit(c, held)

    def nothing():
        return None

    def light_prep():
        task_wave(1)()
        st["light"] = st["drive0"] * st["drive0"] + st["drive1"] * st["drive1"]

    def halves(x, axis):
        h = x.shape[axis] // 2
        return lax.slice_in_dim(x, 0, h, axis=axis), lax.slice_in_dim(x, h, x.shape[axis], axis=axis)

    far_first = list(reversed(bits))
    near_first = list(bits)

    top = far_first[0]
    model_c = chain(model_held, "ag", far_first[:1])
    gains_c = chain(gains_held, "ag", far_first)
    def first_steps():
        task_wave(0)()
        light_prep()

    tasks = [first_steps, task_wave(2)]
    run_group([model_c, gains_c], tasks[0])
    half_a, half_b = halves(model_c["held"], 1)
    model_a = chain(half_a, "ag", far_first[1:], [top])
    model_b = chain(half_b, "ag", swap_first(far_first[1:]), [top])
    light_a, light_b = halves(st["light"].reshape(n_shot, slab, span_y, span_z), 2)
    light_a = chain(light_a, "rs", near_first[:-1], near_first)
    light_b = chain(light_b, "rs", swap_first(near_first[:-1]), near_first)
    for i in range(1, len(bits)):
        run_group([model_a, model_b, gains_c, light_a, light_b], tasks[i] if i < len(tasks) else nothing)
    for i in range(len(bits), len(tasks)):
        tasks[i]()
    model_held = jnp.concatenate([model_a["held"], model_b["held"]], axis=1)
    gains_held = gains_c["held"]
    light_c = chain(jnp.concatenate([light_a["held"], light_b["held"]], axis=2), "rs", near_first[-1:], near_first[-1:])

    def born_pass():
        model = model_held.reshape(span_z, span_x * span_y).T.reshape(span_x, span_y, span_z)
        st["born1"] = model * st["drive0"]
        st["born2"] = born_second(st["born1"], model, st["drive1"])

    run_group([light_c], born_pass)
    born1, born2 = st["born1"], st["born2"]

    image = st["drive0"] * born1 + st["drive1"] * born2
    image_a, image_b = halves(image.reshape(n_shot, slab, span_y, span_z), 2)
    image_a = chain(image_a, "rs", near_first[:-1], near_first)
    image_b = chain(image_b, "rs", swap_first(near_first[:-1]), near_first)
    tasks = [task_wave(3)]
    for i in range(len(bits) - 1):
        run_group([image_a, image_b], tasks[i] if i < len(tasks) else nothing)
    for i in range(len(bits) - 1, len(tasks)):
        tasks[i]()
    last = chain(
        jnp.concatenate([image_a["held"], image_b["held"]], axis=2), "rs", near_first[-1:], near_first[-1:]
    )
    run_group([last], nothing)
    image_part = last["held"][0]
    light_part = light_c["held"][0]

    table_all = gains_held.reshape(n_shot * gains.shape[0], gains.shape[1])
    filt_part = lateral_filter(image_part / (light_part + eps), table_all)
    filt_c = chain(filt_part[None], "ag", far_first[:1])
    run_group([filt_c], nothing)
    part_a, part_b = halves(filt_c["held"], 2)
    filt_a = chain(part_a, "ag", far_first[1:], [top])
    filt_b = chain(part_b, "ag", swap_first(far_first[1:]), [top])
    for i in range(1, len(bits)):
        run_group([filt_a, filt_b], nothing)
    new_model = jnp.concatenate([filt_a["held"], filt_b["held"]], axis=2).reshape(span_x, span_y, span_z)
    filtered = lax.dynamic_slice_in_dim(new_model, me_shot * depth, depth, 2)

    b1 = new_model * st["drive2"]
    b2 = born_second(b1, new_model, st["drive3"])

    receiver_local = receiver_index[0] - offset
    receiver_owned = (receiver_local >= 0) & (receiver_local < cells)
    receiver_safe = jnp.clip(receiver_local, 0, cells - 1)
    row = receiver_safe // span_z
    rz = receiver_safe % span_z
    lane = jnp.arange(span_z)[None, :] == rz[:, None]

    def sample(field):
        rows = jnp.take(field.reshape(span_x * span_y, span_z), row, axis=0)
        picked = jnp.sum(jnp.where(lane, rows, 0.0), axis=1)
        return jnp.where(receiver_owned, picked, 0.0)

    records = jnp.stack([sample(b1), sample(b2)], axis=0)[None]
    traces = records + lax.ppermute(records, "space", [(0, 1), (1, 0)])
    return (filtered, b2[None], traces)


def solution(mesh):
    in_specs = (
        P(("dom", "shot"), "space", None, None),
        P(("dom", "shot"), "space", None, None),
        P(("dom", "space"), None, None),
        P(("dom", "space"), None, "shot"),
        P(("dom", "shot"), None),
        P(("dom", "shot"), None),
        P(("dom", "shot")),
        P(("dom", "shot"), None),
        P("dom"),
    )
    out_specs = (
        P(("dom", "space"), None, "shot"),
        P(("dom", "shot"), "space", None, None),
        P(("dom", "shot"), None, None),
    )
    return jax.shard_map(body, mesh=mesh, in_specs=in_specs, out_specs=out_specs, check_vma=False)
```

```python
import math

import jax
import jax.numpy as jnp
from jax import lax
from jax.sharding import PartitionSpec as P

STEPS_A = 2
STEPS_B = 2


STENCIL = (-205.0 / 72.0, 8.0 / 5.0, -1.0 / 5.0, 8.0 / 315.0, -1.0 / 560.0)
damp_peak = 0.5
eps = 1e-05
HALO = 4


def coefficient(levels):
    speed = 1500.0 + 15.0 * levels.astype(jnp.float32)
    ratio = 0.45 * speed / 5325.0
    return ratio * ratio


def ramp(position, count, lower, upper):
    low_part = jnp.maximum(lower - position, 0.0) / lower
    high_part = jnp.maximum(upper - (count - 1.0 - position), 0.0) / upper
    return low_part * low_part + high_part * high_part


def damping(widths, positions, count_x, count_y, count_z):
    edges = widths.astype(jnp.float32)
    longest = max(positions.shape[0], count_y, count_z)
    line = jnp.arange(longest, dtype=jnp.float32)
    x_line = jnp.pad(positions, (0, longest - positions.shape[0]))
    place = jnp.stack([x_line, line, line])
    count = jnp.stack([jnp.asarray(count_x, jnp.float32), jnp.float32(count_y), jnp.float32(count_z)])[:, None]
    lower = jnp.stack([edges[0], edges[2], edges[4]])[:, None]
    upper = jnp.stack([edges[1], edges[3], edges[5]])[:, None]
    ramps = ramp(place, count, lower, upper)
    along_x = ramps[0, : positions.shape[0]]
    along_y = ramps[1, :count_y]
    along_z = ramps[2, :count_z]
    return damp_peak * (along_x[:, None, None] + along_y[None, :, None] + along_z[None, None, :])


def with_halo(x):
    size = lax.axis_size("space")
    length = x.shape[0]
    if size == 2:
        me = lax.axis_index("space")
        piece = lax.dynamic_slice_in_dim(x, (1 - me) * (length - HALO), HALO, 0)
        got = lax.ppermute(piece, "space", [(0, 1), (1, 0)])
        zeros = jnp.zeros((HALO,) + x.shape[1:], x.dtype)
        padded = jnp.concatenate([zeros, x, zeros], axis=0)
        return lax.dynamic_update_slice_in_dim(padded, got, (1 - me) * (length + HALO), 0)
    up = [(i, (i + 1) % size) for i in range(size - 1)]
    down = [(j, i) for i, j in up]
    before = lax.ppermute(x[length - HALO :], "space", up)
    after = lax.ppermute(x[:HALO], "space", down)
    return jnp.concatenate([before, x, after], axis=0)


def laplace_x(padded):
    width_x = padded.shape[0] - 8
    width_y = padded.shape[1]
    width_z = padded.shape[2]
    full = jnp.pad(padded, [(0, 0), (4, 4), (4, 4)])

    def part(move_x, move_y, move_z):
        return full[
            4 + move_x : 4 + move_x + width_x,
            4 + move_y : 4 + move_y + width_y,
            4 + move_z : 4 + move_z + width_z,
        ]

    total = 3.0 * STENCIL[0] * part(0, 0, 0)
    for reach in range(1, 5):
        beside_all = (
            part(reach, 0, 0)
            + part(-reach, 0, 0)
            + part(0, reach, 0)
            + part(0, -reach, 0)
            + part(0, 0, reach)
            + part(0, 0, -reach)
        )
        total = total + STENCIL[reach] * beside_all
    return total


def lateral_filter(field, table):
    count = field.shape[1]
    index = jnp.arange(count)
    phase = index[:, None] * index[None, :] % count
    angle = 2.0 * math.pi / count * phase.astype(jnp.float32)
    cosine = jnp.cos(angle)
    sine = jnp.sin(angle)
    real_part = jnp.einsum("xyz,yk->xzk", field, cosine, precision=lax.Precision.HIGHEST)
    imag_part = jnp.einsum("xyz,yk->xzk", field, sine, precision=lax.Precision.HIGHEST)
    weight = table[None, :, :]
    back = jnp.einsum("xzk,yk->xyz", real_part * weight, cosine, precision=lax.Precision.HIGHEST)
    back = back + jnp.einsum(
        "xzk,yk->xyz", imag_part * weight, sine, precision=lax.Precision.HIGHEST
    )
    return back / count


def shot_bits(n):
    bits = []
    k = 1
    while k < n:
        bits.append(k)
        k *= 2
    assert k == n
    return bits


def ag_step(held, k, done):
    n = lax.axis_size("shot")
    me = lax.axis_index("shot")
    theirs = lax.ppermute(held, "shot", [(i, i ^ k) for i in range(n)])
    low = 2 ** sum(1 for b in done if b < k)
    shape = (held.shape[0] // low, 1, low) + held.shape[1:]
    mine, other = held.reshape(shape), theirs.reshape(shape)
    first = (me // k) % 2 == 0
    pair = jnp.where(first, jnp.concatenate([mine, other], axis=1), jnp.concatenate([other, mine], axis=1))
    return pair.reshape((2 * held.shape[0],) + held.shape[1:])


def swap_first(order):
    return order[1:2] + order[:1] + order[2:]


def swap_last(order):
    return order[:-2] + order[-1:] + order[-2:-1] if len(order) > 1 else order


def chain(held, kind, order, bits=None):
    if bits is None:
        bits = [] if kind == "ag" else sorted(order)
    return {"held": held, "kind": kind, "order": list(order), "i": 0, "bits": list(bits)}


def chain_step(c):
    k = c["order"][c["i"]]
    if c["kind"] == "ag":
        return ag_step(c["held"], k, c["bits"])
    return rs_step(c["held"], k, c["bits"])


def chain_commit(c, held):
    k = c["order"][c["i"]]
    c["held"] = held
    c["i"] += 1
    if c["kind"] == "ag":
        c["bits"].append(k)
    else:
        c["bits"].remove(k)


def rs_step(held, k, left):
    n = lax.axis_size("shot")
    me = lax.axis_index("shot")
    low = 2 ** left.index(k)
    high = held.shape[0] // (2 * low)
    split = held.reshape((high, 2, low) + held.shape[1:])
    mine = (me // k) % 2
    keep = lax.dynamic_index_in_dim(split, mine, axis=1, keepdims=False)
    send = lax.dynamic_index_in_dim(split, 1 - mine, axis=1, keepdims=False)
    got = lax.ppermute(send, "shot", [(i, i ^ k) for i in range(n)])
    return (keep + got).reshape((high * low,) + held.shape[1:])


def body(
    wave_prev,
    wave_now,
    velocity_code,
    perturb,
    gains,
    wavelet,
    source_index,
    receiver_index,
    absorb_width,
):
    shots, span_x, span_y, span_z = wave_now.shape
    n_shot = lax.axis_size("shot")
    me_shot = lax.axis_index("shot")
    bits = shot_bits(n_shot)
    start_x = lax.axis_index("space") * span_x
    total_x = span_x * lax.axis_size("space")
    speed_term = coefficient(velocity_code)
    positions = start_x.astype(jnp.float32) + jnp.arange(span_x, dtype=jnp.float32)
    absorber = damping(absorb_width, positions, total_x, span_y, span_z)
    cells = span_x * span_y * span_z
    offset = start_x * span_y * span_z
    source_local = source_index - offset
    source_owned = (source_local >= 0) & (source_local < cells)
    source_safe = jnp.clip(source_local, 0, cells - 1)
    plane = span_y * span_z
    sx = source_safe[0] // plane
    sy = (source_safe[0] // span_z) % span_y
    sz = source_safe[0] % span_z
    source_code = lax.dynamic_slice(velocity_code, (sx, sy, sz), (1, 1, 1)).reshape(1)
    source_gain = jnp.where(source_owned, coefficient(source_code), 0.0)
    barrier = lax.optimization_barrier

    hit = (
        (jnp.arange(span_x)[:, None, None] == sx)
        & (jnp.arange(span_y)[None, :, None] == sy)
        & (jnp.arange(span_z)[None, None, :] == sz)
    )

    def inject(field, moment):
        return field + jnp.where(hit, source_gain[0] * wavelet[0, moment], 0.0)

    def wave_step(current, prior, moment, last):
        drive = speed_term * laplace_x(with_halo(current))
        if last:
            return None, drive
        later = inject(2.0 * current - prior + drive - absorber * (current - prior), moment)
        return later, drive

    def born_second(born, field_model, drive):
        return (
            2.0 * born
            + speed_term * laplace_x(with_halo(born))
            - absorber * born
            + field_model * drive
        )

    slab = span_x // n_shot
    depth = perturb.shape[2]
    model_held = perturb.transpose(2, 0, 1).reshape(1, depth, span_x * span_y)
    gains_held = gains[None]
    st = {"w0": wave_now[0], "wp": wave_prev[0]}

    def task_wave(i):
        def run():
            last = i == 3
            cur, pri = (st["w0"], st["wp"]) if i == 0 else (st["w%d" % i], st["w%d" % (i - 1)])
            later, drive = wave_step(cur, pri, i, last)
            st["drive%d" % i] = drive
            if not last:
                st["w%d" % (i + 1)] = later
        return run

    def run_group(chains, compute):
        chains = [c for c in chains if c["i"] < len(c["order"])]
        moved = [chain_step(c) for c in chains]
        compute()
        keys = sorted(st.keys())
        out = barrier((moved, [st[n] for n in keys]))
        st.update(zip(keys, out[1]))
        for c, held in zip(chains, out[0]):
            chain_commit(c, held)

    def nothing():
        return None

    def light_prep():
        task_wave(1)()
        st["light"] = st["drive0"] * st["drive0"] + st["drive1"] * st["drive1"]

    def halves(x, axis):
        h = x.shape[axis] // 2
        return lax.slice_in_dim(x, 0, h, axis=axis), lax.slice_in_dim(x, h, x.shape[axis], axis=axis)

    far_first = list(reversed(bits))
    near_first = list(bits)

    top = far_first[0]
    model_c = chain(model_held, "ag", far_first[:1])
    gains_c = chain(gains_held, "ag", far_first)
    def first_steps():
        task_wave(0)()
        light_prep()

    tasks = [first_steps, task_wave(2)]
    run_group([model_c, gains_c], tasks[0])
    half_a, half_b = halves(model_c["held"], 1)
    model_a = chain(half_a, "ag", far_first[1:], [top])
    model_b = chain(half_b, "ag", swap_first(far_first[1:]), [top])
    light_a, light_b = halves(st["light"].reshape(n_shot, slab, span_y, span_z), 2)
    light_a = chain(light_a, "rs", near_first[:-1], near_first)
    light_b = chain(light_b, "rs", swap_first(near_first[:-1]), near_first)
    light_c = {}

    def light_next():
        if light_a["i"] < len(light_a["order"]):
            return [light_a, light_b]
        if not light_c:
            light_c.update(
                chain(jnp.concatenate([light_a["held"], light_b["held"]], axis=2), "rs", near_first[-1:], near_first[-1:])
            )
        return [light_c]

    for i in range(1, len(bits)):
        extra = light_next() if i == len(bits) - 1 else []
        run_group([model_a, model_b, gains_c] + extra, tasks[i] if i < len(tasks) else nothing)
    for i in range(len(bits), len(tasks)):
        tasks[i]()
    model_held = jnp.concatenate([model_a["held"], model_b["held"]], axis=1)
    gains_held = gains_c["held"]

    def born_pass():
        model = model_held.reshape(span_z, span_x * span_y).T.reshape(span_x, span_y, span_z)
        st["born1"] = model * st["drive0"]
        st["born2"] = born_second(st["born1"], model, st["drive1"])

    run_group(light_next(), born_pass)
    born1, born2 = st["born1"], st["born2"]

    image = st["drive0"] * born1 + st["drive1"] * born2
    image_a, image_b = halves(image.reshape(n_shot, slab, span_y, span_z), 2)
    image_a = chain(image_a, "rs", near_first[:-1], near_first)
    image_b = chain(image_b, "rs", swap_first(near_first[:-1]), near_first)
    tasks = [task_wave(3)]
    for i in range(len(bits) - 1):
        run_group([image_a, image_b] + light_next(), tasks[i] if i < len(tasks) else nothing)
    for i in range(len(bits) - 1, len(tasks)):
        tasks[i]()
    last = chain(
        jnp.concatenate([image_a["held"], image_b["held"]], axis=2), "rs", near_first[-1:], near_first[-1:]
    )
    run_group([last] + light_next(), nothing)
    image_part = last["held"][0]
    light_part = light_c["held"][0]

    table_all = gains_held.reshape(n_shot * gains.shape[0], gains.shape[1])
    filt_part = lateral_filter(image_part / (light_part + eps), table_all)
    filt_c = chain(filt_part[None], "ag", far_first[:1])
    run_group([filt_c], nothing)
    part_a, part_b = halves(filt_c["held"], 2)
    filt_a = chain(part_a, "ag", far_first[1:], [top])
    filt_b = chain(part_b, "ag", swap_first(far_first[1:]), [top])
    for i in range(1, len(bits)):
        run_group([filt_a, filt_b], nothing)
    new_model = jnp.concatenate([filt_a["held"], filt_b["held"]], axis=2).reshape(span_x, span_y, span_z)
    filtered = lax.dynamic_slice_in_dim(new_model, me_shot * depth, depth, 2)

    b1 = new_model * st["drive2"]
    b2 = born_second(b1, new_model, st["drive3"])

    receiver_local = receiver_index[0] - offset
    receiver_owned = (receiver_local >= 0) & (receiver_local < cells)
    receiver_safe = jnp.clip(receiver_local, 0, cells - 1)
    row = receiver_safe // span_z
    rz = receiver_safe % span_z
    lane = jnp.arange(span_z)[None, :] == rz[:, None]

    def sample(field):
        rows = jnp.take(field.reshape(span_x * span_y, span_z), row, axis=0)
        picked = jnp.sum(jnp.where(lane, rows, 0.0), axis=1)
        return jnp.where(receiver_owned, picked, 0.0)

    records = jnp.stack([sample(b1), sample(b2)], axis=0)[None]
    traces = records + lax.ppermute(records, "space", [(0, 1), (1, 0)])
    return (filtered, b2[None], traces)


def solution(mesh):
    in_specs = (
        P(("dom", "shot"), "space", None, None),
        P(("dom", "shot"), "space", None, None),
        P(("dom", "space"), None, None),
        P(("dom", "space"), None, "shot"),
        P(("dom", "shot"), None),
        P(("dom", "shot"), None),
        P(("dom", "shot")),
        P(("dom", "shot"), None),
        P("dom"),
    )
    out_specs = (
        P(("dom", "space"), None, "shot"),
        P(("dom", "shot"), "space", None, None),
        P(("dom", "shot"), None, None),
    )
    return jax.shard_map(body, mesh=mesh, in_specs=in_specs, out_specs=out_specs, check_vma=False)
```

```python
import math

import jax
import jax.numpy as jnp
from jax import lax
from jax.sharding import PartitionSpec as P

STEPS_A = 2
STEPS_B = 2


STENCIL = (-205.0 / 72.0, 8.0 / 5.0, -1.0 / 5.0, 8.0 / 315.0, -1.0 / 560.0)
damp_peak = 0.5
eps = 1e-05
HALO = 4


def coefficient(levels):
    speed = 1500.0 + 15.0 * levels.astype(jnp.float32)
    ratio = 0.45 * speed / 5325.0
    return ratio * ratio


def ramp(position, count, lower, upper):
    low_part = jnp.maximum(lower - position, 0.0) / lower
    high_part = jnp.maximum(upper - (count - 1.0 - position), 0.0) / upper
    return low_part * low_part + high_part * high_part


def damping(widths, positions, count_x, count_y, count_z):
    edges = widths.astype(jnp.float32)
    longest = max(positions.shape[0], count_y, count_z)
    line = jnp.arange(longest, dtype=jnp.float32)
    x_line = jnp.pad(positions, (0, longest - positions.shape[0]))
    place = jnp.stack([x_line, line, line])
    count = jnp.stack([jnp.asarray(count_x, jnp.float32), jnp.float32(count_y), jnp.float32(count_z)])[:, None]
    lower = jnp.stack([edges[0], edges[2], edges[4]])[:, None]
    upper = jnp.stack([edges[1], edges[3], edges[5]])[:, None]
    ramps = ramp(place, count, lower, upper)
    along_x = ramps[0, : positions.shape[0]]
    along_y = ramps[1, :count_y]
    along_z = ramps[2, :count_z]
    return damp_peak * (along_x[:, None, None] + along_y[None, :, None] + along_z[None, None, :])


def with_halo(x):
    size = lax.axis_size("space")
    length = x.shape[0]
    if size == 2:
        me = lax.axis_index("space")
        piece = lax.dynamic_slice_in_dim(x, (1 - me) * (length - HALO), HALO, 0)
        got = lax.ppermute(piece, "space", [(0, 1), (1, 0)])
        zeros = jnp.zeros((HALO,) + x.shape[1:], x.dtype)
        padded = jnp.concatenate([zeros, x, zeros], axis=0)
        return lax.dynamic_update_slice_in_dim(padded, got, (1 - me) * (length + HALO), 0)
    up = [(i, (i + 1) % size) for i in range(size - 1)]
    down = [(j, i) for i, j in up]
    before = lax.ppermute(x[length - HALO :], "space", up)
    after = lax.ppermute(x[:HALO], "space", down)
    return jnp.concatenate([before, x, after], axis=0)


def laplace_x(padded):
    width_x = padded.shape[0] - 8
    width_y = padded.shape[1]
    width_z = padded.shape[2]
    full = jnp.pad(padded, [(0, 0), (4, 4), (4, 4)])

    def part(move_x, move_y, move_z):
        return full[
            4 + move_x : 4 + move_x + width_x,
            4 + move_y : 4 + move_y + width_y,
            4 + move_z : 4 + move_z + width_z,
        ]

    total = 3.0 * STENCIL[0] * part(0, 0, 0)
    for reach in range(1, 5):
        beside_all = (
            part(reach, 0, 0)
            + part(-reach, 0, 0)
            + part(0, reach, 0)
            + part(0, -reach, 0)
            + part(0, 0, reach)
            + part(0, 0, -reach)
        )
        total = total + STENCIL[reach] * beside_all
    return total


def lateral_filter(field, table):
    count = field.shape[1]
    index = jnp.arange(count)
    phase = index[:, None] * index[None, :] % count
    angle = 2.0 * math.pi / count * phase.astype(jnp.float32)
    cosine = jnp.cos(angle)
    sine = jnp.sin(angle)
    real_part = jnp.einsum("xyz,yk->xzk", field, cosine, precision=lax.Precision.HIGHEST)
    imag_part = jnp.einsum("xyz,yk->xzk", field, sine, precision=lax.Precision.HIGHEST)
    weight = table[None, :, :]
    back = jnp.einsum("xzk,yk->xyz", real_part * weight, cosine, precision=lax.Precision.HIGHEST)
    back = back + jnp.einsum(
        "xzk,yk->xyz", imag_part * weight, sine, precision=lax.Precision.HIGHEST
    )
    return back / count


def shot_bits(n):
    bits = []
    k = 1
    while k < n:
        bits.append(k)
        k *= 2
    assert k == n
    return bits


def ag_step(held, k, done):
    n = lax.axis_size("shot")
    me = lax.axis_index("shot")
    theirs = lax.ppermute(held, "shot", [(i, i ^ k) for i in range(n)])
    low = 2 ** sum(1 for b in done if b < k)
    shape = (held.shape[0] // low, 1, low) + held.shape[1:]
    mine, other = held.reshape(shape), theirs.reshape(shape)
    first = (me // k) % 2 == 0
    pair = jnp.where(first, jnp.concatenate([mine, other], axis=1), jnp.concatenate([other, mine], axis=1))
    return pair.reshape((2 * held.shape[0],) + held.shape[1:])


def swap_first(order):
    return order[1:2] + order[:1] + order[2:]


def swap_last(order):
    return order[:-2] + order[-1:] + order[-2:-1] if len(order) > 1 else order


def chain(held, kind, order, bits=None):
    if bits is None:
        bits = [] if kind == "ag" else sorted(order)
    return {"held": held, "kind": kind, "order": list(order), "i": 0, "bits": list(bits)}


def chain_step(c):
    k = c["order"][c["i"]]
    if c["kind"] == "ag":
        return ag_step(c["held"], k, c["bits"])
    return rs_step(c["held"], k, c["bits"])


def chain_commit(c, held):
    k = c["order"][c["i"]]
    c["held"] = held
    c["i"] += 1
    if c["kind"] == "ag":
        c["bits"].append(k)
    else:
        c["bits"].remove(k)


def rs_step(held, k, left):
    n = lax.axis_size("shot")
    me = lax.axis_index("shot")
    low = 2 ** left.index(k)
    high = held.shape[0] // (2 * low)
    split = held.reshape((high, 2, low) + held.shape[1:])
    mine = (me // k) % 2
    keep = lax.dynamic_index_in_dim(split, mine, axis=1, keepdims=False)
    send = lax.dynamic_index_in_dim(split, 1 - mine, axis=1, keepdims=False)
    got = lax.ppermute(send, "shot", [(i, i ^ k) for i in range(n)])
    return (keep + got).reshape((high * low,) + held.shape[1:])


def body(
    wave_prev,
    wave_now,
    velocity_code,
    perturb,
    gains,
    wavelet,
    source_index,
    receiver_index,
    absorb_width,
):
    shots, span_x, span_y, span_z = wave_now.shape
    n_shot = lax.axis_size("shot")
    me_shot = lax.axis_index("shot")
    bits = shot_bits(n_shot)
    start_x = lax.axis_index("space") * span_x
    total_x = span_x * lax.axis_size("space")
    speed_term = coefficient(velocity_code)
    positions = start_x.astype(jnp.float32) + jnp.arange(span_x, dtype=jnp.float32)
    absorber = damping(absorb_width, positions, total_x, span_y, span_z)
    cells = span_x * span_y * span_z
    offset = start_x * span_y * span_z
    source_local = source_index - offset
    source_owned = (source_local >= 0) & (source_local < cells)
    source_safe = jnp.clip(source_local, 0, cells - 1)
    plane = span_y * span_z
    sx = source_safe[0] // plane
    sy = (source_safe[0] // span_z) % span_y
    sz = source_safe[0] % span_z
    source_code = lax.dynamic_slice(velocity_code, (sx, sy, sz), (1, 1, 1)).reshape(1)
    source_gain = jnp.where(source_owned, coefficient(source_code), 0.0)
    barrier = lax.optimization_barrier

    hit = (
        (jnp.arange(span_x)[:, None, None] == sx)
        & (jnp.arange(span_y)[None, :, None] == sy)
        & (jnp.arange(span_z)[None, None, :] == sz)
    )

    def inject(field, moment):
        return field + jnp.where(hit, source_gain[0] * wavelet[0, moment], 0.0)

    def wave_step(current, prior, moment, last):
        if moment == 0:
            inner = barrier(laplace_x(current))
            padded = with_halo(current)
            edge = 2 * HALO
            lap = jnp.concatenate(
                [laplace_x(padded[: edge + HALO]), inner, laplace_x(padded[padded.shape[0] - edge - HALO :])],
                axis=0,
            )
            drive = speed_term * lap
        else:
            drive = speed_term * laplace_x(with_halo(current))
        if last:
            return None, drive
        later = inject(2.0 * current - prior + drive - absorber * (current - prior), moment)
        return later, drive

    def born_second(born, field_model, drive):
        return (
            2.0 * born
            + speed_term * laplace_x(with_halo(born))
            - absorber * born
            + field_model * drive
        )

    slab = span_x // n_shot
    depth = perturb.shape[2]
    model_held = perturb.transpose(2, 0, 1).reshape(1, depth, span_x * span_y)
    gains_held = gains[None]
    st = {"w0": wave_now[0], "wp": wave_prev[0]}

    def task_wave(i):
        def run():
            last = i == 3
            cur, pri = (st["w0"], st["wp"]) if i == 0 else (st["w%d" % i], st["w%d" % (i - 1)])
            later, drive = wave_step(cur, pri, i, last)
            st["drive%d" % i] = drive
            if not last:
                st["w%d" % (i + 1)] = later
        return run

    def run_group(chains, compute):
        chains = [c for c in chains if c["i"] < len(c["order"])]
        moved = [chain_step(c) for c in chains]
        compute()
        keys = sorted(st.keys())
        out = barrier((moved, [st[n] for n in keys]))
        st.update(zip(keys, out[1]))
        for c, held in zip(chains, out[0]):
            chain_commit(c, held)

    def nothing():
        return None

    def light_prep():
        task_wave(1)()
        st["light"] = st["drive0"] * st["drive0"] + st["drive1"] * st["drive1"]

    def halves(x, axis):
        h = x.shape[axis] // 2
        return lax.slice_in_dim(x, 0, h, axis=axis), lax.slice_in_dim(x, h, x.shape[axis], axis=axis)

    far_first = list(reversed(bits))
    near_first = list(bits)

    top = far_first[0]
    model_c = chain(model_held, "ag", far_first[:1])
    gains_c = chain(gains_held, "ag", far_first)
    tasks = [task_wave(0), light_prep, task_wave(2)]
    run_group([model_c, gains_c], tasks[0])
    half_a, half_b = halves(model_c["held"], 1)
    model_a = chain(half_a, "ag", far_first[1:], [top])
    model_b = chain(half_b, "ag", swap_first(far_first[1:]), [top])
    for i in range(1, len(bits)):
        run_group([model_a, model_b, gains_c], tasks[i] if i < len(tasks) else nothing)
    for i in range(len(bits), len(tasks)):
        tasks[i]()
    model_held = jnp.concatenate([model_a["held"], model_b["held"]], axis=1)
    gains_held = gains_c["held"]
    light_a, light_b = halves(st["light"].reshape(n_shot, slab, span_y, span_z), 2)
    light_a = chain(light_a, "rs", near_first[:-1], near_first)
    light_b = chain(light_b, "rs", swap_first(near_first[:-1]), near_first)

    def born_pass():
        model = model_held.reshape(span_z, span_x * span_y).T.reshape(span_x, span_y, span_z)
        st["born1"] = model * st["drive0"]
        st["born2"] = born_second(st["born1"], model, st["drive1"])

    run_group([light_a, light_b], born_pass)
    born1, born2 = st["born1"], st["born2"]

    image = st["drive0"] * born1 + st["drive1"] * born2
    image_a, image_b = halves(image.reshape(n_shot, slab, span_y, span_z), 2)
    image_a = chain(image_a, "rs", near_first[:-1], near_first)
    image_b = chain(image_b, "rs", swap_first(near_first[:-1]), near_first)
    tasks = [task_wave(3)]
    light_c = None
    for i in range(len(bits) - 1):
        group = [image_a, image_b]
        if light_a["i"] < len(light_a["order"]):
            group += [light_a, light_b]
        elif light_c is None:
            light_c = chain(
                jnp.concatenate([light_a["held"], light_b["held"]], axis=2), "rs", near_first[-1:], near_first[-1:]
            )
            group.append(light_c)
        run_group(group, tasks[i] if i < len(tasks) else nothing)
    for i in range(len(bits) - 1, len(tasks)):
        tasks[i]()
    if light_c is None:
        light_c = chain(
            jnp.concatenate([light_a["held"], light_b["held"]], axis=2), "rs", near_first[-1:], near_first[-1:]
        )
    last = chain(
        jnp.concatenate([image_a["held"], image_b["held"]], axis=2), "rs", near_first[-1:], near_first[-1:]
    )
    run_group([last, light_c], nothing)
    image_part = last["held"][0]
    light_part = light_c["held"][0]

    table_all = gains_held.reshape(n_shot * gains.shape[0], gains.shape[1])
    filt_part = lateral_filter(image_part / (light_part + eps), table_all)
    filt_c = chain(filt_part[None], "ag", far_first[:1])
    run_group([filt_c], nothing)
    part_a, part_b = halves(filt_c["held"], 2)
    filt_a = chain(part_a, "ag", far_first[1:], [top])
    filt_b = chain(part_b, "ag", swap_first(far_first[1:]), [top])
    for i in range(1, len(bits)):
        run_group([filt_a, filt_b], nothing)
    new_model = jnp.concatenate([filt_a["held"], filt_b["held"]], axis=2).reshape(span_x, span_y, span_z)
    filtered = lax.dynamic_slice_in_dim(new_model, me_shot * depth, depth, 2)

    b1 = new_model * st["drive2"]
    b2 = born_second(b1, new_model, st["drive3"])

    receiver_local = receiver_index[0] - offset
    receiver_owned = (receiver_local >= 0) & (receiver_local < cells)
    receiver_safe = jnp.clip(receiver_local, 0, cells - 1)
    row = receiver_safe // span_z
    rz = receiver_safe % span_z
    lane = jnp.arange(span_z)[None, :] == rz[:, None]

    def sample(field):
        rows = jnp.take(field.reshape(span_x * span_y, span_z), row, axis=0)
        picked = jnp.sum(jnp.where(lane, rows, 0.0), axis=1)
        return jnp.where(receiver_owned, picked, 0.0)

    records = jnp.stack([sample(b1), sample(b2)], axis=0)[None]
    traces = records + lax.ppermute(records, "space", [(0, 1), (1, 0)])
    return (filtered, b2[None], traces)


def solution(mesh):
    in_specs = (
        P(("dom", "shot"), "space", None, None),
        P(("dom", "shot"), "space", None, None),
        P(("dom", "space"), None, None),
        P(("dom", "space"), None, "shot"),
        P(("dom", "shot"), None),
        P(("dom", "shot"), None),
        P(("dom", "shot")),
        P(("dom", "shot"), None),
        P("dom"),
    )
    out_specs = (
        P(("dom", "space"), None, "shot"),
        P(("dom", "shot"), "space", None, None),
        P(("dom", "shot"), None, None),
    )
    return jax.shard_map(body, mesh=mesh, in_specs=in_specs, out_specs=out_specs, check_vma=False)
```

```python
import math

import jax
import jax.numpy as jnp
from jax import lax
from jax.sharding import PartitionSpec as P

STEPS_A = 2
STEPS_B = 2


STENCIL = (-205.0 / 72.0, 8.0 / 5.0, -1.0 / 5.0, 8.0 / 315.0, -1.0 / 560.0)
damp_peak = 0.5
eps = 1e-05
HALO = 4


def coefficient(levels):
    speed = 1500.0 + 15.0 * levels.astype(jnp.float32)
    ratio = 0.45 * speed / 5325.0
    return ratio * ratio


def ramp(position, count, lower, upper):
    low_part = jnp.maximum(lower - position, 0.0) / lower
    high_part = jnp.maximum(upper - (count - 1.0 - position), 0.0) / upper
    return low_part * low_part + high_part * high_part


def damping(widths, positions, count_x, count_y, count_z):
    edges = widths.astype(jnp.float32)
    longest = max(positions.shape[0], count_y, count_z)
    line = jnp.arange(longest, dtype=jnp.float32)
    x_line = jnp.pad(positions, (0, longest - positions.shape[0]))
    place = jnp.stack([x_line, line, line])
    count = jnp.stack([jnp.asarray(count_x, jnp.float32), jnp.float32(count_y), jnp.float32(count_z)])[:, None]
    lower = jnp.stack([edges[0], edges[2], edges[4]])[:, None]
    upper = jnp.stack([edges[1], edges[3], edges[5]])[:, None]
    ramps = ramp(place, count, lower, upper)
    along_x = ramps[0, : positions.shape[0]]
    along_y = ramps[1, :count_y]
    along_z = ramps[2, :count_z]
    return damp_peak * (along_x[:, None, None] + along_y[None, :, None] + along_z[None, None, :])


def with_halo(x):
    size = lax.axis_size("space")
    length = x.shape[0]
    if size == 2:
        me = lax.axis_index("space")
        piece = lax.dynamic_slice_in_dim(x, (1 - me) * (length - HALO), HALO, 0)
        got = lax.ppermute(piece, "space", [(0, 1), (1, 0)])
        zeros = jnp.zeros((HALO,) + x.shape[1:], x.dtype)
        padded = jnp.concatenate([zeros, x, zeros], axis=0)
        return lax.dynamic_update_slice_in_dim(padded, got, (1 - me) * (length + HALO), 0)
    up = [(i, (i + 1) % size) for i in range(size - 1)]
    down = [(j, i) for i, j in up]
    before = lax.ppermute(x[length - HALO :], "space", up)
    after = lax.ppermute(x[:HALO], "space", down)
    return jnp.concatenate([before, x, after], axis=0)


def laplace_x(padded):
    width_x = padded.shape[0] - 8
    width_y = padded.shape[1]
    width_z = padded.shape[2]
    full = jnp.pad(padded, [(0, 0), (4, 4), (4, 4)])

    def part(move_x, move_y, move_z):
        return full[
            4 + move_x : 4 + move_x + width_x,
            4 + move_y : 4 + move_y + width_y,
            4 + move_z : 4 + move_z + width_z,
        ]

    total = 3.0 * STENCIL[0] * part(0, 0, 0)
    for reach in range(1, 5):
        beside_all = (
            part(reach, 0, 0)
            + part(-reach, 0, 0)
            + part(0, reach, 0)
            + part(0, -reach, 0)
            + part(0, 0, reach)
            + part(0, 0, -reach)
        )
        total = total + STENCIL[reach] * beside_all
    return total


def lateral_filter(field, table):
    count = field.shape[1]
    index = jnp.arange(count)
    phase = index[:, None] * index[None, :] % count
    angle = 2.0 * math.pi / count * phase.astype(jnp.float32)
    cosine = jnp.cos(angle)
    sine = jnp.sin(angle)
    real_part = jnp.einsum("xyz,yk->xzk", field, cosine, precision=lax.Precision.HIGHEST)
    imag_part = jnp.einsum("xyz,yk->xzk", field, sine, precision=lax.Precision.HIGHEST)
    weight = table[None, :, :]
    back = jnp.einsum("xzk,yk->xyz", real_part * weight, cosine, precision=lax.Precision.HIGHEST)
    back = back + jnp.einsum(
        "xzk,yk->xyz", imag_part * weight, sine, precision=lax.Precision.HIGHEST
    )
    return back / count


def shot_bits(n):
    bits = []
    k = 1
    while k < n:
        bits.append(k)
        k *= 2
    assert k == n
    return bits


def ag_step(held, k, done):
    n = lax.axis_size("shot")
    me = lax.axis_index("shot")
    theirs = lax.ppermute(held, "shot", [(i, i ^ k) for i in range(n)])
    low = 2 ** sum(1 for b in done if b < k)
    shape = (held.shape[0] // low, 1, low) + held.shape[1:]
    mine, other = held.reshape(shape), theirs.reshape(shape)
    first = (me // k) % 2 == 0
    pair = jnp.where(first, jnp.concatenate([mine, other], axis=1), jnp.concatenate([other, mine], axis=1))
    return pair.reshape((2 * held.shape[0],) + held.shape[1:])


def swap_first(order):
    return order[1:2] + order[:1] + order[2:]


def swap_last(order):
    return order[:-2] + order[-1:] + order[-2:-1] if len(order) > 1 else order


def chain(held, kind, order, bits=None):
    if bits is None:
        bits = [] if kind == "ag" else sorted(order)
    return {"held": held, "kind": kind, "order": list(order), "i": 0, "bits": list(bits)}


def split_step(held, k, left):
    me = lax.axis_index("shot")
    low = 2 ** left.index(k)
    high = held.shape[0] // (2 * low)
    split = held.reshape((high, 2, low) + held.shape[1:])
    mine = (me // k) % 2
    keep = lax.dynamic_index_in_dim(split, mine, axis=1, keepdims=False)
    send = lax.dynamic_index_in_dim(split, 1 - mine, axis=1, keepdims=False)
    shape = (high * low,) + held.shape[1:]
    return keep.reshape(shape), send.reshape(shape)


def chain_step(c):
    k = c["order"][c["i"]]
    if c["kind"] == "pre":
        n = lax.axis_size("shot")
        keep, send = c["slices"]()
        return keep + lax.ppermute(send, "shot", [(i, i ^ k) for i in range(n)])
    if c["kind"] == "ag":
        return ag_step(c["held"], k, c["bits"])
    return rs_step(c["held"], k, c["bits"])


def chain_commit(c, held):
    k = c["order"][c["i"]]
    c["held"] = held
    c["i"] += 1
    if c["kind"] == "ag":
        c["bits"].append(k)
    else:
        c["kind"] = "rs"
        c["bits"].remove(k)


def rs_step(held, k, left):
    n = lax.axis_size("shot")
    me = lax.axis_index("shot")
    low = 2 ** left.index(k)
    high = held.shape[0] // (2 * low)
    split = held.reshape((high, 2, low) + held.shape[1:])
    mine = (me // k) % 2
    keep = lax.dynamic_index_in_dim(split, mine, axis=1, keepdims=False)
    send = lax.dynamic_index_in_dim(split, 1 - mine, axis=1, keepdims=False)
    got = lax.ppermute(send, "shot", [(i, i ^ k) for i in range(n)])
    return (keep + got).reshape((high * low,) + held.shape[1:])


def body(
    wave_prev,
    wave_now,
    velocity_code,
    perturb,
    gains,
    wavelet,
    source_index,
    receiver_index,
    absorb_width,
):
    shots, span_x, span_y, span_z = wave_now.shape
    n_shot = lax.axis_size("shot")
    me_shot = lax.axis_index("shot")
    bits = shot_bits(n_shot)
    start_x = lax.axis_index("space") * span_x
    total_x = span_x * lax.axis_size("space")
    speed_term = coefficient(velocity_code)
    positions = start_x.astype(jnp.float32) + jnp.arange(span_x, dtype=jnp.float32)
    absorber = damping(absorb_width, positions, total_x, span_y, span_z)
    cells = span_x * span_y * span_z
    offset = start_x * span_y * span_z
    source_local = source_index - offset
    source_owned = (source_local >= 0) & (source_local < cells)
    source_safe = jnp.clip(source_local, 0, cells - 1)
    plane = span_y * span_z
    sx = source_safe[0] // plane
    sy = (source_safe[0] // span_z) % span_y
    sz = source_safe[0] % span_z
    source_code = lax.dynamic_slice(velocity_code, (sx, sy, sz), (1, 1, 1)).reshape(1)
    source_gain = jnp.where(source_owned, coefficient(source_code), 0.0)
    barrier = lax.optimization_barrier

    hit = (
        (jnp.arange(span_x)[:, None, None] == sx)
        & (jnp.arange(span_y)[None, :, None] == sy)
        & (jnp.arange(span_z)[None, None, :] == sz)
    )

    def inject(field, moment):
        return field + jnp.where(hit, source_gain[0] * wavelet[0, moment], 0.0)

    def wave_step(current, prior, moment, last):
        if moment == 0:
            inner = barrier(laplace_x(current))
            padded = with_halo(current)
            edge = 2 * HALO
            lap = jnp.concatenate(
                [laplace_x(padded[: edge + HALO]), inner, laplace_x(padded[padded.shape[0] - edge - HALO :])],
                axis=0,
            )
            drive = speed_term * lap
        else:
            drive = speed_term * laplace_x(with_halo(current))
        if last:
            return None, drive
        later = inject(2.0 * current - prior + drive - absorber * (current - prior), moment)
        return later, drive

    def born_second(born, field_model, drive):
        return (
            2.0 * born
            + speed_term * laplace_x(with_halo(born))
            - absorber * born
            + field_model * drive
        )

    slab = span_x // n_shot
    depth = perturb.shape[2]
    model_held = perturb.transpose(2, 0, 1).reshape(1, depth, span_x * span_y)
    gains_held = gains[None]
    st = {"w0": wave_now[0], "wp": wave_prev[0]}

    def task_wave(i):
        def run():
            last = i == 3
            cur, pri = (st["w0"], st["wp"]) if i == 0 else (st["w%d" % i], st["w%d" % (i - 1)])
            later, drive = wave_step(cur, pri, i, last)
            st["drive%d" % i] = drive
            if not last:
                st["w%d" % (i + 1)] = later
        return run

    def run_group(chains, compute):
        chains = [c for c in chains if c["i"] < len(c["order"])]
        moved = [chain_step(c) for c in chains]
        compute()
        keys = sorted(st.keys())
        out = barrier((moved, [st[n] for n in keys]))
        st.update(zip(keys, out[1]))
        for c, held in zip(chains, out[0]):
            chain_commit(c, held)

    def nothing():
        return None

    def light_prep():
        task_wave(1)()
        st["light"] = st["drive0"] * st["drive0"] + st["drive1"] * st["drive1"]

    def halves(x, axis):
        h = x.shape[axis] // 2
        return lax.slice_in_dim(x, 0, h, axis=axis), lax.slice_in_dim(x, h, x.shape[axis], axis=axis)

    far_first = list(reversed(bits))
    near_first = list(bits)

    top = far_first[0]
    model_c = chain(model_held, "ag", far_first[:1])
    gains_c = chain(gains_held, "ag", far_first)
    light_orders = {"la": near_first[:-1], "lb": swap_first(near_first[:-1])}

    def wave_and_split():
        task_wave(2)()
        pieces = halves(st["light"].reshape(n_shot, slab, span_y, span_z), 2)
        for (name, order), piece in zip(sorted(light_orders.items()), pieces):
            st[name + "_keep"], st[name + "_send"] = split_step(piece, order[0], list(near_first))

    tasks = [task_wave(0), light_prep, wave_and_split]
    run_group([model_c, gains_c], tasks[0])
    half_a, half_b = halves(model_c["held"], 1)
    model_a = chain(half_a, "ag", far_first[1:], [top])
    model_b = chain(half_b, "ag", swap_first(far_first[1:]), [top])
    for i in range(1, len(bits)):
        run_group([model_a, model_b, gains_c], tasks[i] if i < len(tasks) else nothing)
    for i in range(len(bits), len(tasks)):
        tasks[i]()
    model_held = jnp.concatenate([model_a["held"], model_b["held"]], axis=1)
    gains_held = gains_c["held"]
    light_a = chain(None, "pre", light_orders["la"], near_first)
    light_b = chain(None, "pre", light_orders["lb"], near_first)
    light_a["slices"] = lambda: (st["la_keep"], st["la_send"])
    light_b["slices"] = lambda: (st["lb_keep"], st["lb_send"])

    def born_pass():
        model = model_held.reshape(span_z, span_x * span_y).T.reshape(span_x, span_y, span_z)
        st["born1"] = model * st["drive0"]
        st["born2"] = born_second(st["born1"], model, st["drive1"])

    run_group([light_a, light_b], born_pass)
    born1, born2 = st["born1"], st["born2"]

    image = st["drive0"] * born1 + st["drive1"] * born2
    image_a, image_b = halves(image.reshape(n_shot, slab, span_y, span_z), 2)
    image_a = chain(image_a, "rs", near_first[:-1], near_first)
    image_b = chain(image_b, "rs", swap_first(near_first[:-1]), near_first)
    tasks = [task_wave(3)]
    light_c = None
    for i in range(len(bits) - 1):
        group = [image_a, image_b]
        if light_a["i"] < len(light_a["order"]):
            group += [light_a, light_b]
        elif light_c is None:
            light_c = chain(
                jnp.concatenate([light_a["held"], light_b["held"]], axis=2), "rs", near_first[-1:], near_first[-1:]
            )
            group.append(light_c)
        run_group(group, tasks[i] if i < len(tasks) else nothing)
    for i in range(len(bits) - 1, len(tasks)):
        tasks[i]()
    if light_c is None:
        light_c = chain(
            jnp.concatenate([light_a["held"], light_b["held"]], axis=2), "rs", near_first[-1:], near_first[-1:]
        )
    last = chain(
        jnp.concatenate([image_a["held"], image_b["held"]], axis=2), "rs", near_first[-1:], near_first[-1:]
    )
    run_group([last, light_c], nothing)
    image_part = last["held"][0]
    light_part = light_c["held"][0]

    table_all = gains_held.reshape(n_shot * gains.shape[0], gains.shape[1])
    filt_part = lateral_filter(image_part / (light_part + eps), table_all)
    filt_c = chain(filt_part[None], "ag", far_first[:1])
    run_group([filt_c], nothing)
    part_a, part_b = halves(filt_c["held"], 2)
    filt_a = chain(part_a, "ag", far_first[1:], [top])
    filt_b = chain(part_b, "ag", swap_first(far_first[1:]), [top])
    for i in range(1, len(bits)):
        run_group([filt_a, filt_b], nothing)
    new_model = jnp.concatenate([filt_a["held"], filt_b["held"]], axis=2).reshape(span_x, span_y, span_z)
    filtered = lax.dynamic_slice_in_dim(new_model, me_shot * depth, depth, 2)

    b1 = new_model * st["drive2"]
    b2 = born_second(b1, new_model, st["drive3"])

    receiver_local = receiver_index[0] - offset
    receiver_owned = (receiver_local >= 0) & (receiver_local < cells)
    receiver_safe = jnp.clip(receiver_local, 0, cells - 1)
    row = receiver_safe // span_z
    rz = receiver_safe % span_z
    lane = jnp.arange(span_z)[None, :] == rz[:, None]

    def sample(field):
        rows = jnp.take(field.reshape(span_x * span_y, span_z), row, axis=0)
        picked = jnp.sum(jnp.where(lane, rows, 0.0), axis=1)
        return jnp.where(receiver_owned, picked, 0.0)

    records = jnp.stack([sample(b1), sample(b2)], axis=0)[None]
    traces = records + lax.ppermute(records, "space", [(0, 1), (1, 0)])
    return (filtered, b2[None], traces)


def solution(mesh):
    in_specs = (
        P(("dom", "shot"), "space", None, None),
        P(("dom", "shot"), "space", None, None),
        P(("dom", "space"), None, None),
        P(("dom", "space"), None, "shot"),
        P(("dom", "shot"), None),
        P(("dom", "shot"), None),
        P(("dom", "shot")),
        P(("dom", "shot"), None),
        P("dom"),
    )
    out_specs = (
        P(("dom", "space"), None, "shot"),
        P(("dom", "shot"), "space", None, None),
        P(("dom", "shot"), None, None),
    )
    return jax.shard_map(body, mesh=mesh, in_specs=in_specs, out_specs=out_specs, check_vma=False)
```

```python
import math

import jax
import jax.numpy as jnp
from jax import lax
from jax.sharding import PartitionSpec as P

STEPS_A = 2
STEPS_B = 2


STENCIL = (-205.0 / 72.0, 8.0 / 5.0, -1.0 / 5.0, 8.0 / 315.0, -1.0 / 560.0)
damp_peak = 0.5
eps = 1e-05
HALO = 4


def coefficient(levels):
    speed = 1500.0 + 15.0 * levels.astype(jnp.float32)
    ratio = 0.45 * speed / 5325.0
    return ratio * ratio


def ramp(position, count, lower, upper):
    low_part = jnp.maximum(lower - position, 0.0) / lower
    high_part = jnp.maximum(upper - (count - 1.0 - position), 0.0) / upper
    return low_part * low_part + high_part * high_part


def damping(widths, positions, count_x, count_y, count_z):
    edges = widths.astype(jnp.float32)
    longest = max(positions.shape[0], count_y, count_z)
    line = jnp.arange(longest, dtype=jnp.float32)
    x_line = jnp.pad(positions, (0, longest - positions.shape[0]))
    place = jnp.stack([x_line, line, line])
    count = jnp.stack([jnp.asarray(count_x, jnp.float32), jnp.float32(count_y), jnp.float32(count_z)])[:, None]
    lower = jnp.stack([edges[0], edges[2], edges[4]])[:, None]
    upper = jnp.stack([edges[1], edges[3], edges[5]])[:, None]
    ramps = ramp(place, count, lower, upper)
    along_x = ramps[0, : positions.shape[0]]
    along_y = ramps[1, :count_y]
    along_z = ramps[2, :count_z]
    return damp_peak * (along_x[:, None, None] + along_y[None, :, None] + along_z[None, None, :])


def with_halo(x):
    size = lax.axis_size("space")
    length = x.shape[0]
    if size == 2:
        me = lax.axis_index("space")
        piece = lax.dynamic_slice_in_dim(x, (1 - me) * (length - HALO), HALO, 0)
        got = lax.ppermute(piece, "space", [(0, 1), (1, 0)])
        zeros = jnp.zeros((HALO,) + x.shape[1:], x.dtype)
        padded = jnp.concatenate([zeros, x, zeros], axis=0)
        return lax.dynamic_update_slice_in_dim(padded, got, (1 - me) * (length + HALO), 0)
    up = [(i, (i + 1) % size) for i in range(size - 1)]
    down = [(j, i) for i, j in up]
    before = lax.ppermute(x[length - HALO :], "space", up)
    after = lax.ppermute(x[:HALO], "space", down)
    return jnp.concatenate([before, x, after], axis=0)


def laplace_x(padded):
    width_x = padded.shape[0] - 8
    width_y = padded.shape[1]
    width_z = padded.shape[2]
    full = jnp.pad(padded, [(0, 0), (4, 4), (4, 4)])

    def part(move_x, move_y, move_z):
        return full[
            4 + move_x : 4 + move_x + width_x,
            4 + move_y : 4 + move_y + width_y,
            4 + move_z : 4 + move_z + width_z,
        ]

    total = 3.0 * STENCIL[0] * part(0, 0, 0)
    for reach in range(1, 5):
        beside_all = (
            part(reach, 0, 0)
            + part(-reach, 0, 0)
            + part(0, reach, 0)
            + part(0, -reach, 0)
            + part(0, 0, reach)
            + part(0, 0, -reach)
        )
        total = total + STENCIL[reach] * beside_all
    return total


def lateral_filter(field, table):
    count = field.shape[1]
    index = jnp.arange(count)
    phase = index[:, None] * index[None, :] % count
    angle = 2.0 * math.pi / count * phase.astype(jnp.float32)
    cosine = jnp.cos(angle)
    sine = jnp.sin(angle)
    real_part = jnp.einsum("xyz,yk->xzk", field, cosine, precision=lax.Precision.HIGHEST)
    imag_part = jnp.einsum("xyz,yk->xzk", field, sine, precision=lax.Precision.HIGHEST)
    weight = table[None, :, :]
    back = jnp.einsum("xzk,yk->xyz", real_part * weight, cosine, precision=lax.Precision.HIGHEST)
    back = back + jnp.einsum(
        "xzk,yk->xyz", imag_part * weight, sine, precision=lax.Precision.HIGHEST
    )
    return back / count


def shot_bits(n):
    bits = []
    k = 1
    while k < n:
        bits.append(k)
        k *= 2
    assert k == n
    return bits


def ag_step(held, k, done):
    n = lax.axis_size("shot")
    me = lax.axis_index("shot")
    theirs = lax.ppermute(held, "shot", [(i, i ^ k) for i in range(n)])
    low = 2 ** sum(1 for b in done if b < k)
    shape = (held.shape[0] // low, 1, low) + held.shape[1:]
    mine, other = held.reshape(shape), theirs.reshape(shape)
    first = (me // k) % 2 == 0
    pair = jnp.where(first, jnp.concatenate([mine, other], axis=1), jnp.concatenate([other, mine], axis=1))
    return pair.reshape((2 * held.shape[0],) + held.shape[1:])


def swap_first(order):
    return order[1:2] + order[:1] + order[2:]


def swap_last(order):
    return order[:-2] + order[-1:] + order[-2:-1] if len(order) > 1 else order


def chain(held, kind, order, bits=None):
    if bits is None:
        bits = [] if kind == "ag" else sorted(order)
    return {"held": held, "kind": kind, "order": list(order), "i": 0, "bits": list(bits)}


def split_step(held, k, left):
    me = lax.axis_index("shot")
    low = 2 ** left.index(k)
    high = held.shape[0] // (2 * low)
    split = held.reshape((high, 2, low) + held.shape[1:])
    mine = (me // k) % 2
    keep = lax.dynamic_index_in_dim(split, mine, axis=1, keepdims=False)
    send = lax.dynamic_index_in_dim(split, 1 - mine, axis=1, keepdims=False)
    shape = (high * low,) + held.shape[1:]
    return keep.reshape(shape), send.reshape(shape)


def chain_step(c):
    k = c["order"][c["i"]]
    if c["kind"] == "pre":
        n = lax.axis_size("shot")
        keep, send = c["slices"]()
        return keep + lax.ppermute(send, "shot", [(i, i ^ k) for i in range(n)])
    if c["kind"] == "ag":
        return ag_step(c["held"], k, c["bits"])
    return rs_step(c["held"], k, c["bits"])


def chain_commit(c, held):
    k = c["order"][c["i"]]
    c["held"] = held
    c["i"] += 1
    if c["kind"] == "ag":
        c["bits"].append(k)
    else:
        c["kind"] = "rs"
        c["bits"].remove(k)


def rs_step(held, k, left):
    n = lax.axis_size("shot")
    me = lax.axis_index("shot")
    low = 2 ** left.index(k)
    high = held.shape[0] // (2 * low)
    split = held.reshape((high, 2, low) + held.shape[1:])
    mine = (me // k) % 2
    keep = lax.dynamic_index_in_dim(split, mine, axis=1, keepdims=False)
    send = lax.dynamic_index_in_dim(split, 1 - mine, axis=1, keepdims=False)
    got = lax.ppermute(send, "shot", [(i, i ^ k) for i in range(n)])
    return (keep + got).reshape((high * low,) + held.shape[1:])


def body(
    wave_prev,
    wave_now,
    velocity_code,
    perturb,
    gains,
    wavelet,
    source_index,
    receiver_index,
    absorb_width,
):
    shots, span_x, span_y, span_z = wave_now.shape
    n_shot = lax.axis_size("shot")
    me_shot = lax.axis_index("shot")
    bits = shot_bits(n_shot)
    start_x = lax.axis_index("space") * span_x
    total_x = span_x * lax.axis_size("space")
    speed_term = coefficient(velocity_code)
    positions = start_x.astype(jnp.float32) + jnp.arange(span_x, dtype=jnp.float32)
    absorber = damping(absorb_width, positions, total_x, span_y, span_z)
    cells = span_x * span_y * span_z
    offset = start_x * span_y * span_z
    source_local = source_index - offset
    source_owned = (source_local >= 0) & (source_local < cells)
    source_safe = jnp.clip(source_local, 0, cells - 1)
    plane = span_y * span_z
    sx = source_safe[0] // plane
    sy = (source_safe[0] // span_z) % span_y
    sz = source_safe[0] % span_z
    source_code = lax.dynamic_slice(velocity_code, (sx, sy, sz), (1, 1, 1)).reshape(1)
    source_gain = jnp.where(source_owned, coefficient(source_code), 0.0)
    barrier = lax.optimization_barrier

    hit = (
        (jnp.arange(span_x)[:, None, None] == sx)
        & (jnp.arange(span_y)[None, :, None] == sy)
        & (jnp.arange(span_z)[None, None, :] == sz)
    )

    def inject(field, moment):
        return field + jnp.where(hit, source_gain[0] * wavelet[0, moment], 0.0)

    def wave_step(current, prior, moment, last):
        if moment == 0:
            inner = barrier(laplace_x(current))
            padded = with_halo(current)
            edge = 2 * HALO
            lap = jnp.concatenate(
                [laplace_x(padded[: edge + HALO]), inner, laplace_x(padded[padded.shape[0] - edge - HALO :])],
                axis=0,
            )
            drive = speed_term * lap
        else:
            drive = speed_term * laplace_x(with_halo(current))
        if last:
            return None, drive
        later = inject(2.0 * current - prior + drive - absorber * (current - prior), moment)
        return later, drive

    def born_second(born, field_model, drive):
        return (
            2.0 * born
            + speed_term * laplace_x(with_halo(born))
            - absorber * born
            + field_model * drive
        )

    slab = span_x // n_shot
    depth = perturb.shape[2]
    model_held = perturb.transpose(2, 0, 1).reshape(1, depth, span_x * span_y)
    gains_held = gains[None]
    st = {"w0": wave_now[0], "wp": wave_prev[0]}

    def task_wave(i):
        def run():
            last = i == 3
            cur, pri = (st["w0"], st["wp"]) if i == 0 else (st["w%d" % i], st["w%d" % (i - 1)])
            later, drive = wave_step(cur, pri, i, last)
            st["drive%d" % i] = drive
            if not last:
                st["w%d" % (i + 1)] = later
        return run

    def run_group(chains, compute):
        chains = [c for c in chains if c["i"] < len(c["order"])]
        moved = [chain_step(c) for c in chains]
        compute()
        keys = sorted(st.keys())
        out = barrier((moved, [st[n] for n in keys]))
        st.update(zip(keys, out[1]))
        for c, held in zip(chains, out[0]):
            chain_commit(c, held)

    def nothing():
        return None

    def light_prep():
        task_wave(1)()
        st["light"] = st["drive0"] * st["drive0"] + st["drive1"] * st["drive1"]

    def halves(x, axis):
        h = x.shape[axis] // 2
        return lax.slice_in_dim(x, 0, h, axis=axis), lax.slice_in_dim(x, h, x.shape[axis], axis=axis)

    far_first = list(reversed(bits))
    near_first = list(bits)

    top = far_first[0]
    model_c = chain(model_held, "ag", far_first[:1])
    gains_c = chain(gains_held, "ag", far_first)
    light_orders = {"la": near_first[:-1], "lb": swap_first(near_first[:-1])}

    def wave_and_split():
        task_wave(2)()
        pieces = halves(st["light"].reshape(n_shot, slab, span_y, span_z), 2)
        for (name, order), piece in zip(sorted(light_orders.items()), pieces):
            st[name + "_keep"], st[name + "_send"] = split_step(piece, order[0], list(near_first))

    tasks = [task_wave(0), light_prep, wave_and_split]
    run_group([model_c], tasks[0])
    half_a, half_b = halves(model_c["held"], 1)
    model_a = chain(half_a, "ag", far_first[1:], [top])
    model_b = chain(half_b, "ag", swap_first(far_first[1:]), [top])
    for i in range(1, len(bits)):
        run_group([model_a, model_b], tasks[i] if i < len(tasks) else nothing)
    for i in range(len(bits), len(tasks)):
        tasks[i]()
    model_held = jnp.concatenate([model_a["held"], model_b["held"]], axis=1)
    light_a = chain(None, "pre", light_orders["la"], near_first)
    light_b = chain(None, "pre", light_orders["lb"], near_first)
    light_a["slices"] = lambda: (st["la_keep"], st["la_send"])
    light_b["slices"] = lambda: (st["lb_keep"], st["lb_send"])

    def born_pass():
        model = model_held.reshape(span_z, span_x * span_y).T.reshape(span_x, span_y, span_z)
        st["born1"] = model * st["drive0"]
        st["born2"] = born_second(st["born1"], model, st["drive1"])

    run_group([light_a, light_b], born_pass)
    born1, born2 = st["born1"], st["born2"]

    image = st["drive0"] * born1 + st["drive1"] * born2
    image_a, image_b = halves(image.reshape(n_shot, slab, span_y, span_z), 2)
    image_a = chain(image_a, "rs", near_first[:-1], near_first)
    image_b = chain(image_b, "rs", swap_first(near_first[:-1]), near_first)
    tasks = [task_wave(3)]
    light_c = None
    for i in range(len(bits) - 1):
        group = [image_a, image_b, gains_c]
        if light_a["i"] < len(light_a["order"]):
            group += [light_a, light_b]
        elif light_c is None:
            light_c = chain(
                jnp.concatenate([light_a["held"], light_b["held"]], axis=2), "rs", near_first[-1:], near_first[-1:]
            )
            group.append(light_c)
        run_group(group, tasks[i] if i < len(tasks) else nothing)
    for i in range(len(bits) - 1, len(tasks)):
        tasks[i]()
    if light_c is None:
        light_c = chain(
            jnp.concatenate([light_a["held"], light_b["held"]], axis=2), "rs", near_first[-1:], near_first[-1:]
        )
    last = chain(
        jnp.concatenate([image_a["held"], image_b["held"]], axis=2), "rs", near_first[-1:], near_first[-1:]
    )
    run_group([last, light_c, gains_c], nothing)
    while gains_c["i"] < len(gains_c["order"]):
        run_group([gains_c], nothing)
    gains_held = gains_c["held"]
    image_part = last["held"][0]
    light_part = light_c["held"][0]

    table_all = gains_held.reshape(n_shot * gains.shape[0], gains.shape[1])
    filt_part = lateral_filter(image_part / (light_part + eps), table_all)
    filt_c = chain(filt_part[None], "ag", far_first[:1])
    run_group([filt_c], nothing)
    part_a, part_b = halves(filt_c["held"], 2)
    filt_a = chain(part_a, "ag", far_first[1:], [top])
    filt_b = chain(part_b, "ag", swap_first(far_first[1:]), [top])
    for i in range(1, len(bits)):
        run_group([filt_a, filt_b], nothing)
    new_model = jnp.concatenate([filt_a["held"], filt_b["held"]], axis=2).reshape(span_x, span_y, span_z)
    filtered = lax.dynamic_slice_in_dim(new_model, me_shot * depth, depth, 2)

    b1 = new_model * st["drive2"]
    b2 = born_second(b1, new_model, st["drive3"])

    receiver_local = receiver_index[0] - offset
    receiver_owned = (receiver_local >= 0) & (receiver_local < cells)
    receiver_safe = jnp.clip(receiver_local, 0, cells - 1)
    row = receiver_safe // span_z
    rz = receiver_safe % span_z
    lane = jnp.arange(span_z)[None, :] == rz[:, None]

    def sample(field):
        rows = jnp.take(field.reshape(span_x * span_y, span_z), row, axis=0)
        picked = jnp.sum(jnp.where(lane, rows, 0.0), axis=1)
        return jnp.where(receiver_owned, picked, 0.0)

    records = jnp.stack([sample(b1), sample(b2)], axis=0)[None]
    traces = records + lax.ppermute(records, "space", [(0, 1), (1, 0)])
    return (filtered, b2[None], traces)


def solution(mesh):
    in_specs = (
        P(("dom", "shot"), "space", None, None),
        P(("dom", "shot"), "space", None, None),
        P(("dom", "space"), None, None),
        P(("dom", "space"), None, "shot"),
        P(("dom", "shot"), None),
        P(("dom", "shot"), None),
        P(("dom", "shot")),
        P(("dom", "shot"), None),
        P("dom"),
    )
    out_specs = (
        P(("dom", "space"), None, "shot"),
        P(("dom", "shot"), "space", None, None),
        P(("dom", "shot"), None, None),
    )
    return jax.shard_map(body, mesh=mesh, in_specs=in_specs, out_specs=out_specs, check_vma=False)
```

```python
import math

import jax
import jax.numpy as jnp
from jax import lax
from jax.sharding import PartitionSpec as P

STEPS_A = 2
STEPS_B = 2


STENCIL = (-205.0 / 72.0, 8.0 / 5.0, -1.0 / 5.0, 8.0 / 315.0, -1.0 / 560.0)
damp_peak = 0.5
eps = 1e-05
HALO = 4


def coefficient(levels):
    speed = 1500.0 + 15.0 * levels.astype(jnp.float32)
    ratio = 0.45 * speed / 5325.0
    return ratio * ratio


def ramp(position, count, lower, upper):
    low_part = jnp.maximum(lower - position, 0.0) / lower
    high_part = jnp.maximum(upper - (count - 1.0 - position), 0.0) / upper
    return low_part * low_part + high_part * high_part


def damping(widths, positions, count_x, count_y, count_z):
    edges = widths.astype(jnp.float32)
    longest = max(positions.shape[0], count_y, count_z)
    line = jnp.arange(longest, dtype=jnp.float32)
    x_line = jnp.pad(positions, (0, longest - positions.shape[0]))
    place = jnp.stack([x_line, line, line])
    count = jnp.stack([jnp.asarray(count_x, jnp.float32), jnp.float32(count_y), jnp.float32(count_z)])[:, None]
    lower = jnp.stack([edges[0], edges[2], edges[4]])[:, None]
    upper = jnp.stack([edges[1], edges[3], edges[5]])[:, None]
    ramps = ramp(place, count, lower, upper)
    along_x = ramps[0, : positions.shape[0]]
    along_y = ramps[1, :count_y]
    along_z = ramps[2, :count_z]
    return damp_peak * (along_x[:, None, None] + along_y[None, :, None] + along_z[None, None, :])


def with_halo(x):
    size = lax.axis_size("space")
    length = x.shape[0]
    if size == 2:
        me = lax.axis_index("space")
        piece = lax.dynamic_slice_in_dim(x, (1 - me) * (length - HALO), HALO, 0)
        got = lax.ppermute(piece, "space", [(0, 1), (1, 0)])
        zeros = jnp.zeros((HALO,) + x.shape[1:], x.dtype)
        padded = jnp.concatenate([zeros, x, zeros], axis=0)
        return lax.dynamic_update_slice_in_dim(padded, got, (1 - me) * (length + HALO), 0)
    up = [(i, (i + 1) % size) for i in range(size - 1)]
    down = [(j, i) for i, j in up]
    before = lax.ppermute(x[length - HALO :], "space", up)
    after = lax.ppermute(x[:HALO], "space", down)
    return jnp.concatenate([before, x, after], axis=0)


def laplace_x(padded):
    width_x = padded.shape[0] - 8
    width_y = padded.shape[1]
    width_z = padded.shape[2]
    full = jnp.pad(padded, [(0, 0), (4, 4), (4, 4)])

    def part(move_x, move_y, move_z):
        return full[
            4 + move_x : 4 + move_x + width_x,
            4 + move_y : 4 + move_y + width_y,
            4 + move_z : 4 + move_z + width_z,
        ]

    total = 3.0 * STENCIL[0] * part(0, 0, 0)
    for reach in range(1, 5):
        beside_all = (
            part(reach, 0, 0)
            + part(-reach, 0, 0)
            + part(0, reach, 0)
            + part(0, -reach, 0)
            + part(0, 0, reach)
            + part(0, 0, -reach)
        )
        total = total + STENCIL[reach] * beside_all
    return total


def lateral_filter(field, table):
    count = field.shape[1]
    index = jnp.arange(count)
    phase = index[:, None] * index[None, :] % count
    angle = 2.0 * math.pi / count * phase.astype(jnp.float32)
    cosine = jnp.cos(angle)
    sine = jnp.sin(angle)
    real_part = jnp.einsum("xyz,yk->xzk", field, cosine, precision=lax.Precision.HIGHEST)
    imag_part = jnp.einsum("xyz,yk->xzk", field, sine, precision=lax.Precision.HIGHEST)
    weight = table[None, :, :]
    back = jnp.einsum("xzk,yk->xyz", real_part * weight, cosine, precision=lax.Precision.HIGHEST)
    back = back + jnp.einsum(
        "xzk,yk->xyz", imag_part * weight, sine, precision=lax.Precision.HIGHEST
    )
    return back / count


def shot_bits(n):
    bits = []
    k = 1
    while k < n:
        bits.append(k)
        k *= 2
    assert k == n
    return bits


def ag_step(held, k, done):
    n = lax.axis_size("shot")
    me = lax.axis_index("shot")
    theirs = lax.ppermute(held, "shot", [(i, i ^ k) for i in range(n)])
    low = 2 ** sum(1 for b in done if b < k)
    shape = (held.shape[0] // low, 1, low) + held.shape[1:]
    mine, other = held.reshape(shape), theirs.reshape(shape)
    first = (me // k) % 2 == 0
    pair = jnp.where(first, jnp.concatenate([mine, other], axis=1), jnp.concatenate([other, mine], axis=1))
    return pair.reshape((2 * held.shape[0],) + held.shape[1:])


def swap_first(order):
    return order[1:2] + order[:1] + order[2:]


def swap_last(order):
    return order[:-2] + order[-1:] + order[-2:-1] if len(order) > 1 else order


def chain(held, kind, order, bits=None):
    if bits is None:
        bits = [] if kind == "ag" else sorted(order)
    return {"held": held, "kind": kind, "order": list(order), "i": 0, "bits": list(bits)}


def split_step(held, k, left):
    me = lax.axis_index("shot")
    low = 2 ** left.index(k)
    high = held.shape[0] // (2 * low)
    split = held.reshape((high, 2, low) + held.shape[1:])
    mine = (me // k) % 2
    keep = lax.dynamic_index_in_dim(split, mine, axis=1, keepdims=False)
    send = lax.dynamic_index_in_dim(split, 1 - mine, axis=1, keepdims=False)
    shape = (high * low,) + held.shape[1:]
    return keep.reshape(shape), send.reshape(shape)


def chain_step(c):
    k = c["order"][c["i"]]
    if c["kind"] == "pre":
        n = lax.axis_size("shot")
        keep, send = c["slices"]()
        return keep + lax.ppermute(send, "shot", [(i, i ^ k) for i in range(n)])
    if c["kind"] == "ag":
        return ag_step(c["held"], k, c["bits"])
    return rs_step(c["held"], k, c["bits"])


def chain_commit(c, held):
    k = c["order"][c["i"]]
    c["held"] = held
    c["i"] += 1
    if c["kind"] == "ag":
        c["bits"].append(k)
    else:
        c["kind"] = "rs"
        c["bits"].remove(k)


def rs_step(held, k, left):
    n = lax.axis_size("shot")
    me = lax.axis_index("shot")
    low = 2 ** left.index(k)
    high = held.shape[0] // (2 * low)
    split = held.reshape((high, 2, low) + held.shape[1:])
    mine = (me // k) % 2
    keep = lax.dynamic_index_in_dim(split, mine, axis=1, keepdims=False)
    send = lax.dynamic_index_in_dim(split, 1 - mine, axis=1, keepdims=False)
    got = lax.ppermute(send, "shot", [(i, i ^ k) for i in range(n)])
    return (keep + got).reshape((high * low,) + held.shape[1:])


def body(
    wave_prev,
    wave_now,
    velocity_code,
    perturb,
    gains,
    wavelet,
    source_index,
    receiver_index,
    absorb_width,
):
    shots, span_x, span_y, span_z = wave_now.shape
    n_shot = lax.axis_size("shot")
    me_shot = lax.axis_index("shot")
    bits = shot_bits(n_shot)
    start_x = lax.axis_index("space") * span_x
    total_x = span_x * lax.axis_size("space")
    speed_term = coefficient(velocity_code)
    positions = start_x.astype(jnp.float32) + jnp.arange(span_x, dtype=jnp.float32)
    absorber = damping(absorb_width, positions, total_x, span_y, span_z)
    cells = span_x * span_y * span_z
    offset = start_x * span_y * span_z
    source_local = source_index - offset
    source_owned = (source_local >= 0) & (source_local < cells)
    source_safe = jnp.clip(source_local, 0, cells - 1)
    plane = span_y * span_z
    sx = source_safe[0] // plane
    sy = (source_safe[0] // span_z) % span_y
    sz = source_safe[0] % span_z
    source_code = lax.dynamic_slice(velocity_code, (sx, sy, sz), (1, 1, 1)).reshape(1)
    source_gain = jnp.where(source_owned, coefficient(source_code), 0.0)
    barrier = lax.optimization_barrier

    hit = (
        (jnp.arange(span_x)[:, None, None] == sx)
        & (jnp.arange(span_y)[None, :, None] == sy)
        & (jnp.arange(span_z)[None, None, :] == sz)
    )

    def inject(field, moment):
        return field + jnp.where(hit, source_gain[0] * wavelet[0, moment], 0.0)

    def wave_step(current, prior, moment, last):
        if moment == 0:
            inner = barrier(laplace_x(current))
            padded = with_halo(current)
            edge = 2 * HALO
            lap = jnp.concatenate(
                [laplace_x(padded[: edge + HALO]), inner, laplace_x(padded[padded.shape[0] - edge - HALO :])],
                axis=0,
            )
            drive = speed_term * lap
        else:
            drive = speed_term * laplace_x(with_halo(current))
        if last:
            return None, drive
        later = inject(2.0 * current - prior + drive - absorber * (current - prior), moment)
        return later, drive

    def born_second(born, field_model, drive):
        return (
            2.0 * born
            + speed_term * laplace_x(with_halo(born))
            - absorber * born
            + field_model * drive
        )

    slab = span_x // n_shot
    depth = perturb.shape[2]
    model_held = perturb.transpose(2, 0, 1).reshape(1, depth, span_x * span_y)
    gains_held = gains[None]
    st = {"w0": wave_now[0], "wp": wave_prev[0]}

    def task_wave(i):
        def run():
            last = i == 3
            cur, pri = (st["w0"], st["wp"]) if i == 0 else (st["w%d" % i], st["w%d" % (i - 1)])
            later, drive = wave_step(cur, pri, i, last)
            st["drive%d" % i] = drive
            if not last:
                st["w%d" % (i + 1)] = later
        return run

    def run_group(chains, compute):
        chains = [c for c in chains if c["i"] < len(c["order"])]
        moved = [chain_step(c) for c in chains]
        compute()
        keys = sorted(st.keys())
        out = barrier((moved, [st[n] for n in keys]))
        st.update(zip(keys, out[1]))
        for c, held in zip(chains, out[0]):
            chain_commit(c, held)

    def nothing():
        return None

    def light_prep():
        task_wave(1)()
        st["light"] = st["drive0"] * st["drive0"] + st["drive1"] * st["drive1"]

    def halves(x, axis):
        h = x.shape[axis] // 2
        return lax.slice_in_dim(x, 0, h, axis=axis), lax.slice_in_dim(x, h, x.shape[axis], axis=axis)

    far_first = list(reversed(bits))
    near_first = list(bits)

    top = far_first[0]
    model_c = chain(model_held, "ag", far_first[:1])
    gains_c = chain(gains_held, "ag", far_first)
    light_orders = {"la": near_first[:-1], "lb": swap_first(near_first[:-1])}

    def wave_and_split():
        pieces = halves(st["light"].reshape(n_shot, slab, span_y, span_z), 2)
        for (name, order), piece in zip(sorted(light_orders.items()), pieces):
            st[name + "_keep"], st[name + "_send"] = split_step(piece, order[0], list(near_first))

    tasks = [task_wave(0), light_prep, wave_and_split]
    run_group([model_c, gains_c], tasks[0])
    half_a, half_b = halves(model_c["held"], 1)
    model_a = chain(half_a, "ag", far_first[1:], [top])
    model_b = chain(half_b, "ag", swap_first(far_first[1:]), [top])
    for i in range(1, len(bits)):
        run_group([model_a, model_b, gains_c], tasks[i] if i < len(tasks) else nothing)
    for i in range(len(bits), len(tasks)):
        tasks[i]()
    model_held = jnp.concatenate([model_a["held"], model_b["held"]], axis=1)
    gains_held = gains_c["held"]
    light_a = chain(None, "pre", light_orders["la"], near_first)
    light_b = chain(None, "pre", light_orders["lb"], near_first)
    light_a["slices"] = lambda: (st["la_keep"], st["la_send"])
    light_b["slices"] = lambda: (st["lb_keep"], st["lb_send"])

    def born_pass():
        model = model_held.reshape(span_z, span_x * span_y).T.reshape(span_x, span_y, span_z)
        st["born1"] = model * st["drive0"]
        st["born2"] = born_second(st["born1"], model, st["drive1"])

    run_group([light_a, light_b], born_pass)
    born1, born2 = st["born1"], st["born2"]

    image = st["drive0"] * born1 + st["drive1"] * born2
    image_a, image_b = halves(image.reshape(n_shot, slab, span_y, span_z), 2)
    image_a = chain(image_a, "rs", near_first[:-1], near_first)
    image_b = chain(image_b, "rs", swap_first(near_first[:-1]), near_first)
    tasks = [task_wave(2), task_wave(3)]
    light_c = None
    for i in range(len(bits) - 1):
        group = [image_a, image_b]
        if light_a["i"] < len(light_a["order"]):
            group += [light_a, light_b]
        elif light_c is None:
            light_c = chain(
                jnp.concatenate([light_a["held"], light_b["held"]], axis=2), "rs", near_first[-1:], near_first[-1:]
            )
            group.append(light_c)
        run_group(group, tasks[i] if i < len(tasks) else nothing)
    for i in range(len(bits) - 1, len(tasks)):
        tasks[i]()
    if light_c is None:
        light_c = chain(
            jnp.concatenate([light_a["held"], light_b["held"]], axis=2), "rs", near_first[-1:], near_first[-1:]
        )
    last = chain(
        jnp.concatenate([image_a["held"], image_b["held"]], axis=2), "rs", near_first[-1:], near_first[-1:]
    )
    run_group([last, light_c], nothing)
    image_part = last["held"][0]
    light_part = light_c["held"][0]

    table_all = gains_held.reshape(n_shot * gains.shape[0], gains.shape[1])
    filt_part = lateral_filter(image_part / (light_part + eps), table_all)
    filt_c = chain(filt_part[None], "ag", far_first[:1])
    run_group([filt_c], nothing)
    part_a, part_b = halves(filt_c["held"], 2)
    filt_a = chain(part_a, "ag", far_first[1:], [top])
    filt_b = chain(part_b, "ag", swap_first(far_first[1:]), [top])
    for i in range(1, len(bits)):
        run_group([filt_a, filt_b], nothing)
    new_model = jnp.concatenate([filt_a["held"], filt_b["held"]], axis=2).reshape(span_x, span_y, span_z)
    filtered = lax.dynamic_slice_in_dim(new_model, me_shot * depth, depth, 2)

    b1 = new_model * st["drive2"]
    b2 = born_second(b1, new_model, st["drive3"])

    receiver_local = receiver_index[0] - offset
    receiver_owned = (receiver_local >= 0) & (receiver_local < cells)
    receiver_safe = jnp.clip(receiver_local, 0, cells - 1)
    row = receiver_safe // span_z
    rz = receiver_safe % span_z
    lane = jnp.arange(span_z)[None, :] == rz[:, None]

    def sample(field):
        rows = jnp.take(field.reshape(span_x * span_y, span_z), row, axis=0)
        picked = jnp.sum(jnp.where(lane, rows, 0.0), axis=1)
        return jnp.where(receiver_owned, picked, 0.0)

    records = jnp.stack([sample(b1), sample(b2)], axis=0)[None]
    traces = records + lax.ppermute(records, "space", [(0, 1), (1, 0)])
    return (filtered, b2[None], traces)


def solution(mesh):
    in_specs = (
        P(("dom", "shot"), "space", None, None),
        P(("dom", "shot"), "space", None, None),
        P(("dom", "space"), None, None),
        P(("dom", "space"), None, "shot"),
        P(("dom", "shot"), None),
        P(("dom", "shot"), None),
        P(("dom", "shot")),
        P(("dom", "shot"), None),
        P("dom"),
    )
    out_specs = (
        P(("dom", "space"), None, "shot"),
        P(("dom", "shot"), "space", None, None),
        P(("dom", "shot"), None, None),
    )
    return jax.shard_map(body, mesh=mesh, in_specs=in_specs, out_specs=out_specs, check_vma=False)
```

```python
import math

import jax
import jax.numpy as jnp
from jax import lax
from jax.sharding import PartitionSpec as P

STEPS_A = 2
STEPS_B = 2


STENCIL = (-205.0 / 72.0, 8.0 / 5.0, -1.0 / 5.0, 8.0 / 315.0, -1.0 / 560.0)
damp_peak = 0.5
eps = 1e-05
HALO = 4


def coefficient(levels):
    speed = 1500.0 + 15.0 * levels.astype(jnp.float32)
    ratio = 0.45 * speed / 5325.0
    return ratio * ratio


def ramp(position, count, lower, upper):
    low_part = jnp.maximum(lower - position, 0.0) / lower
    high_part = jnp.maximum(upper - (count - 1.0 - position), 0.0) / upper
    return low_part * low_part + high_part * high_part


def damping(widths, positions, count_x, count_y, count_z):
    edges = widths.astype(jnp.float32)
    longest = max(positions.shape[0], count_y, count_z)
    line = jnp.arange(longest, dtype=jnp.float32)
    x_line = jnp.pad(positions, (0, longest - positions.shape[0]))
    place = jnp.stack([x_line, line, line])
    count = jnp.stack([jnp.asarray(count_x, jnp.float32), jnp.float32(count_y), jnp.float32(count_z)])[:, None]
    lower = jnp.stack([edges[0], edges[2], edges[4]])[:, None]
    upper = jnp.stack([edges[1], edges[3], edges[5]])[:, None]
    ramps = ramp(place, count, lower, upper)
    along_x = ramps[0, : positions.shape[0]]
    along_y = ramps[1, :count_y]
    along_z = ramps[2, :count_z]
    return damp_peak * (along_x[:, None, None] + along_y[None, :, None] + along_z[None, None, :])


def with_halo(x):
    size = lax.axis_size("space")
    length = x.shape[0]
    if size == 2:
        me = lax.axis_index("space")
        piece = lax.dynamic_slice_in_dim(x, (1 - me) * (length - HALO), HALO, 0)
        got = lax.ppermute(piece, "space", [(0, 1), (1, 0)])
        zeros = jnp.zeros((HALO,) + x.shape[1:], x.dtype)
        padded = jnp.concatenate([zeros, x, zeros], axis=0)
        return lax.dynamic_update_slice_in_dim(padded, got, (1 - me) * (length + HALO), 0)
    up = [(i, (i + 1) % size) for i in range(size - 1)]
    down = [(j, i) for i, j in up]
    before = lax.ppermute(x[length - HALO :], "space", up)
    after = lax.ppermute(x[:HALO], "space", down)
    return jnp.concatenate([before, x, after], axis=0)


def laplace_x(padded):
    width_x = padded.shape[0] - 8
    width_y = padded.shape[1]
    width_z = padded.shape[2]
    full = jnp.pad(padded, [(0, 0), (4, 4), (4, 4)])

    def part(move_x, move_y, move_z):
        return full[
            4 + move_x : 4 + move_x + width_x,
            4 + move_y : 4 + move_y + width_y,
            4 + move_z : 4 + move_z + width_z,
        ]

    total = 3.0 * STENCIL[0] * part(0, 0, 0)
    for reach in range(1, 5):
        beside_all = (
            part(reach, 0, 0)
            + part(-reach, 0, 0)
            + part(0, reach, 0)
            + part(0, -reach, 0)
            + part(0, 0, reach)
            + part(0, 0, -reach)
        )
        total = total + STENCIL[reach] * beside_all
    return total


def lateral_filter(field, table):
    count = field.shape[1]
    index = jnp.arange(count)
    phase = index[:, None] * index[None, :] % count
    angle = 2.0 * math.pi / count * phase.astype(jnp.float32)
    cosine = jnp.cos(angle)
    sine = jnp.sin(angle)
    real_part = jnp.einsum("xyz,yk->xzk", field, cosine, precision=lax.Precision.HIGHEST)
    imag_part = jnp.einsum("xyz,yk->xzk", field, sine, precision=lax.Precision.HIGHEST)
    weight = table[None, :, :]
    back = jnp.einsum("xzk,yk->xyz", real_part * weight, cosine, precision=lax.Precision.HIGHEST)
    back = back + jnp.einsum(
        "xzk,yk->xyz", imag_part * weight, sine, precision=lax.Precision.HIGHEST
    )
    return back / count


def shot_bits(n):
    bits = []
    k = 1
    while k < n:
        bits.append(k)
        k *= 2
    assert k == n
    return bits


def ag_step(held, k, done):
    n = lax.axis_size("shot")
    me = lax.axis_index("shot")
    theirs = lax.ppermute(held, "shot", [(i, i ^ k) for i in range(n)])
    low = 2 ** sum(1 for b in done if b < k)
    shape = (held.shape[0] // low, 1, low) + held.shape[1:]
    mine, other = held.reshape(shape), theirs.reshape(shape)
    first = (me // k) % 2 == 0
    pair = jnp.where(first, jnp.concatenate([mine, other], axis=1), jnp.concatenate([other, mine], axis=1))
    return pair.reshape((2 * held.shape[0],) + held.shape[1:])


def swap_first(order):
    return order[1:2] + order[:1] + order[2:]


def swap_last(order):
    return order[:-2] + order[-1:] + order[-2:-1] if len(order) > 1 else order


def chain(held, kind, order, bits=None):
    if bits is None:
        bits = [] if kind == "ag" else sorted(order)
    return {"held": held, "kind": kind, "order": list(order), "i": 0, "bits": list(bits)}


def split_step(held, k, left):
    me = lax.axis_index("shot")
    low = 2 ** left.index(k)
    high = held.shape[0] // (2 * low)
    split = held.reshape((high, 2, low) + held.shape[1:])
    mine = (me // k) % 2
    keep = lax.dynamic_index_in_dim(split, mine, axis=1, keepdims=False)
    send = lax.dynamic_index_in_dim(split, 1 - mine, axis=1, keepdims=False)
    shape = (high * low,) + held.shape[1:]
    return keep.reshape(shape), send.reshape(shape)


def chain_step(c):
    k = c["order"][c["i"]]
    if c["kind"] == "pre":
        n = lax.axis_size("shot")
        keep, send = c["slices"]()
        return keep + lax.ppermute(send, "shot", [(i, i ^ k) for i in range(n)])
    if c["kind"] == "ag":
        return ag_step(c["held"], k, c["bits"])
    return rs_step(c["held"], k, c["bits"])


def chain_commit(c, held):
    k = c["order"][c["i"]]
    c["held"] = held
    c["i"] += 1
    if c["kind"] == "ag":
        c["bits"].append(k)
    else:
        c["kind"] = "rs"
        c["bits"].remove(k)


def rs_step(held, k, left):
    n = lax.axis_size("shot")
    me = lax.axis_index("shot")
    low = 2 ** left.index(k)
    high = held.shape[0] // (2 * low)
    split = held.reshape((high, 2, low) + held.shape[1:])
    mine = (me // k) % 2
    keep = lax.dynamic_index_in_dim(split, mine, axis=1, keepdims=False)
    send = lax.dynamic_index_in_dim(split, 1 - mine, axis=1, keepdims=False)
    got = lax.ppermute(send, "shot", [(i, i ^ k) for i in range(n)])
    return (keep + got).reshape((high * low,) + held.shape[1:])


def body(
    wave_prev,
    wave_now,
    velocity_code,
    perturb,
    gains,
    wavelet,
    source_index,
    receiver_index,
    absorb_width,
):
    shots, span_x, span_y, span_z = wave_now.shape
    n_shot = lax.axis_size("shot")
    me_shot = lax.axis_index("shot")
    bits = shot_bits(n_shot)
    start_x = lax.axis_index("space") * span_x
    total_x = span_x * lax.axis_size("space")
    speed_term = coefficient(velocity_code)
    positions = start_x.astype(jnp.float32) + jnp.arange(span_x, dtype=jnp.float32)
    absorber = damping(absorb_width, positions, total_x, span_y, span_z)
    cells = span_x * span_y * span_z
    offset = start_x * span_y * span_z
    source_local = source_index - offset
    source_owned = (source_local >= 0) & (source_local < cells)
    source_safe = jnp.clip(source_local, 0, cells - 1)
    plane = span_y * span_z
    sx = source_safe[0] // plane
    sy = (source_safe[0] // span_z) % span_y
    sz = source_safe[0] % span_z
    source_code = lax.dynamic_slice(velocity_code, (sx, sy, sz), (1, 1, 1)).reshape(1)
    source_gain = jnp.where(source_owned, coefficient(source_code), 0.0)
    barrier = lax.optimization_barrier

    hit = (
        (jnp.arange(span_x)[:, None, None] == sx)
        & (jnp.arange(span_y)[None, :, None] == sy)
        & (jnp.arange(span_z)[None, None, :] == sz)
    )

    def inject(field, moment):
        return field + jnp.where(hit, source_gain[0] * wavelet[0, moment], 0.0)

    def wave_step(current, prior, moment, last):
        if moment == 0:
            inner = barrier(laplace_x(current))
            padded = with_halo(current)
            edge = 2 * HALO
            lap = jnp.concatenate(
                [laplace_x(padded[: edge + HALO]), inner, laplace_x(padded[padded.shape[0] - edge - HALO :])],
                axis=0,
            )
            drive = speed_term * lap
        else:
            drive = speed_term * laplace_x(with_halo(current))
        if last:
            return None, drive
        later = inject(2.0 * current - prior + drive - absorber * (current - prior), moment)
        return later, drive

    def born_second(born, field_model, drive):
        return (
            2.0 * born
            + speed_term * laplace_x(with_halo(born))
            - absorber * born
            + field_model * drive
        )

    slab = span_x // n_shot
    depth = perturb.shape[2]
    model_held = perturb.transpose(2, 0, 1).reshape(1, depth, span_x * span_y)
    gains_held = gains[None]
    st = {"w0": wave_now[0], "wp": wave_prev[0]}

    def task_wave(i):
        def run():
            last = i == 3
            cur, pri = (st["w0"], st["wp"]) if i == 0 else (st["w%d" % i], st["w%d" % (i - 1)])
            later, drive = wave_step(cur, pri, i, last)
            st["drive%d" % i] = drive
            if not last:
                st["w%d" % (i + 1)] = later
        return run

    def run_group(chains, compute):
        chains = [c for c in chains if c["i"] < len(c["order"])]
        moved = [chain_step(c) for c in chains]
        compute()
        keys = sorted(st.keys())
        out = barrier((moved, [st[n] for n in keys]))
        st.update(zip(keys, out[1]))
        for c, held in zip(chains, out[0]):
            chain_commit(c, held)

    def nothing():
        return None

    def light_prep():
        task_wave(1)()
        st["light"] = st["drive0"] * st["drive0"] + st["drive1"] * st["drive1"]

    def halves(x, axis):
        h = x.shape[axis] // 2
        return lax.slice_in_dim(x, 0, h, axis=axis), lax.slice_in_dim(x, h, x.shape[axis], axis=axis)

    far_first = list(reversed(bits))
    near_first = list(bits)

    top = far_first[0]
    model_c = chain(model_held, "ag", far_first[:1])
    gains_c = chain(gains_held, "ag", far_first)
    light_orders = {"la": near_first[:-1], "lb": swap_first(near_first[:-1])}

    def wave_and_split():
        task_wave(2)()
        pieces = halves(st["light"].reshape(n_shot, slab, span_y, span_z), 2)
        for (name, order), piece in zip(sorted(light_orders.items()), pieces):
            st[name + "_keep"], st[name + "_send"] = split_step(piece, order[0], list(near_first))

    tasks = [task_wave(0), light_prep, wave_and_split]
    run_group([model_c, gains_c], tasks[0])
    half_a, half_b = halves(model_c["held"], 2)
    model_a = chain(half_a, "ag", far_first[1:], [top])
    model_b = chain(half_b, "ag", swap_first(far_first[1:]), [top])
    for i in range(1, len(bits)):
        run_group([model_a, model_b, gains_c], tasks[i] if i < len(tasks) else nothing)
    for i in range(len(bits), len(tasks)):
        tasks[i]()
    model_lo, model_hi = model_a["held"], model_b["held"]
    gains_held = gains_c["held"]
    light_a = chain(None, "pre", light_orders["la"], near_first)
    light_b = chain(None, "pre", light_orders["lb"], near_first)
    light_a["slices"] = lambda: (st["la_keep"], st["la_send"])
    light_b["slices"] = lambda: (st["lb_keep"], st["lb_send"])

    def born_pass():
        model = jnp.concatenate(
            [m.reshape(span_z, m.shape[2]).T for m in (model_lo, model_hi)], axis=0
        ).reshape(span_x, span_y, span_z)
        st["born1"] = model * st["drive0"]
        st["born2"] = born_second(st["born1"], model, st["drive1"])

    run_group([light_a, light_b], born_pass)
    born1, born2 = st["born1"], st["born2"]

    image = st["drive0"] * born1 + st["drive1"] * born2
    image_a, image_b = halves(image.reshape(n_shot, slab, span_y, span_z), 2)
    image_a = chain(image_a, "rs", near_first[:-1], near_first)
    image_b = chain(image_b, "rs", swap_first(near_first[:-1]), near_first)
    tasks = [task_wave(3)]
    light_c = None
    for i in range(len(bits) - 1):
        group = [image_a, image_b]
        if light_a["i"] < len(light_a["order"]):
            group += [light_a, light_b]
        elif light_c is None:
            light_c = chain(
                jnp.concatenate([light_a["held"], light_b["held"]], axis=2), "rs", near_first[-1:], near_first[-1:]
            )
            group.append(light_c)
        run_group(group, tasks[i] if i < len(tasks) else nothing)
    for i in range(len(bits) - 1, len(tasks)):
        tasks[i]()
    if light_c is None:
        light_c = chain(
            jnp.concatenate([light_a["held"], light_b["held"]], axis=2), "rs", near_first[-1:], near_first[-1:]
        )
    last = chain(
        jnp.concatenate([image_a["held"], image_b["held"]], axis=2), "rs", near_first[-1:], near_first[-1:]
    )
    run_group([last, light_c], nothing)
    image_part = last["held"][0]
    light_part = light_c["held"][0]

    table_all = gains_held.reshape(n_shot * gains.shape[0], gains.shape[1])
    filt_part = lateral_filter(image_part / (light_part + eps), table_all)
    filt_c = chain(filt_part[None], "ag", far_first[:1])
    run_group([filt_c], nothing)
    part_a, part_b = halves(filt_c["held"], 2)
    filt_a = chain(part_a, "ag", far_first[1:], [top])
    filt_b = chain(part_b, "ag", swap_first(far_first[1:]), [top])
    for i in range(1, len(bits)):
        run_group([filt_a, filt_b], nothing)
    new_model = jnp.concatenate([filt_a["held"], filt_b["held"]], axis=2).reshape(span_x, span_y, span_z)
    filtered = lax.dynamic_slice_in_dim(new_model, me_shot * depth, depth, 2)

    b1 = new_model * st["drive2"]
    b2 = born_second(b1, new_model, st["drive3"])

    receiver_local = receiver_index[0] - offset
    receiver_owned = (receiver_local >= 0) & (receiver_local < cells)
    receiver_safe = jnp.clip(receiver_local, 0, cells - 1)
    row = receiver_safe // span_z
    rz = receiver_safe % span_z
    lane = jnp.arange(span_z)[None, :] == rz[:, None]

    def sample(field):
        rows = jnp.take(field.reshape(span_x * span_y, span_z), row, axis=0)
        picked = jnp.sum(jnp.where(lane, rows, 0.0), axis=1)
        return jnp.where(receiver_owned, picked, 0.0)

    records = jnp.stack([sample(b1), sample(b2)], axis=0)[None]
    traces = records + lax.ppermute(records, "space", [(0, 1), (1, 0)])
    return (filtered, b2[None], traces)


def solution(mesh):
    in_specs = (
        P(("dom", "shot"), "space", None, None),
        P(("dom", "shot"), "space", None, None),
        P(("dom", "space"), None, None),
        P(("dom", "space"), None, "shot"),
        P(("dom", "shot"), None),
        P(("dom", "shot"), None),
        P(("dom", "shot")),
        P(("dom", "shot"), None),
        P("dom"),
    )
    out_specs = (
        P(("dom", "space"), None, "shot"),
        P(("dom", "shot"), "space", None, None),
        P(("dom", "shot"), None, None),
    )
    return jax.shard_map(body, mesh=mesh, in_specs=in_specs, out_specs=out_specs, check_vma=False)
```

```python
import math

import jax
import jax.numpy as jnp
from jax import lax
from jax.sharding import PartitionSpec as P

STEPS_A = 2
STEPS_B = 2


STENCIL = (-205.0 / 72.0, 8.0 / 5.0, -1.0 / 5.0, 8.0 / 315.0, -1.0 / 560.0)
damp_peak = 0.5
eps = 1e-05
HALO = 4


def coefficient(levels):
    speed = 1500.0 + 15.0 * levels.astype(jnp.float32)
    ratio = 0.45 * speed / 5325.0
    return ratio * ratio


def ramp(position, count, lower, upper):
    low_part = jnp.maximum(lower - position, 0.0) / lower
    high_part = jnp.maximum(upper - (count - 1.0 - position), 0.0) / upper
    return low_part * low_part + high_part * high_part


def damping(widths, positions, count_x, count_y, count_z):
    edges = widths.astype(jnp.float32)
    longest = max(positions.shape[0], count_y, count_z)
    line = jnp.arange(longest, dtype=jnp.float32)
    x_line = jnp.pad(positions, (0, longest - positions.shape[0]))
    place = jnp.stack([x_line, line, line])
    count = jnp.stack([jnp.asarray(count_x, jnp.float32), jnp.float32(count_y), jnp.float32(count_z)])[:, None]
    lower = jnp.stack([edges[0], edges[2], edges[4]])[:, None]
    upper = jnp.stack([edges[1], edges[3], edges[5]])[:, None]
    ramps = ramp(place, count, lower, upper)
    along_x = ramps[0, : positions.shape[0]]
    along_y = ramps[1, :count_y]
    along_z = ramps[2, :count_z]
    return damp_peak * (along_x[:, None, None] + along_y[None, :, None] + along_z[None, None, :])


def with_halo(x):
    size = lax.axis_size("space")
    length = x.shape[0]
    if size == 2:
        me = lax.axis_index("space")
        piece = lax.dynamic_slice_in_dim(x, (1 - me) * (length - HALO), HALO, 0)
        got = lax.ppermute(piece, "space", [(0, 1), (1, 0)])
        zeros = jnp.zeros((HALO,) + x.shape[1:], x.dtype)
        padded = jnp.concatenate([zeros, x, zeros], axis=0)
        return lax.dynamic_update_slice_in_dim(padded, got, (1 - me) * (length + HALO), 0)
    up = [(i, (i + 1) % size) for i in range(size - 1)]
    down = [(j, i) for i, j in up]
    before = lax.ppermute(x[length - HALO :], "space", up)
    after = lax.ppermute(x[:HALO], "space", down)
    return jnp.concatenate([before, x, after], axis=0)


def laplace_x(padded):
    width_x = padded.shape[0] - 8
    width_y = padded.shape[1]
    width_z = padded.shape[2]
    full = jnp.pad(padded, [(0, 0), (4, 4), (4, 4)])

    def part(move_x, move_y, move_z):
        return full[
            4 + move_x : 4 + move_x + width_x,
            4 + move_y : 4 + move_y + width_y,
            4 + move_z : 4 + move_z + width_z,
        ]

    total = 3.0 * STENCIL[0] * part(0, 0, 0)
    for reach in range(1, 5):
        beside_all = (
            part(reach, 0, 0)
            + part(-reach, 0, 0)
            + part(0, reach, 0)
            + part(0, -reach, 0)
            + part(0, 0, reach)
            + part(0, 0, -reach)
        )
        total = total + STENCIL[reach] * beside_all
    return total


def lateral_filter(field, table):
    count = field.shape[1]
    index = jnp.arange(count)
    phase = index[:, None] * index[None, :] % count
    angle = 2.0 * math.pi / count * phase.astype(jnp.float32)
    cosine = jnp.cos(angle)
    sine = jnp.sin(angle)
    real_part = jnp.einsum("xyz,yk->xzk", field, cosine, precision=lax.Precision.HIGHEST)
    imag_part = jnp.einsum("xyz,yk->xzk", field, sine, precision=lax.Precision.HIGHEST)
    weight = table[None, :, :]
    back = jnp.einsum("xzk,yk->xyz", real_part * weight, cosine, precision=lax.Precision.HIGHEST)
    back = back + jnp.einsum(
        "xzk,yk->xyz", imag_part * weight, sine, precision=lax.Precision.HIGHEST
    )
    return back / count


def shot_bits(n):
    bits = []
    k = 1
    while k < n:
        bits.append(k)
        k *= 2
    assert k == n
    return bits


def ag_step(held, k, done):
    n = lax.axis_size("shot")
    me = lax.axis_index("shot")
    theirs = lax.ppermute(held, "shot", [(i, i ^ k) for i in range(n)])
    low = 2 ** sum(1 for b in done if b < k)
    shape = (held.shape[0] // low, 1, low) + held.shape[1:]
    mine, other = held.reshape(shape), theirs.reshape(shape)
    at = (me // k) % 2
    pair = jnp.zeros((shape[0], 2) + shape[2:], held.dtype)
    pair = lax.dynamic_update_slice_in_dim(pair, mine, at, axis=1)
    pair = lax.dynamic_update_slice_in_dim(pair, other, 1 - at, axis=1)
    return pair.reshape((2 * held.shape[0],) + held.shape[1:])


def swap_first(order):
    return order[1:2] + order[:1] + order[2:]


def swap_last(order):
    return order[:-2] + order[-1:] + order[-2:-1] if len(order) > 1 else order


def chain(held, kind, order, bits=None):
    if bits is None:
        bits = [] if kind == "ag" else sorted(order)
    return {"held": held, "kind": kind, "order": list(order), "i": 0, "bits": list(bits)}


def split_step(held, k, left):
    me = lax.axis_index("shot")
    low = 2 ** left.index(k)
    high = held.shape[0] // (2 * low)
    split = held.reshape((high, 2, low) + held.shape[1:])
    mine = (me // k) % 2
    keep = lax.dynamic_index_in_dim(split, mine, axis=1, keepdims=False)
    send = lax.dynamic_index_in_dim(split, 1 - mine, axis=1, keepdims=False)
    shape = (high * low,) + held.shape[1:]
    return keep.reshape(shape), send.reshape(shape)


def chain_step(c):
    k = c["order"][c["i"]]
    if c["kind"] == "pre":
        n = lax.axis_size("shot")
        keep, send = c["slices"]()
        return keep + lax.ppermute(send, "shot", [(i, i ^ k) for i in range(n)])
    if c["kind"] == "ag":
        return ag_step(c["held"], k, c["bits"])
    return rs_step(c["held"], k, c["bits"])


def chain_commit(c, held):
    k = c["order"][c["i"]]
    c["held"] = held
    c["i"] += 1
    if c["kind"] == "ag":
        c["bits"].append(k)
    else:
        c["kind"] = "rs"
        c["bits"].remove(k)


def rs_step(held, k, left):
    n = lax.axis_size("shot")
    me = lax.axis_index("shot")
    low = 2 ** left.index(k)
    high = held.shape[0] // (2 * low)
    split = held.reshape((high, 2, low) + held.shape[1:])
    mine = (me // k) % 2
    keep = lax.dynamic_index_in_dim(split, mine, axis=1, keepdims=False)
    send = lax.dynamic_index_in_dim(split, 1 - mine, axis=1, keepdims=False)
    got = lax.ppermute(send, "shot", [(i, i ^ k) for i in range(n)])
    return (keep + got).reshape((high * low,) + held.shape[1:])


def body(
    wave_prev,
    wave_now,
    velocity_code,
    perturb,
    gains,
    wavelet,
    source_index,
    receiver_index,
    absorb_width,
):
    shots, span_x, span_y, span_z = wave_now.shape
    n_shot = lax.axis_size("shot")
    me_shot = lax.axis_index("shot")
    bits = shot_bits(n_shot)
    start_x = lax.axis_index("space") * span_x
    total_x = span_x * lax.axis_size("space")
    speed_term = coefficient(velocity_code)
    positions = start_x.astype(jnp.float32) + jnp.arange(span_x, dtype=jnp.float32)
    absorber = damping(absorb_width, positions, total_x, span_y, span_z)
    cells = span_x * span_y * span_z
    offset = start_x * span_y * span_z
    source_local = source_index - offset
    source_owned = (source_local >= 0) & (source_local < cells)
    source_safe = jnp.clip(source_local, 0, cells - 1)
    plane = span_y * span_z
    sx = source_safe[0] // plane
    sy = (source_safe[0] // span_z) % span_y
    sz = source_safe[0] % span_z
    source_code = lax.dynamic_slice(velocity_code, (sx, sy, sz), (1, 1, 1)).reshape(1)
    source_gain = jnp.where(source_owned, coefficient(source_code), 0.0)
    barrier = lax.optimization_barrier

    hit = (
        (jnp.arange(span_x)[:, None, None] == sx)
        & (jnp.arange(span_y)[None, :, None] == sy)
        & (jnp.arange(span_z)[None, None, :] == sz)
    )

    def inject(field, moment):
        return field + jnp.where(hit, source_gain[0] * wavelet[0, moment], 0.0)

    def wave_step(current, prior, moment, last):
        if moment == 0:
            inner = barrier(laplace_x(current))
            padded = with_halo(current)
            edge = 2 * HALO
            lap = jnp.concatenate(
                [laplace_x(padded[: edge + HALO]), inner, laplace_x(padded[padded.shape[0] - edge - HALO :])],
                axis=0,
            )
            drive = speed_term * lap
        else:
            drive = speed_term * laplace_x(with_halo(current))
        if last:
            return None, drive
        later = inject(2.0 * current - prior + drive - absorber * (current - prior), moment)
        return later, drive

    def born_second(born, field_model, drive):
        return (
            2.0 * born
            + speed_term * laplace_x(with_halo(born))
            - absorber * born
            + field_model * drive
        )

    slab = span_x // n_shot
    depth = perturb.shape[2]
    model_held = perturb.transpose(2, 0, 1).reshape(1, depth, span_x * span_y)
    gains_held = gains[None]
    st = {"w0": wave_now[0], "wp": wave_prev[0]}

    def task_wave(i):
        def run():
            last = i == 3
            cur, pri = (st["w0"], st["wp"]) if i == 0 else (st["w%d" % i], st["w%d" % (i - 1)])
            later, drive = wave_step(cur, pri, i, last)
            st["drive%d" % i] = drive
            if not last:
                st["w%d" % (i + 1)] = later
        return run

    def run_group(chains, compute):
        chains = [c for c in chains if c["i"] < len(c["order"])]
        moved = [chain_step(c) for c in chains]
        compute()
        keys = sorted(st.keys())
        out = barrier((moved, [st[n] for n in keys]))
        st.update(zip(keys, out[1]))
        for c, held in zip(chains, out[0]):
            chain_commit(c, held)

    def nothing():
        return None

    def light_prep():
        task_wave(1)()
        st["light"] = st["drive0"] * st["drive0"] + st["drive1"] * st["drive1"]

    def halves(x, axis):
        h = x.shape[axis] // 2
        return lax.slice_in_dim(x, 0, h, axis=axis), lax.slice_in_dim(x, h, x.shape[axis], axis=axis)

    far_first = list(reversed(bits))
    near_first = list(bits)

    top = far_first[0]
    model_c = chain(model_held, "ag", far_first[:1])
    gains_c = chain(gains_held, "ag", far_first)
    light_orders = {"la": near_first[:-1], "lb": swap_first(near_first[:-1])}

    def wave_and_split():
        task_wave(2)()
        pieces = halves(st["light"].reshape(n_shot, slab, span_y, span_z), 2)
        for (name, order), piece in zip(sorted(light_orders.items()), pieces):
            st[name + "_keep"], st[name + "_send"] = split_step(piece, order[0], list(near_first))

    tasks = [task_wave(0), light_prep, wave_and_split]
    run_group([model_c, gains_c], tasks[0])
    half_a, half_b = halves(model_c["held"], 1)
    model_a = chain(half_a, "ag", far_first[1:], [top])
    model_b = chain(half_b, "ag", swap_first(far_first[1:]), [top])
    for i in range(1, len(bits)):
        run_group([model_a, model_b, gains_c], tasks[i] if i < len(tasks) else nothing)
    for i in range(len(bits), len(tasks)):
        tasks[i]()
    model_held = jnp.concatenate([model_a["held"], model_b["held"]], axis=1)
    gains_held = gains_c["held"]
    light_a = chain(None, "pre", light_orders["la"], near_first)
    light_b = chain(None, "pre", light_orders["lb"], near_first)
    light_a["slices"] = lambda: (st["la_keep"], st["la_send"])
    light_b["slices"] = lambda: (st["lb_keep"], st["lb_send"])

    def born_pass():
        model = model_held.reshape(span_z, span_x * span_y).T.reshape(span_x, span_y, span_z)
        st["born1"] = model * st["drive0"]
        st["born2"] = born_second(st["born1"], model, st["drive1"])

    run_group([light_a, light_b], born_pass)
    born1, born2 = st["born1"], st["born2"]

    image = st["drive0"] * born1 + st["drive1"] * born2
    image_a, image_b = halves(image.reshape(n_shot, slab, span_y, span_z), 2)
    image_a = chain(image_a, "rs", near_first[:-1], near_first)
    image_b = chain(image_b, "rs", swap_first(near_first[:-1]), near_first)
    tasks = [task_wave(3)]
    light_c = None
    for i in range(len(bits) - 1):
        group = [image_a, image_b]
        if light_a["i"] < len(light_a["order"]):
            group += [light_a, light_b]
        elif light_c is None:
            light_c = chain(
                jnp.concatenate([light_a["held"], light_b["held"]], axis=2), "rs", near_first[-1:], near_first[-1:]
            )
            group.append(light_c)
        run_group(group, tasks[i] if i < len(tasks) else nothing)
    for i in range(len(bits) - 1, len(tasks)):
        tasks[i]()
    if light_c is None:
        light_c = chain(
            jnp.concatenate([light_a["held"], light_b["held"]], axis=2), "rs", near_first[-1:], near_first[-1:]
        )
    last = chain(
        jnp.concatenate([image_a["held"], image_b["held"]], axis=2), "rs", near_first[-1:], near_first[-1:]
    )
    run_group([last, light_c], nothing)
    image_part = last["held"][0]
    light_part = light_c["held"][0]

    table_all = gains_held.reshape(n_shot * gains.shape[0], gains.shape[1])
    filt_part = lateral_filter(image_part / (light_part + eps), table_all)
    filt_c = chain(filt_part[None], "ag", far_first[:1])
    run_group([filt_c], nothing)
    part_a, part_b = halves(filt_c["held"], 2)
    filt_a = chain(part_a, "ag", far_first[1:], [top])
    filt_b = chain(part_b, "ag", swap_first(far_first[1:]), [top])
    for i in range(1, len(bits)):
        run_group([filt_a, filt_b], nothing)
    new_model = jnp.concatenate([filt_a["held"], filt_b["held"]], axis=2).reshape(span_x, span_y, span_z)
    filtered = lax.dynamic_slice_in_dim(new_model, me_shot * depth, depth, 2)

    b1 = new_model * st["drive2"]
    b2 = born_second(b1, new_model, st["drive3"])

    receiver_local = receiver_index[0] - offset
    receiver_owned = (receiver_local >= 0) & (receiver_local < cells)
    receiver_safe = jnp.clip(receiver_local, 0, cells - 1)
    row = receiver_safe // span_z
    rz = receiver_safe % span_z
    lane = jnp.arange(span_z)[None, :] == rz[:, None]

    def sample(field):
        rows = jnp.take(field.reshape(span_x * span_y, span_z), row, axis=0)
        picked = jnp.sum(jnp.where(lane, rows, 0.0), axis=1)
        return jnp.where(receiver_owned, picked, 0.0)

    records = jnp.stack([sample(b1), sample(b2)], axis=0)[None]
    traces = records + lax.ppermute(records, "space", [(0, 1), (1, 0)])
    return (filtered, b2[None], traces)


def solution(mesh):
    in_specs = (
        P(("dom", "shot"), "space", None, None),
        P(("dom", "shot"), "space", None, None),
        P(("dom", "space"), None, None),
        P(("dom", "space"), None, "shot"),
        P(("dom", "shot"), None),
        P(("dom", "shot"), None),
        P(("dom", "shot")),
        P(("dom", "shot"), None),
        P("dom"),
    )
    out_specs = (
        P(("dom", "space"), None, "shot"),
        P(("dom", "shot"), "space", None, None),
        P(("dom", "shot"), None, None),
    )
    return jax.shard_map(body, mesh=mesh, in_specs=in_specs, out_specs=out_specs, check_vma=False)
```

```python
import math

import jax
import jax.numpy as jnp
from jax import lax
from jax.sharding import PartitionSpec as P

STEPS_A = 2
STEPS_B = 2


STENCIL = (-205.0 / 72.0, 8.0 / 5.0, -1.0 / 5.0, 8.0 / 315.0, -1.0 / 560.0)
damp_peak = 0.5
eps = 1e-05
HALO = 4


def coefficient(levels):
    speed = 1500.0 + 15.0 * levels.astype(jnp.float32)
    ratio = 0.45 * speed / 5325.0
    return ratio * ratio


def ramp(position, count, lower, upper):
    low_part = jnp.maximum(lower - position, 0.0) / lower
    high_part = jnp.maximum(upper - (count - 1.0 - position), 0.0) / upper
    return low_part * low_part + high_part * high_part


def damping(widths, positions, count_x, count_y, count_z):
    edges = widths.astype(jnp.float32)
    longest = max(positions.shape[0], count_y, count_z)
    line = jnp.arange(longest, dtype=jnp.float32)
    x_line = jnp.pad(positions, (0, longest - positions.shape[0]))
    place = jnp.stack([x_line, line, line])
    count = jnp.stack([jnp.asarray(count_x, jnp.float32), jnp.float32(count_y), jnp.float32(count_z)])[:, None]
    lower = jnp.stack([edges[0], edges[2], edges[4]])[:, None]
    upper = jnp.stack([edges[1], edges[3], edges[5]])[:, None]
    ramps = ramp(place, count, lower, upper)
    along_x = ramps[0, : positions.shape[0]]
    along_y = ramps[1, :count_y]
    along_z = ramps[2, :count_z]
    return damp_peak * (along_x[:, None, None] + along_y[None, :, None] + along_z[None, None, :])


def with_halo(x):
    size = lax.axis_size("space")
    length = x.shape[0]
    if size == 2:
        me = lax.axis_index("space")
        piece = lax.dynamic_slice_in_dim(x, (1 - me) * (length - HALO), HALO, 0)
        got = lax.ppermute(piece, "space", [(0, 1), (1, 0)])
        zeros = jnp.zeros((HALO,) + x.shape[1:], x.dtype)
        padded = jnp.concatenate([zeros, x, zeros], axis=0)
        return lax.dynamic_update_slice_in_dim(padded, got, (1 - me) * (length + HALO), 0)
    up = [(i, (i + 1) % size) for i in range(size - 1)]
    down = [(j, i) for i, j in up]
    before = lax.ppermute(x[length - HALO :], "space", up)
    after = lax.ppermute(x[:HALO], "space", down)
    return jnp.concatenate([before, x, after], axis=0)


def laplace_x(padded):
    width_x = padded.shape[0] - 8
    width_y = padded.shape[1]
    width_z = padded.shape[2]
    full = jnp.pad(padded, [(0, 0), (4, 4), (4, 4)])

    def part(move_x, move_y, move_z):
        return full[
            4 + move_x : 4 + move_x + width_x,
            4 + move_y : 4 + move_y + width_y,
            4 + move_z : 4 + move_z + width_z,
        ]

    total = 3.0 * STENCIL[0] * part(0, 0, 0)
    for reach in range(1, 5):
        beside_all = (
            part(reach, 0, 0)
            + part(-reach, 0, 0)
            + part(0, reach, 0)
            + part(0, -reach, 0)
            + part(0, 0, reach)
            + part(0, 0, -reach)
        )
        total = total + STENCIL[reach] * beside_all
    return total


def lateral_filter(field, table):
    count = field.shape[1]
    index = jnp.arange(count)
    phase = index[:, None] * index[None, :] % count
    angle = 2.0 * math.pi / count * phase.astype(jnp.float32)
    cosine = jnp.cos(angle)
    sine = jnp.sin(angle)
    real_part = jnp.einsum("xyz,yk->xzk", field, cosine, precision=lax.Precision.HIGHEST)
    imag_part = jnp.einsum("xyz,yk->xzk", field, sine, precision=lax.Precision.HIGHEST)
    weight = table[None, :, :]
    back = jnp.einsum("xzk,yk->xyz", real_part * weight, cosine, precision=lax.Precision.HIGHEST)
    back = back + jnp.einsum(
        "xzk,yk->xyz", imag_part * weight, sine, precision=lax.Precision.HIGHEST
    )
    return back / count


def shot_bits(n):
    bits = []
    k = 1
    while k < n:
        bits.append(k)
        k *= 2
    assert k == n
    return bits


def ag_step(held, k, done):
    n = lax.axis_size("shot")
    me = lax.axis_index("shot")
    theirs = lax.ppermute(held, "shot", [(i, i ^ k) for i in range(n)])
    low = 2 ** sum(1 for b in done if b < k)
    shape = (held.shape[0] // low, 1, low) + held.shape[1:]
    mine, other = held.reshape(shape), theirs.reshape(shape)
    first = (me // k) % 2 == 0
    pair = jnp.where(first, jnp.concatenate([mine, other], axis=1), jnp.concatenate([other, mine], axis=1))
    return pair.reshape((2 * held.shape[0],) + held.shape[1:])


def swap_first(order):
    return order[1:2] + order[:1] + order[2:]


def swap_last(order):
    return order[:-2] + order[-1:] + order[-2:-1] if len(order) > 1 else order


def chain(held, kind, order, bits=None):
    if bits is None:
        bits = [] if kind == "ag" else sorted(order)
    return {"held": held, "kind": kind, "order": list(order), "i": 0, "bits": list(bits)}


def split_step(held, k, left):
    me = lax.axis_index("shot")
    low = 2 ** left.index(k)
    high = held.shape[0] // (2 * low)
    split = held.reshape((high, 2, low) + held.shape[1:])
    mine = (me // k) % 2
    keep = lax.dynamic_index_in_dim(split, mine, axis=1, keepdims=False)
    send = lax.dynamic_index_in_dim(split, 1 - mine, axis=1, keepdims=False)
    shape = (high * low,) + held.shape[1:]
    return keep.reshape(shape), send.reshape(shape)


def chain_step(c):
    k = c["order"][c["i"]]
    if c["kind"] == "pre":
        n = lax.axis_size("shot")
        keep, send = c["slices"]()
        return keep + lax.ppermute(send, "shot", [(i, i ^ k) for i in range(n)])
    if c["kind"] == "ag":
        return ag_step(c["held"], k, c["bits"])
    return rs_step(c["held"], k, c["bits"])


def chain_commit(c, held):
    k = c["order"][c["i"]]
    c["held"] = held
    c["i"] += 1
    if c["kind"] == "ag":
        c["bits"].append(k)
    else:
        c["kind"] = "rs"
        c["bits"].remove(k)


def rs_step(held, k, left):
    n = lax.axis_size("shot")
    me = lax.axis_index("shot")
    low = 2 ** left.index(k)
    high = held.shape[0] // (2 * low)
    split = held.reshape((high, 2, low) + held.shape[1:])
    mine = (me // k) % 2
    keep = lax.dynamic_index_in_dim(split, mine, axis=1, keepdims=False)
    send = lax.dynamic_index_in_dim(split, 1 - mine, axis=1, keepdims=False)
    got = lax.ppermute(send, "shot", [(i, i ^ k) for i in range(n)])
    return (keep + got).reshape((high * low,) + held.shape[1:])


def body(
    wave_prev,
    wave_now,
    velocity_code,
    perturb,
    gains,
    wavelet,
    source_index,
    receiver_index,
    absorb_width,
):
    shots, span_x, span_y, span_z = wave_now.shape
    n_shot = lax.axis_size("shot")
    me_shot = lax.axis_index("shot")
    bits = shot_bits(n_shot)
    start_x = lax.axis_index("space") * span_x
    total_x = span_x * lax.axis_size("space")
    speed_term = coefficient(velocity_code)
    positions = start_x.astype(jnp.float32) + jnp.arange(span_x, dtype=jnp.float32)
    absorber = damping(absorb_width, positions, total_x, span_y, span_z)
    cells = span_x * span_y * span_z
    offset = start_x * span_y * span_z
    source_local = source_index - offset
    source_owned = (source_local >= 0) & (source_local < cells)
    source_safe = jnp.clip(source_local, 0, cells - 1)
    plane = span_y * span_z
    sx = source_safe[0] // plane
    sy = (source_safe[0] // span_z) % span_y
    sz = source_safe[0] % span_z
    source_code = lax.dynamic_slice(velocity_code, (sx, sy, sz), (1, 1, 1)).reshape(1)
    source_gain = jnp.where(source_owned, coefficient(source_code), 0.0)
    barrier = lax.optimization_barrier

    hit = (
        (jnp.arange(span_x)[:, None, None] == sx)
        & (jnp.arange(span_y)[None, :, None] == sy)
        & (jnp.arange(span_z)[None, None, :] == sz)
    )

    def inject(field, moment):
        return field + jnp.where(hit, source_gain[0] * wavelet[0, moment], 0.0)

    def wave_step(current, prior, moment, last):
        if moment == 0:
            inner = barrier(laplace_x(current))
            padded = with_halo(current)
            edge = 2 * HALO
            lap = jnp.concatenate(
                [laplace_x(padded[: edge + HALO]), inner, laplace_x(padded[padded.shape[0] - edge - HALO :])],
                axis=0,
            )
            drive = speed_term * lap
        else:
            drive = speed_term * laplace_x(with_halo(current))
        if last:
            return None, drive
        later = inject(2.0 * current - prior + drive - absorber * (current - prior), moment)
        return later, drive

    def born_second(born, field_model, drive):
        return (
            2.0 * born
            + speed_term * laplace_x(with_halo(born))
            - absorber * born
            + field_model * drive
        )

    slab = span_x // n_shot
    depth = perturb.shape[2]
    model_held = perturb.transpose(2, 0, 1).reshape(1, depth, span_x * span_y)
    gains_held = gains[None]
    st = {"w0": wave_now[0], "wp": wave_prev[0]}

    def task_wave(i):
        def run():
            last = i == 3
            cur, pri = (st["w0"], st["wp"]) if i == 0 else (st["w%d" % i], st["w%d" % (i - 1)])
            later, drive = wave_step(cur, pri, i, last)
            st["drive%d" % i] = drive
            if not last:
                st["w%d" % (i + 1)] = later
        return run

    def run_group(chains, compute):
        chains = [c for c in chains if c["i"] < len(c["order"])]
        moved = [chain_step(c) for c in chains]
        compute()
        keys = sorted(st.keys())
        out = barrier((moved, [st[n] for n in keys]))
        st.update(zip(keys, out[1]))
        for c, held in zip(chains, out[0]):
            chain_commit(c, held)

    def nothing():
        return None

    def light_prep():
        task_wave(1)()
        st["light"] = st["drive0"] * st["drive0"] + st["drive1"] * st["drive1"]

    def halves(x, axis):
        h = x.shape[axis] // 2
        return lax.slice_in_dim(x, 0, h, axis=axis), lax.slice_in_dim(x, h, x.shape[axis], axis=axis)

    far_first = list(reversed(bits))
    near_first = list(bits)

    top = far_first[0]
    model_c = chain(model_held, "ag", far_first[:1])
    gains_c = chain(gains_held, "ag", far_first)
    light_orders = {"la": near_first[:-1], "lb": swap_first(near_first[:-1])}

    def wave_and_split():
        task_wave(2)()
        pieces = halves(st["light"].reshape(n_shot, slab, span_y, span_z), 2)
        for (name, order), piece in zip(sorted(light_orders.items()), pieces):
            st[name + "_keep"], st[name + "_send"] = split_step(piece, order[0], list(near_first))

    tasks = [task_wave(0), light_prep, wave_and_split]
    run_group([model_c, gains_c], tasks[0])
    half_a, half_b = halves(model_c["held"], 1)
    model_a = chain(half_a, "ag", far_first[1:], [top])
    model_b = chain(half_b, "ag", swap_first(far_first[1:]), [top])
    for i in range(1, len(bits)):
        run_group([model_a, model_b, gains_c], tasks[i] if i < len(tasks) else nothing)
    for i in range(len(bits), len(tasks)):
        tasks[i]()
    model_held = jnp.concatenate([model_a["held"], model_b["held"]], axis=1)
    gains_held = gains_c["held"]
    light_a = chain(None, "pre", light_orders["la"], near_first)
    light_b = chain(None, "pre", light_orders["lb"], near_first)
    light_a["slices"] = lambda: (st["la_keep"], st["la_send"])
    light_b["slices"] = lambda: (st["lb_keep"], st["lb_send"])

    def born_first():
        model = model_held.reshape(span_z, span_x * span_y).T.reshape(span_x, span_y, span_z)
        st["model"] = model
        st["born1"] = model * st["drive0"]

    def born_next():
        st["born2"] = born_second(st["born1"], st["model"], st["drive1"])

    run_group([light_a, light_b], born_first)
    run_group([light_a, light_b], born_next)
    born1, born2 = st["born1"], st["born2"]

    image = st["drive0"] * born1 + st["drive1"] * born2
    image_a, image_b = halves(image.reshape(n_shot, slab, span_y, span_z), 2)
    image_a = chain(image_a, "rs", near_first[:-1], near_first)
    image_b = chain(image_b, "rs", swap_first(near_first[:-1]), near_first)
    tasks = [task_wave(3)]
    light_c = None
    for i in range(len(bits) - 1):
        group = [image_a, image_b]
        if light_a["i"] < len(light_a["order"]):
            group += [light_a, light_b]
        elif light_c is None:
            light_c = chain(
                jnp.concatenate([light_a["held"], light_b["held"]], axis=2), "rs", near_first[-1:], near_first[-1:]
            )
            group.append(light_c)
        run_group(group, tasks[i] if i < len(tasks) else nothing)
    for i in range(len(bits) - 1, len(tasks)):
        tasks[i]()
    if light_c is None:
        light_c = chain(
            jnp.concatenate([light_a["held"], light_b["held"]], axis=2), "rs", near_first[-1:], near_first[-1:]
        )
    last = chain(
        jnp.concatenate([image_a["held"], image_b["held"]], axis=2), "rs", near_first[-1:], near_first[-1:]
    )
    run_group([last, light_c], nothing)
    image_part = last["held"][0]
    light_part = light_c["held"][0]

    table_all = gains_held.reshape(n_shot * gains.shape[0], gains.shape[1])
    filt_part = lateral_filter(image_part / (light_part + eps), table_all)
    filt_c = chain(filt_part[None], "ag", far_first[:1])
    run_group([filt_c], nothing)
    part_a, part_b = halves(filt_c["held"], 2)
    filt_a = chain(part_a, "ag", far_first[1:], [top])
    filt_b = chain(part_b, "ag", swap_first(far_first[1:]), [top])
    for i in range(1, len(bits)):
        run_group([filt_a, filt_b], nothing)
    new_model = jnp.concatenate([filt_a["held"], filt_b["held"]], axis=2).reshape(span_x, span_y, span_z)
    filtered = lax.dynamic_slice_in_dim(new_model, me_shot * depth, depth, 2)

    b1 = new_model * st["drive2"]
    b2 = born_second(b1, new_model, st["drive3"])

    receiver_local = receiver_index[0] - offset
    receiver_owned = (receiver_local >= 0) & (receiver_local < cells)
    receiver_safe = jnp.clip(receiver_local, 0, cells - 1)
    row = receiver_safe // span_z
    rz = receiver_safe % span_z
    lane = jnp.arange(span_z)[None, :] == rz[:, None]

    def sample(field):
        rows = jnp.take(field.reshape(span_x * span_y, span_z), row, axis=0)
        picked = jnp.sum(jnp.where(lane, rows, 0.0), axis=1)
        return jnp.where(receiver_owned, picked, 0.0)

    records = jnp.stack([sample(b1), sample(b2)], axis=0)[None]
    traces = records + lax.ppermute(records, "space", [(0, 1), (1, 0)])
    return (filtered, b2[None], traces)


def solution(mesh):
    in_specs = (
        P(("dom", "shot"), "space", None, None),
        P(("dom", "shot"), "space", None, None),
        P(("dom", "space"), None, None),
        P(("dom", "space"), None, "shot"),
        P(("dom", "shot"), None),
        P(("dom", "shot"), None),
        P(("dom", "shot")),
        P(("dom", "shot"), None),
        P("dom"),
    )
    out_specs = (
        P(("dom", "space"), None, "shot"),
        P(("dom", "shot"), "space", None, None),
        P(("dom", "shot"), None, None),
    )
    return jax.shard_map(body, mesh=mesh, in_specs=in_specs, out_specs=out_specs, check_vma=False)
```

```python
import math

import jax
import jax.numpy as jnp
from jax import lax
from jax.sharding import PartitionSpec as P

STEPS_A = 2
STEPS_B = 2


STENCIL = (-205.0 / 72.0, 8.0 / 5.0, -1.0 / 5.0, 8.0 / 315.0, -1.0 / 560.0)
damp_peak = 0.5
eps = 1e-05
HALO = 4


def coefficient(levels):
    speed = 1500.0 + 15.0 * levels.astype(jnp.float32)
    ratio = 0.45 * speed / 5325.0
    return ratio * ratio


def ramp(position, count, lower, upper):
    low_part = jnp.maximum(lower - position, 0.0) / lower
    high_part = jnp.maximum(upper - (count - 1.0 - position), 0.0) / upper
    return low_part * low_part + high_part * high_part


def damping(widths, positions, count_x, count_y, count_z):
    edges = widths.astype(jnp.float32)
    longest = max(positions.shape[0], count_y, count_z)
    line = jnp.arange(longest, dtype=jnp.float32)
    x_line = jnp.pad(positions, (0, longest - positions.shape[0]))
    place = jnp.stack([x_line, line, line])
    count = jnp.stack([jnp.asarray(count_x, jnp.float32), jnp.float32(count_y), jnp.float32(count_z)])[:, None]
    lower = jnp.stack([edges[0], edges[2], edges[4]])[:, None]
    upper = jnp.stack([edges[1], edges[3], edges[5]])[:, None]
    ramps = ramp(place, count, lower, upper)
    along_x = ramps[0, : positions.shape[0]]
    along_y = ramps[1, :count_y]
    along_z = ramps[2, :count_z]
    return damp_peak * (along_x[:, None, None] + along_y[None, :, None] + along_z[None, None, :])


def with_halo(x):
    size = lax.axis_size("space")
    length = x.shape[0]
    if size == 2:
        me = lax.axis_index("space")
        piece = lax.dynamic_slice_in_dim(x, (1 - me) * (length - HALO), HALO, 0)
        got = lax.ppermute(piece, "space", [(0, 1), (1, 0)])
        zeros = jnp.zeros((HALO,) + x.shape[1:], x.dtype)
        padded = jnp.concatenate([zeros, x, zeros], axis=0)
        return lax.dynamic_update_slice_in_dim(padded, got, (1 - me) * (length + HALO), 0)
    up = [(i, (i + 1) % size) for i in range(size - 1)]
    down = [(j, i) for i, j in up]
    before = lax.ppermute(x[length - HALO :], "space", up)
    after = lax.ppermute(x[:HALO], "space", down)
    return jnp.concatenate([before, x, after], axis=0)


def laplace_x(padded):
    width_x = padded.shape[0] - 8
    width_y = padded.shape[1]
    width_z = padded.shape[2]
    full = jnp.pad(padded, [(0, 0), (4, 4), (4, 4)])

    def part(move_x, move_y, move_z):
        return full[
            4 + move_x : 4 + move_x + width_x,
            4 + move_y : 4 + move_y + width_y,
            4 + move_z : 4 + move_z + width_z,
        ]

    total = 3.0 * STENCIL[0] * part(0, 0, 0)
    for reach in range(1, 5):
        beside_all = (
            part(reach, 0, 0)
            + part(-reach, 0, 0)
            + part(0, reach, 0)
            + part(0, -reach, 0)
            + part(0, 0, reach)
            + part(0, 0, -reach)
        )
        total = total + STENCIL[reach] * beside_all
    return total


def lateral_filter(field, table):
    count = field.shape[1]
    index = jnp.arange(count)
    phase = index[:, None] * index[None, :] % count
    angle = 2.0 * math.pi / count * phase.astype(jnp.float32)
    cosine = jnp.cos(angle)
    sine = jnp.sin(angle)
    real_part = jnp.einsum("xyz,yk->xzk", field, cosine, precision=lax.Precision.HIGHEST)
    imag_part = jnp.einsum("xyz,yk->xzk", field, sine, precision=lax.Precision.HIGHEST)
    weight = table[None, :, :]
    back = jnp.einsum("xzk,yk->xyz", real_part * weight, cosine, precision=lax.Precision.HIGHEST)
    back = back + jnp.einsum(
        "xzk,yk->xyz", imag_part * weight, sine, precision=lax.Precision.HIGHEST
    )
    return back / count


def shot_bits(n):
    bits = []
    k = 1
    while k < n:
        bits.append(k)
        k *= 2
    assert k == n
    return bits


def ag_step(held, k, done):
    n = lax.axis_size("shot")
    me = lax.axis_index("shot")
    theirs = lax.ppermute(held, "shot", [(i, i ^ k) for i in range(n)])
    low = 2 ** sum(1 for b in done if b < k)
    shape = (held.shape[0] // low, 1, low) + held.shape[1:]
    mine, other = held.reshape(shape), theirs.reshape(shape)
    first = (me // k) % 2 == 0
    pair = jnp.where(first, jnp.concatenate([mine, other], axis=1), jnp.concatenate([other, mine], axis=1))
    return pair.reshape((2 * held.shape[0],) + held.shape[1:])


def swap_first(order):
    return order[1:2] + order[:1] + order[2:]


def swap_last(order):
    return order[:-2] + order[-1:] + order[-2:-1] if len(order) > 1 else order


def chain(held, kind, order, bits=None):
    if bits is None:
        bits = [] if kind == "ag" else sorted(order)
    return {"held": held, "kind": kind, "order": list(order), "i": 0, "bits": list(bits)}


def split_step(held, k, left):
    me = lax.axis_index("shot")
    low = 2 ** left.index(k)
    high = held.shape[0] // (2 * low)
    split = held.reshape((high, 2, low) + held.shape[1:])
    mine = (me // k) % 2
    keep = lax.dynamic_index_in_dim(split, mine, axis=1, keepdims=False)
    send = lax.dynamic_index_in_dim(split, 1 - mine, axis=1, keepdims=False)
    shape = (high * low,) + held.shape[1:]
    return keep.reshape(shape), send.reshape(shape)


def chain_step(c):
    k = c["order"][c["i"]]
    if c["kind"] == "pre":
        n = lax.axis_size("shot")
        keep, send = c["slices"]()
        return keep + lax.ppermute(send, "shot", [(i, i ^ k) for i in range(n)])
    if c["kind"] == "ag":
        return ag_step(c["held"], k, c["bits"])
    return rs_step(c["held"], k, c["bits"])


def chain_commit(c, held):
    k = c["order"][c["i"]]
    c["held"] = held
    c["i"] += 1
    if c["kind"] == "ag":
        c["bits"].append(k)
    else:
        c["kind"] = "rs"
        c["bits"].remove(k)


def rs_step(held, k, left):
    n = lax.axis_size("shot")
    me = lax.axis_index("shot")
    low = 2 ** left.index(k)
    high = held.shape[0] // (2 * low)
    split = held.reshape((high, 2, low) + held.shape[1:])
    mine = (me // k) % 2
    keep = lax.dynamic_index_in_dim(split, mine, axis=1, keepdims=False)
    send = lax.dynamic_index_in_dim(split, 1 - mine, axis=1, keepdims=False)
    got = lax.ppermute(send, "shot", [(i, i ^ k) for i in range(n)])
    return (keep + got).reshape((high * low,) + held.shape[1:])


def body(
    wave_prev,
    wave_now,
    velocity_code,
    perturb,
    gains,
    wavelet,
    source_index,
    receiver_index,
    absorb_width,
):
    shots, span_x, span_y, span_z = wave_now.shape
    n_shot = lax.axis_size("shot")
    me_shot = lax.axis_index("shot")
    bits = shot_bits(n_shot)
    start_x = lax.axis_index("space") * span_x
    total_x = span_x * lax.axis_size("space")
    speed_term = coefficient(velocity_code)
    positions = start_x.astype(jnp.float32) + jnp.arange(span_x, dtype=jnp.float32)
    absorber = damping(absorb_width, positions, total_x, span_y, span_z)
    cells = span_x * span_y * span_z
    offset = start_x * span_y * span_z
    source_local = source_index - offset
    source_owned = (source_local >= 0) & (source_local < cells)
    source_safe = jnp.clip(source_local, 0, cells - 1)
    plane = span_y * span_z
    sx = source_safe[0] // plane
    sy = (source_safe[0] // span_z) % span_y
    sz = source_safe[0] % span_z
    source_code = lax.dynamic_slice(velocity_code, (sx, sy, sz), (1, 1, 1)).reshape(1)
    source_gain = jnp.where(source_owned, coefficient(source_code), 0.0)
    barrier = lax.optimization_barrier

    hit = (
        (jnp.arange(span_x)[:, None, None] == sx)
        & (jnp.arange(span_y)[None, :, None] == sy)
        & (jnp.arange(span_z)[None, None, :] == sz)
    )

    def inject(field, moment):
        return field + jnp.where(hit, source_gain[0] * wavelet[0, moment], 0.0)

    def wave_step(current, prior, moment, last):
        drive = speed_term * laplace_x(with_halo(current))
        if last:
            return None, drive
        later = inject(2.0 * current - prior + drive - absorber * (current - prior), moment)
        return later, drive

    def born_second(born, field_model, drive):
        return (
            2.0 * born
            + speed_term * laplace_x(with_halo(born))
            - absorber * born
            + field_model * drive
        )

    slab = span_x // n_shot
    depth = perturb.shape[2]
    model_held = perturb.transpose(2, 0, 1).reshape(1, depth, span_x * span_y)
    gains_held = gains[None]
    st = {"w0": wave_now[0], "wp": wave_prev[0]}

    def task_wave(i):
        def run():
            last = i == 3
            cur, pri = (st["w0"], st["wp"]) if i == 0 else (st["w%d" % i], st["w%d" % (i - 1)])
            later, drive = wave_step(cur, pri, i, last)
            st["drive%d" % i] = drive
            if not last:
                st["w%d" % (i + 1)] = later
        return run

    def run_group(chains, compute):
        chains = [c for c in chains if c["i"] < len(c["order"])]
        moved = [chain_step(c) for c in chains]
        compute()
        keys = sorted(st.keys())
        out = barrier((moved, [st[n] for n in keys]))
        st.update(zip(keys, out[1]))
        for c, held in zip(chains, out[0]):
            chain_commit(c, held)

    def nothing():
        return None

    def light_prep():
        task_wave(1)()
        st["light"] = st["drive0"] * st["drive0"] + st["drive1"] * st["drive1"]

    def halves(x, axis):
        h = x.shape[axis] // 2
        return lax.slice_in_dim(x, 0, h, axis=axis), lax.slice_in_dim(x, h, x.shape[axis], axis=axis)

    far_first = list(reversed(bits))
    near_first = list(bits)

    top = far_first[0]
    model_c = chain(model_held, "ag", far_first[:1])
    gains_c = chain(gains_held, "ag", far_first)
    light_orders = {"la": near_first[:-1], "lb": swap_first(near_first[:-1])}

    def wave_and_split():
        task_wave(2)()
        pieces = halves(st["light"].reshape(n_shot, slab, span_y, span_z), 2)
        for (name, order), piece in zip(sorted(light_orders.items()), pieces):
            st[name + "_keep"], st[name + "_send"] = split_step(piece, order[0], list(near_first))

    tasks = [task_wave(0), light_prep, wave_and_split]
    run_group([model_c, gains_c], tasks[0])
    half_a, half_b = halves(model_c["held"], 1)
    model_a = chain(half_a, "ag", far_first[1:], [top])
    model_b = chain(half_b, "ag", swap_first(far_first[1:]), [top])
    for i in range(1, len(bits)):
        run_group([model_a, model_b, gains_c], tasks[i] if i < len(tasks) else nothing)
    for i in range(len(bits), len(tasks)):
        tasks[i]()
    model_held = jnp.concatenate([model_a["held"], model_b["held"]], axis=1)
    gains_held = gains_c["held"]
    light_a = chain(None, "pre", light_orders["la"], near_first)
    light_b = chain(None, "pre", light_orders["lb"], near_first)
    light_a["slices"] = lambda: (st["la_keep"], st["la_send"])
    light_b["slices"] = lambda: (st["lb_keep"], st["lb_send"])

    def born_pass():
        model = model_held.reshape(span_z, span_x * span_y).T.reshape(span_x, span_y, span_z)
        st["born1"] = model * st["drive0"]
        st["born2"] = born_second(st["born1"], model, st["drive1"])

    run_group([light_a, light_b], born_pass)
    born1, born2 = st["born1"], st["born2"]

    image = st["drive0"] * born1 + st["drive1"] * born2
    image_a, image_b = halves(image.reshape(n_shot, slab, span_y, span_z), 2)
    image_a = chain(image_a, "rs", near_first[:-1], near_first)
    image_b = chain(image_b, "rs", swap_first(near_first[:-1]), near_first)
    tasks = [task_wave(3)]
    light_c = None
    for i in range(len(bits) - 1):
        group = [image_a, image_b]
        if light_a["i"] < len(light_a["order"]):
            group += [light_a, light_b]
        elif light_c is None:
            light_c = chain(
                jnp.concatenate([light_a["held"], light_b["held"]], axis=2), "rs", near_first[-1:], near_first[-1:]
            )
            group.append(light_c)
        run_group(group, tasks[i] if i < len(tasks) else nothing)
    for i in range(len(bits) - 1, len(tasks)):
        tasks[i]()
    if light_c is None:
        light_c = chain(
            jnp.concatenate([light_a["held"], light_b["held"]], axis=2), "rs", near_first[-1:], near_first[-1:]
        )
    last = chain(
        jnp.concatenate([image_a["held"], image_b["held"]], axis=2), "rs", near_first[-1:], near_first[-1:]
    )
    run_group([last, light_c], nothing)
    image_part = last["held"][0]
    light_part = light_c["held"][0]

    table_all = gains_held.reshape(n_shot * gains.shape[0], gains.shape[1])
    filt_part = lateral_filter(image_part / (light_part + eps), table_all)
    filt_c = chain(filt_part[None], "ag", far_first[:1])
    run_group([filt_c], nothing)
    part_a, part_b = halves(filt_c["held"], 2)
    filt_a = chain(part_a, "ag", far_first[1:], [top])
    filt_b = chain(part_b, "ag", swap_first(far_first[1:]), [top])
    for i in range(1, len(bits)):
        run_group([filt_a, filt_b], nothing)
    new_model = jnp.concatenate([filt_a["held"], filt_b["held"]], axis=2).reshape(span_x, span_y, span_z)
    filtered = lax.dynamic_slice_in_dim(new_model, me_shot * depth, depth, 2)

    b1 = new_model * st["drive2"]
    b2 = born_second(b1, new_model, st["drive3"])

    receiver_local = receiver_index[0] - offset
    receiver_owned = (receiver_local >= 0) & (receiver_local < cells)
    receiver_safe = jnp.clip(receiver_local, 0, cells - 1)
    row = receiver_safe // span_z
    rz = receiver_safe % span_z
    lane = jnp.arange(span_z)[None, :] == rz[:, None]

    def sample(field):
        rows = jnp.take(field.reshape(span_x * span_y, span_z), row, axis=0)
        picked = jnp.sum(jnp.where(lane, rows, 0.0), axis=1)
        return jnp.where(receiver_owned, picked, 0.0)

    records = jnp.stack([sample(b1), sample(b2)], axis=0)[None]
    traces = records + lax.ppermute(records, "space", [(0, 1), (1, 0)])
    return (filtered, b2[None], traces)


def solution(mesh):
    in_specs = (
        P(("dom", "shot"), "space", None, None),
        P(("dom", "shot"), "space", None, None),
        P(("dom", "space"), None, None),
        P(("dom", "space"), None, "shot"),
        P(("dom", "shot"), None),
        P(("dom", "shot"), None),
        P(("dom", "shot")),
        P(("dom", "shot"), None),
        P("dom"),
    )
    out_specs = (
        P(("dom", "space"), None, "shot"),
        P(("dom", "shot"), "space", None, None),
        P(("dom", "shot"), None, None),
    )
    return jax.shard_map(body, mesh=mesh, in_specs=in_specs, out_specs=out_specs, check_vma=False)
```

```python
import math

import jax
import jax.numpy as jnp
from jax import lax
from jax.sharding import PartitionSpec as P

STEPS_A = 2
STEPS_B = 2


STENCIL = (-205.0 / 72.0, 8.0 / 5.0, -1.0 / 5.0, 8.0 / 315.0, -1.0 / 560.0)
damp_peak = 0.5
eps = 1e-05
HALO = 4


def coefficient(levels):
    speed = 1500.0 + 15.0 * levels.astype(jnp.float32)
    ratio = 0.45 * speed / 5325.0
    return ratio * ratio


def ramp(position, count, lower, upper):
    low_part = jnp.maximum(lower - position, 0.0) / lower
    high_part = jnp.maximum(upper - (count - 1.0 - position), 0.0) / upper
    return low_part * low_part + high_part * high_part


def damping(widths, positions, count_x, count_y, count_z):
    edges = widths.astype(jnp.float32)
    longest = max(positions.shape[0], count_y, count_z)
    line = jnp.arange(longest, dtype=jnp.float32)
    x_line = jnp.pad(positions, (0, longest - positions.shape[0]))
    place = jnp.stack([x_line, line, line])
    count = jnp.stack([jnp.asarray(count_x, jnp.float32), jnp.float32(count_y), jnp.float32(count_z)])[:, None]
    lower = jnp.stack([edges[0], edges[2], edges[4]])[:, None]
    upper = jnp.stack([edges[1], edges[3], edges[5]])[:, None]
    ramps = ramp(place, count, lower, upper)
    along_x = ramps[0, : positions.shape[0]]
    along_y = ramps[1, :count_y]
    along_z = ramps[2, :count_z]
    return damp_peak * (along_x[:, None, None] + along_y[None, :, None] + along_z[None, None, :])


def with_halo(x):
    size = lax.axis_size("space")
    length = x.shape[0]
    if size == 2:
        me = lax.axis_index("space")
        piece = lax.dynamic_slice_in_dim(x, (1 - me) * (length - HALO), HALO, 0)
        got = lax.ppermute(piece, "space", [(0, 1), (1, 0)])
        zeros = jnp.zeros((HALO,) + x.shape[1:], x.dtype)
        padded = jnp.concatenate([zeros, x, zeros], axis=0)
        return lax.dynamic_update_slice_in_dim(padded, got, (1 - me) * (length + HALO), 0)
    up = [(i, (i + 1) % size) for i in range(size - 1)]
    down = [(j, i) for i, j in up]
    before = lax.ppermute(x[length - HALO :], "space", up)
    after = lax.ppermute(x[:HALO], "space", down)
    return jnp.concatenate([before, x, after], axis=0)


def laplace_x(padded):
    width_x = padded.shape[0] - 8
    width_y = padded.shape[1]
    width_z = padded.shape[2]
    full = jnp.pad(padded, [(0, 0), (4, 4), (4, 4)])

    def part(move_x, move_y, move_z):
        return full[
            4 + move_x : 4 + move_x + width_x,
            4 + move_y : 4 + move_y + width_y,
            4 + move_z : 4 + move_z + width_z,
        ]

    total = 3.0 * STENCIL[0] * part(0, 0, 0)
    for reach in range(1, 5):
        beside_all = (
            part(reach, 0, 0)
            + part(-reach, 0, 0)
            + part(0, reach, 0)
            + part(0, -reach, 0)
            + part(0, 0, reach)
            + part(0, 0, -reach)
        )
        total = total + STENCIL[reach] * beside_all
    return total


def lateral_filter(field, table):
    count = field.shape[1]
    index = jnp.arange(count)
    phase = index[:, None] * index[None, :] % count
    angle = 2.0 * math.pi / count * phase.astype(jnp.float32)
    cosine = jnp.cos(angle)
    sine = jnp.sin(angle)
    real_part = jnp.einsum("xyz,yk->xzk", field, cosine, precision=lax.Precision.HIGH)
    imag_part = jnp.einsum("xyz,yk->xzk", field, sine, precision=lax.Precision.HIGH)
    weight = table[None, :, :]
    back = jnp.einsum("xzk,yk->xyz", real_part * weight, cosine, precision=lax.Precision.HIGH)
    back = back + jnp.einsum(
        "xzk,yk->xyz", imag_part * weight, sine, precision=lax.Precision.HIGH
    )
    return back / count


def shot_bits(n):
    bits = []
    k = 1
    while k < n:
        bits.append(k)
        k *= 2
    assert k == n
    return bits


def ag_step(held, k, done):
    n = lax.axis_size("shot")
    me = lax.axis_index("shot")
    theirs = lax.ppermute(held, "shot", [(i, i ^ k) for i in range(n)])
    low = 2 ** sum(1 for b in done if b < k)
    shape = (held.shape[0] // low, 1, low) + held.shape[1:]
    mine, other = held.reshape(shape), theirs.reshape(shape)
    first = (me // k) % 2 == 0
    pair = jnp.where(first, jnp.concatenate([mine, other], axis=1), jnp.concatenate([other, mine], axis=1))
    return pair.reshape((2 * held.shape[0],) + held.shape[1:])


def swap_first(order):
    return order[1:2] + order[:1] + order[2:]


def swap_last(order):
    return order[:-2] + order[-1:] + order[-2:-1] if len(order) > 1 else order


def chain(held, kind, order, bits=None):
    if bits is None:
        bits = [] if kind == "ag" else sorted(order)
    return {"held": held, "kind": kind, "order": list(order), "i": 0, "bits": list(bits)}


def split_step(held, k, left):
    me = lax.axis_index("shot")
    low = 2 ** left.index(k)
    high = held.shape[0] // (2 * low)
    split = held.reshape((high, 2, low) + held.shape[1:])
    mine = (me // k) % 2
    keep = lax.dynamic_index_in_dim(split, mine, axis=1, keepdims=False)
    send = lax.dynamic_index_in_dim(split, 1 - mine, axis=1, keepdims=False)
    shape = (high * low,) + held.shape[1:]
    return keep.reshape(shape), send.reshape(shape)


def chain_step(c):
    k = c["order"][c["i"]]
    if c["kind"] == "pre":
        n = lax.axis_size("shot")
        keep, send = c["slices"]()
        return keep + lax.ppermute(send, "shot", [(i, i ^ k) for i in range(n)])
    if c["kind"] == "ag":
        return ag_step(c["held"], k, c["bits"])
    return rs_step(c["held"], k, c["bits"])


def chain_commit(c, held):
    k = c["order"][c["i"]]
    c["held"] = held
    c["i"] += 1
    if c["kind"] == "ag":
        c["bits"].append(k)
    else:
        c["kind"] = "rs"
        c["bits"].remove(k)


def rs_step(held, k, left):
    n = lax.axis_size("shot")
    me = lax.axis_index("shot")
    low = 2 ** left.index(k)
    high = held.shape[0] // (2 * low)
    split = held.reshape((high, 2, low) + held.shape[1:])
    mine = (me // k) % 2
    keep = lax.dynamic_index_in_dim(split, mine, axis=1, keepdims=False)
    send = lax.dynamic_index_in_dim(split, 1 - mine, axis=1, keepdims=False)
    got = lax.ppermute(send, "shot", [(i, i ^ k) for i in range(n)])
    return (keep + got).reshape((high * low,) + held.shape[1:])


def body(
    wave_prev,
    wave_now,
    velocity_code,
    perturb,
    gains,
    wavelet,
    source_index,
    receiver_index,
    absorb_width,
):
    shots, span_x, span_y, span_z = wave_now.shape
    n_shot = lax.axis_size("shot")
    me_shot = lax.axis_index("shot")
    bits = shot_bits(n_shot)
    start_x = lax.axis_index("space") * span_x
    total_x = span_x * lax.axis_size("space")
    speed_term = coefficient(velocity_code)
    positions = start_x.astype(jnp.float32) + jnp.arange(span_x, dtype=jnp.float32)
    absorber = damping(absorb_width, positions, total_x, span_y, span_z)
    cells = span_x * span_y * span_z
    offset = start_x * span_y * span_z
    source_local = source_index - offset
    source_owned = (source_local >= 0) & (source_local < cells)
    source_safe = jnp.clip(source_local, 0, cells - 1)
    plane = span_y * span_z
    sx = source_safe[0] // plane
    sy = (source_safe[0] // span_z) % span_y
    sz = source_safe[0] % span_z
    source_code = lax.dynamic_slice(velocity_code, (sx, sy, sz), (1, 1, 1)).reshape(1)
    source_gain = jnp.where(source_owned, coefficient(source_code), 0.0)
    barrier = lax.optimization_barrier

    hit = (
        (jnp.arange(span_x)[:, None, None] == sx)
        & (jnp.arange(span_y)[None, :, None] == sy)
        & (jnp.arange(span_z)[None, None, :] == sz)
    )

    def inject(field, moment):
        return field + jnp.where(hit, source_gain[0] * wavelet[0, moment], 0.0)

    def wave_step(current, prior, moment, last):
        if moment == 0:
            inner = barrier(laplace_x(current))
            padded = with_halo(current)
            edge = 2 * HALO
            lap = jnp.concatenate(
                [laplace_x(padded[: edge + HALO]), inner, laplace_x(padded[padded.shape[0] - edge - HALO :])],
                axis=0,
            )
            drive = speed_term * lap
        else:
            drive = speed_term * laplace_x(with_halo(current))
        if last:
            return None, drive
        later = inject(2.0 * current - prior + drive - absorber * (current - prior), moment)
        return later, drive

    def born_second(born, field_model, drive):
        return (
            2.0 * born
            + speed_term * laplace_x(with_halo(born))
            - absorber * born
            + field_model * drive
        )

    slab = span_x // n_shot
    depth = perturb.shape[2]
    model_held = perturb.transpose(2, 0, 1).reshape(1, depth, span_x * span_y)
    gains_held = gains[None]
    st = {"w0": wave_now[0], "wp": wave_prev[0]}

    def task_wave(i):
        def run():
            last = i == 3
            cur, pri = (st["w0"], st["wp"]) if i == 0 else (st["w%d" % i], st["w%d" % (i - 1)])
            later, drive = wave_step(cur, pri, i, last)
            st["drive%d" % i] = drive
            if not last:
                st["w%d" % (i + 1)] = later
        return run

    def run_group(chains, compute):
        chains = [c for c in chains if c["i"] < len(c["order"])]
        moved = [chain_step(c) for c in chains]
        compute()
        keys = sorted(st.keys())
        out = barrier((moved, [st[n] for n in keys]))
        st.update(zip(keys, out[1]))
        for c, held in zip(chains, out[0]):
            chain_commit(c, held)

    def nothing():
        return None

    def light_prep():
        task_wave(1)()
        st["light"] = st["drive0"] * st["drive0"] + st["drive1"] * st["drive1"]

    def halves(x, axis):
        h = x.shape[axis] // 2
        return lax.slice_in_dim(x, 0, h, axis=axis), lax.slice_in_dim(x, h, x.shape[axis], axis=axis)

    far_first = list(reversed(bits))
    near_first = list(bits)

    top = far_first[0]
    model_c = chain(model_held, "ag", far_first[:1])
    gains_c = chain(gains_held, "ag", far_first)
    light_orders = {"la": near_first[:-1], "lb": swap_first(near_first[:-1])}

    def wave_and_split():
        task_wave(2)()
        pieces = halves(st["light"].reshape(n_shot, slab, span_y, span_z), 2)
        for (name, order), piece in zip(sorted(light_orders.items()), pieces):
            st[name + "_keep"], st[name + "_send"] = split_step(piece, order[0], list(near_first))

    tasks = [task_wave(0), light_prep, wave_and_split]
    run_group([model_c, gains_c], tasks[0])
    half_a, half_b = halves(model_c["held"], 1)
    model_a = chain(half_a, "ag", far_first[1:], [top])
    model_b = chain(half_b, "ag", swap_first(far_first[1:]), [top])
    for i in range(1, len(bits)):
        run_group([model_a, model_b, gains_c], tasks[i] if i < len(tasks) else nothing)
    for i in range(len(bits), len(tasks)):
        tasks[i]()
    model_held = jnp.concatenate([model_a["held"], model_b["held"]], axis=1)
    gains_held = gains_c["held"]
    light_a = chain(None, "pre", light_orders["la"], near_first)
    light_b = chain(None, "pre", light_orders["lb"], near_first)
    light_a["slices"] = lambda: (st["la_keep"], st["la_send"])
    light_b["slices"] = lambda: (st["lb_keep"], st["lb_send"])

    def born_pass():
        model = model_held.reshape(span_z, span_x * span_y).T.reshape(span_x, span_y, span_z)
        st["born1"] = model * st["drive0"]
        st["born2"] = born_second(st["born1"], model, st["drive1"])

    run_group([light_a, light_b], born_pass)
    born1, born2 = st["born1"], st["born2"]

    image = st["drive0"] * born1 + st["drive1"] * born2
    image_a, image_b = halves(image.reshape(n_shot, slab, span_y, span_z), 2)
    image_a = chain(image_a, "rs", near_first[:-1], near_first)
    image_b = chain(image_b, "rs", swap_first(near_first[:-1]), near_first)
    tasks = [task_wave(3)]
    light_c = None
    for i in range(len(bits) - 1):
        group = [image_a, image_b]
        if light_a["i"] < len(light_a["order"]):
            group += [light_a, light_b]
        elif light_c is None:
            light_c = chain(
                jnp.concatenate([light_a["held"], light_b["held"]], axis=2), "rs", near_first[-1:], near_first[-1:]
            )
            group.append(light_c)
        run_group(group, tasks[i] if i < len(tasks) else nothing)
    for i in range(len(bits) - 1, len(tasks)):
        tasks[i]()
    if light_c is None:
        light_c = chain(
            jnp.concatenate([light_a["held"], light_b["held"]], axis=2), "rs", near_first[-1:], near_first[-1:]
        )
    last = chain(
        jnp.concatenate([image_a["held"], image_b["held"]], axis=2), "rs", near_first[-1:], near_first[-1:]
    )
    run_group([last, light_c], nothing)
    image_part = last["held"][0]
    light_part = light_c["held"][0]

    table_all = gains_held.reshape(n_shot * gains.shape[0], gains.shape[1])
    filt_part = lateral_filter(image_part / (light_part + eps), table_all)
    filt_c = chain(filt_part[None], "ag", far_first[:1])
    run_group([filt_c], nothing)
    part_a, part_b = halves(filt_c["held"], 2)
    filt_a = chain(part_a, "ag", far_first[1:], [top])
    filt_b = chain(part_b, "ag", swap_first(far_first[1:]), [top])
    for i in range(1, len(bits)):
        run_group([filt_a, filt_b], nothing)
    new_model = jnp.concatenate([filt_a["held"], filt_b["held"]], axis=2).reshape(span_x, span_y, span_z)
    filtered = lax.dynamic_slice_in_dim(new_model, me_shot * depth, depth, 2)

    b1 = new_model * st["drive2"]
    b2 = born_second(b1, new_model, st["drive3"])

    receiver_local = receiver_index[0] - offset
    receiver_owned = (receiver_local >= 0) & (receiver_local < cells)
    receiver_safe = jnp.clip(receiver_local, 0, cells - 1)
    row = receiver_safe // span_z
    rz = receiver_safe % span_z
    lane = jnp.arange(span_z)[None, :] == rz[:, None]

    def sample(field):
        rows = jnp.take(field.reshape(span_x * span_y, span_z), row, axis=0)
        picked = jnp.sum(jnp.where(lane, rows, 0.0), axis=1)
        return jnp.where(receiver_owned, picked, 0.0)

    records = jnp.stack([sample(b1), sample(b2)], axis=0)[None]
    traces = records + lax.ppermute(records, "space", [(0, 1), (1, 0)])
    return (filtered, b2[None], traces)


def solution(mesh):
    in_specs = (
        P(("dom", "shot"), "space", None, None),
        P(("dom", "shot"), "space", None, None),
        P(("dom", "space"), None, None),
        P(("dom", "space"), None, "shot"),
        P(("dom", "shot"), None),
        P(("dom", "shot"), None),
        P(("dom", "shot")),
        P(("dom", "shot"), None),
        P("dom"),
    )
    out_specs = (
        P(("dom", "space"), None, "shot"),
        P(("dom", "shot"), "space", None, None),
        P(("dom", "shot"), None, None),
    )
    return jax.shard_map(body, mesh=mesh, in_specs=in_specs, out_specs=out_specs, check_vma=False)
```
